32 devices in a mesh: dp: 8 (over z, core), shard: 4 (over y, x).
Axes of the slice: x: 2, y: 2, z: 4, core: 2. Of those that a mesh axis runs over, the one named last changes fastest.
Arguments:
- text_in: bfloat16 [32, 512, 768], P(('dp', 'shard')), may hold values from -6 to 6
- layout_in: bfloat16 [32, 512, 192], P(('dp', 'shard')), may hold values from -6 to 6
- lengths: int32 [32], P(('dp', 'shard')), may hold values from 40 to 512, as said below
- text_attn: bfloat16 [768, 3072], P(('dp', 'shard')), may hold values from -2 to 2
- text_w1: bfloat16 [768, 3072], P(('dp', 'shard')), may hold values from -0.21875 to 0.21875
- text_w2: bfloat16 [3072, 768], P(('dp', 'shard')), may hold values from -0.109375 to 0.109375
- text_vectors: bfloat16 [9216], P(('dp', 'shard')), may hold values from -2 to 2
- layout_attn: bfloat16 [768, 192], P(('dp', 'shard')), may hold values from -2 to 2
- layout_w1: bfloat16 [192, 768], P(None, ('dp', 'shard')), may hold values from -0.4375 to 0.4375
- layout_w2: bfloat16 [768, 192], P(('dp', 'shard')), may hold values from -0.21875 to 0.21875
- layout_vectors: bfloat16 [2304], P(('dp', 'shard')), may hold values from -2 to 2
- cot_text: bfloat16 [32, 512, 768], P(('dp', 'shard')), may hold values from -6 to 6
- cot_layout: bfloat16 [32, 512, 192], P(('dp', 'shard')), may hold values from -6 to 6
Outputs:
- out_text: bfloat16 [32, 512, 768], P(('dp', 'shard'))
- out_layout: bfloat16 [32, 512, 192], P(('dp', 'shard'))
- grad_text_in: float32 [32, 512, 768], P(('dp', 'shard'))
- grad_layout_in: float32 [32, 512, 192], P(('dp', 'shard'))
- grad_text_attn: float32 [768, 3072], P(('dp', 'shard'))
- grad_text_w1: float32 [768, 3072], P(('dp', 'shard'))
- grad_text_w2: float32 [3072, 768], P(('dp', 'shard'))
- grad_text_vectors: float32 [9216], P(('dp', 'shard'))
- grad_layout_attn: float32 [768, 192], P(('dp', 'shard'))
- grad_layout_w1: float32 [192, 768], P(None, ('dp', 'shard'))
- grad_layout_w2: float32 [768, 192], P(('dp', 'shard'))
- grad_layout_vectors: float32 [2304], P(('dp', 'shard'))
The draws below stay inside these ranges and needn't reach their ends.
Inputs may be any that keep to these rules, and one draw needn't show every extreme that they name: `lengths`: the real tokens of a page fill its first slots; the first page of the batch is full and the second holds 40 tokens.
All inputs are finite; a program needn't handle non-finite values.
Results may differ from the reference program's by a relative error of at most 0.012.
The reference program's roundings to bfloat16 on the way count: a program that leaves them out, or rounds other values in their place, can miss the bound.
Values may be sent and summed in bfloat16 or wider, within the bound.
No kernel may reach another device: no remote copies, remote signals or barrier semaphores. Data moves between devices by JAX's collectives and lax.ppermute only.
A program may use at most 192 MiB of HBM per device.

```python
import jax
import jax.numpy as jnp
from jax import lax

H = 12
HD = 64
LHD = 16
FF = 3072
LFF = 768
D = 768
LD = 192
SLOTS = 512
LEN_MIN = 40
PAGES = 32


OUT_GAIN = 5.0


def attn_draw(key, width):
    noise = jnp.clip(jax.random.normal(key, (4 * width, width), jnp.float32), -3.0, 3.0)
    row_index = jnp.arange(4 * width)
    factor = jnp.where(row_index < 3 * width, 1.0, OUT_GAIN) / jnp.sqrt(jnp.float32(width))
    return noise * factor[:, None]


def attn_draw_columns(key, width):
    noise = jnp.clip(jax.random.normal(key, (width, 4 * width), jnp.float32), -3.0, 3.0)
    column_index = jnp.arange(4 * width)
    factor = jnp.where(column_index < 3 * width, 1.0, OUT_GAIN) / jnp.sqrt(jnp.float32(width))
    return noise * factor[None, :]


def vector_draw(key, width, wide):
    noise = jnp.clip(jax.random.normal(key, (8 * width + wide,), jnp.float32), -3.0, 3.0)
    segment = jnp.arange(8 * width + wide) // width
    is_scale = (segment == 3) | (segment == 6)
    return jnp.where(is_scale, 1.0 + 0.25 * noise, 0.5 * noise)


def draw_text_attn(key, part):
    return attn_draw_columns(key, D).astype(jnp.bfloat16)


def draw_layout_attn(key, part):
    return attn_draw(key, LD).astype(jnp.bfloat16)


def draw_text_vectors(key, part):
    return vector_draw(key, D, FF).astype(jnp.bfloat16)


def draw_layout_vectors(key, part):
    return vector_draw(key, LD, LFF).astype(jnp.bfloat16)


def draw_lengths(key, part):
    drawn = jax.random.randint(key, (PAGES,), LEN_MIN, SLOTS + 1, dtype=jnp.int32)
    return drawn.at[0].set(SLOTS).at[1].set(LEN_MIN)


def raised(array, stream_key, source, target, parts, factor):
    def block_of(position):
        return (jnp.arange(array.shape[position]) // (array.shape[position] // parts)).reshape((-1,) + (1,) * (array.ndim - 1 - position))

    near = jax.random.permutation(stream_key, parts)[block_of(target)]
    second = (block_of(target) + parts // 2) % parts
    return jnp.where((block_of(source) == near) | (block_of(source) == second), factor * array, array)


def block_levels(stream_key, dims, split, low, top_value):
    factor_of = 1.0
    for position, parts in split:
        draws = jax.random.uniform(jax.random.fold_in(jax.random.fold_in(stream_key, 6), position), (parts,), jnp.float32, low / len(split), top_value / len(split))
        factor_of = factor_of * jnp.repeat(jnp.exp(draws), dims[position] // parts).reshape((-1,) + (1,) * (len(dims) - 1 - position))
    return factor_of


def normal_values(stream_key, dims, deviation, bound, split=(), kind=jnp.bfloat16):
    values = deviation * jax.random.normal(stream_key, dims, jnp.float32)
    if split:
        values = values * block_levels(stream_key, dims, split, -0.22, 0.18)
    return jnp.clip(values, -bound, bound).astype(kind)


def bell_draw_with(own_key, shape, spread, reach, split, heavy, kind=jnp.bfloat16):
    values = spread * jax.random.normal(own_key, shape, jnp.float32)
    if split:
        values = values * block_levels(own_key, shape, split, -0.22, 0.18)
    return jnp.clip(raised(values, jax.random.fold_in(own_key, 3), *heavy), -reach, reach).astype(kind)


def setup_inputs(seed: int = 0) -> dict:
    key_of = jax.random.split(jax.random.key(seed), 14)
    text_in = normal_values(key_of[0], (PAGES, SLOTS, D), 1.0, 6.0, ((0, 32),))
    layout_in = normal_values(key_of[1], (PAGES, SLOTS, LD), 1.0, 6.0, ((0, 32),))
    lengths = draw_lengths(jax.random.fold_in(key_of[13], 71), 0)
    text_attn = draw_text_attn(jax.random.fold_in(key_of[13], 71), 0)
    text_w1 = normal_values(key_of[4], (D, FF), D ** -0.5, 0.21875, ((0, 32),))
    text_w2 = normal_values(key_of[5], (FF, D), FF ** -0.5, 0.109375, ((0, 32),))
    text_vectors = draw_text_vectors(jax.random.fold_in(key_of[13], 71), 0)
    layout_attn = draw_layout_attn(jax.random.fold_in(key_of[13], 71), 0)
    layout_w1 = normal_values(key_of[8], (LD, LFF), LD ** -0.5, 0.4375, ((1, 32),))
    layout_w2 = normal_values(key_of[9], (LFF, LD), LFF ** -0.5, 0.21875, ((0, 32),))
    layout_vectors = draw_layout_vectors(jax.random.fold_in(key_of[13], 71), 0)
    cot_text = bell_draw_with(key_of[11], (PAGES, SLOTS, D), 1.0, 6.0, ((0, 32),), (0, 2, 32, 2.75))
    cot_layout = bell_draw_with(key_of[12], (PAGES, SLOTS, LD), 1.0, 6.0, ((0, 32),), (0, 2, 32, 2.75))
    return {"text_in": text_in, "layout_in": layout_in, "lengths": lengths, "text_attn": text_attn, "text_w1": text_w1, "text_w2": text_w2, "text_vectors": text_vectors, "layout_attn": layout_attn, "layout_w1": layout_w1, "layout_w2": layout_w2, "layout_vectors": layout_vectors, "cot_text": cot_text, "cot_layout": cot_layout}


EPS = 1e-05
NEG = -1000000000.0
HIGH = lax.Precision.HIGHEST

@jax.custom_vjp
def low(v):
    return lax.optimization_barrier(v.astype(jnp.bfloat16)).astype(jnp.float32)

@jax.custom_vjp
def low_back(v):
    return v

def low_keep(v):
    return (low(v), None)

def low_pass(kept, grad):
    return (grad,)

def back_keep(v):
    return (v, None)

def back_low(kept, grad):
    return (low(grad),)
low.defvjp(low_keep, low_pass)
low_back.defvjp(back_keep, back_low)

def rounded(values):
    return low(low_back(values))

def project(inputs, matrix):
    return jnp.dot(inputs, matrix, precision=HIGH)

def block_of(attn, index, width, columns):
    if columns:
        return attn[:, index * width:(index + 1) * width]
    return attn[index * width:(index + 1) * width]

def split_heads(values):
    return values.reshape(values.shape[0], H, -1)

def head_scores(query_rows, key_rows, factor):
    return factor * jnp.einsum('qhd,khd->hqk', split_heads(query_rows), split_heads(key_rows), precision=HIGH)

def softmax_rows(scores, valid):
    scores = jnp.where(valid[None, None, :], scores, NEG)
    row_max = lax.optimization_barrier(jnp.max(scores, -1, keepdims=True))
    exponent = jnp.exp(scores - row_max)
    return exponent / lax.optimization_barrier(jnp.sum(exponent, -1, keepdims=True))

def context_of(probs, value_rows):
    mixed = jnp.einsum('hqk,khd->qhd', low(probs), split_heads(value_rows), precision=HIGH)
    return rounded(mixed.reshape(mixed.shape[0], -1))

def normalize(values, scale_row, shift_row):
    centered = values - lax.optimization_barrier(jnp.mean(values, -1, keepdims=True))
    variance = lax.optimization_barrier(jnp.mean(centered * centered, -1, keepdims=True))
    return centered * lax.rsqrt(variance + EPS) * scale_row + shift_row

def vector_parts(packed, width):
    pieces = [packed[index * width:(index + 1) * width] for index in range(8)]
    return pieces + [packed[8 * width:]]

def query_key(inputs, attn, packed, width, columns):
    pieces = vector_parts(packed, width)
    query_rows = rounded(project(inputs, block_of(attn, 0, width, columns)) + pieces[0])
    key_rows = rounded(project(inputs, block_of(attn, 1, width, columns)))
    return (query_rows, key_rows)

def value_of(inputs, attn, packed, width, columns):
    pieces = vector_parts(packed, width)
    return rounded(project(inputs, block_of(attn, 2, width, columns)) + pieces[1])

def branch(inputs, context, attn, packed, first, second, width, columns):
    pieces = vector_parts(packed, width)
    first_res = inputs + (low_back(project(context, block_of(attn, 3, width, columns))) + pieces[2])
    hidden = normalize(first_res, pieces[3], pieces[4])
    inner = low_back(project(low(hidden), first)) + pieces[8]
    activated = jax.nn.gelu(inner, approximate=False)
    second_res = hidden + (low_back(project(low(activated), second)) + pieces[5])
    return normalize(second_res, pieces[6], pieces[7])

def page_forward(params, text_rows, layout_rows, fixed_scores, valid):
    text_attn, text_w1, text_w2, text_vec, layout_attn, layout_w1, layout_w2, layout_vec = params
    width = text_rows.shape[1]
    narrow = layout_rows.shape[1]
    text_q, text_k = query_key(text_rows, text_attn, text_vec, width, True)
    text_v = value_of(text_rows, text_attn, text_vec, width, True)
    layout_q, layout_k = query_key(layout_rows, layout_attn, layout_vec, narrow, False)
    layout_v = value_of(layout_rows, layout_attn, layout_vec, narrow, False)
    text_s = low_back(head_scores(text_q, text_k, HD ** (-0.5)))
    layout_s = low_back(head_scores(layout_q, layout_k, LHD ** (-0.5)))
    text_p = softmax_rows(text_s + layout_s, valid)
    layout_p = softmax_rows(fixed_scores + layout_s, valid)
    text_ctx = context_of(text_p, text_v)
    layout_ctx = context_of(layout_p, layout_v)
    mask = valid[:, None].astype(text_rows.dtype)
    text_out = branch(text_rows, text_ctx, text_attn, text_vec, text_w1, text_w2, width, True)
    layout_out = branch(layout_rows, layout_ctx, layout_attn, layout_vec, layout_w1, layout_w2, narrow, False)
    return (text_out * mask, layout_out * mask)

def reference(text_in, layout_in, lengths, text_attn, text_w1, text_w2, text_vectors, layout_attn, layout_w1, layout_w2, layout_vectors, cot_text, cot_layout):
    params = tuple((matrix.astype(jnp.float32) for matrix in (text_attn, text_w1, text_w2, text_vectors, layout_attn, layout_w1, layout_w2, layout_vectors)))
    slots = text_in.shape[1]

    def one_page(totals, page):
        text_rows, layout_rows, length, text_cot, layout_cot = page
        text_rows = text_rows.astype(jnp.float32)
        layout_rows = layout_rows.astype(jnp.float32)
        valid = jnp.arange(slots, dtype=jnp.int32) < length
        width = text_rows.shape[1]
        fixed_q, fixed_k = query_key(text_rows, params[0], params[3], width, True)
        fixed_scores = head_scores(fixed_q, fixed_k, HD ** (-0.5))

        def forward(weights, text_part, layout_part):
            return page_forward(weights, text_part, layout_part, fixed_scores, valid)
        (text_out, layout_out), pull = jax.vjp(forward, params, text_rows, layout_rows)
        grad_params, grad_text, grad_layout = pull((text_cot.astype(jnp.float32), layout_cot.astype(jnp.float32)))
        totals = jax.tree.map(jnp.add, totals, grad_params)
        return (totals, (text_out.astype(jnp.bfloat16), layout_out.astype(jnp.bfloat16), grad_text, grad_layout))
    zeros = tuple((jnp.zeros_like(matrix) for matrix in params))
    totals, outputs = lax.scan(one_page, zeros, (text_in, layout_in, lengths, cot_text, cot_layout))
    return (outputs[0], outputs[1], outputs[2], outputs[3], totals[0], totals[1], totals[2], totals[3], totals[4], totals[5], totals[6], totals[7])
```

```python
import jax
import jax.numpy as jnp
from jax import lax
from jax.sharding import PartitionSpec as P

H = 12
HD = 64
LHD = 16


EPS = 1e-05
NEG = -1000000000.0


def normalize(values, scale_row, shift_row):
    centered = values - jnp.mean(values, -1, keepdims=True)
    variance = jnp.mean(centered * centered, -1, keepdims=True)
    return centered * lax.rsqrt(variance + EPS) * scale_row + shift_row


def gelu_exact(values):
    return jax.nn.gelu(values, approximate=False)


def vector_parts(packed, width):
    pieces = [packed[index * width : (index + 1) * width] for index in range(8)]
    return pieces + [packed[8 * width :]]


def split_heads(values):
    return values.reshape(values.shape[0], H, -1)


def block_of(attn, index, width, columns):
    if columns:
        return attn[:, index * width : (index + 1) * width]
    return attn[index * width : (index + 1) * width]


def project_three(inputs, attn, packed, width, columns):
    if columns:
        three = attn[:, 0 : 3 * width].reshape(width, 3, width)
        mixed = jnp.einsum("sd,dje->sje", inputs, three, preferred_element_type=jnp.float32)
    else:
        three = attn[0 : 3 * width].reshape(3, width, width)
        mixed = jnp.einsum("sd,jde->sje", inputs, three, preferred_element_type=jnp.float32)
    pieces = vector_parts(packed.astype(jnp.float32), width)
    offsets = jnp.stack([pieces[0], jnp.zeros_like(pieces[0]), pieces[1]])
    return (mixed + offsets[None]).astype(jnp.bfloat16)


def score_table(text_three, layout_three, valid):
    text_part = jnp.einsum(
        "qhd,khd->hqk",
        split_heads(text_three[:, 0]),
        split_heads(text_three[:, 1]),
        preferred_element_type=jnp.float32,
    )
    layout_part = jnp.einsum(
        "qhd,khd->hqk",
        split_heads(layout_three[:, 0]),
        split_heads(layout_three[:, 1]),
        preferred_element_type=jnp.float32,
    )
    joined = text_part * HD ** (-0.5) + layout_part * LHD ** (-0.5)
    return jnp.where(valid[None, None, :], joined, NEG)


def attend(text_three, layout_three, valid):
    scores = score_table(text_three, layout_three, valid)
    row_max = jnp.max(scores, -1, keepdims=True)
    exponent = jnp.exp(scores - row_max)
    row_total = jnp.sum(exponent, -1, keepdims=True)
    weights = (exponent / row_total).astype(jnp.bfloat16)
    slots = text_three.shape[0]
    text_ctx = jnp.einsum(
        "hqk,khd->qhd", weights, split_heads(text_three[:, 2]), preferred_element_type=jnp.float32
    )
    layout_ctx = jnp.einsum(
        "hqk,khd->qhd", weights, split_heads(layout_three[:, 2]), preferred_element_type=jnp.float32
    )
    log_total = (row_max + jnp.log(row_total))[..., 0]
    return (
        text_ctx.reshape(slots, -1).astype(jnp.bfloat16),
        layout_ctx.reshape(slots, -1).astype(jnp.bfloat16),
        log_total,
    )


def attend_back(text_three, layout_three, valid, log_total, text_grad, layout_grad):
    scores = score_table(text_three, layout_three, valid)
    probs = jnp.exp(scores - log_total[..., None])
    weights = probs.astype(jnp.bfloat16)
    text_heads = split_heads(text_grad)
    layout_heads = split_heads(layout_grad)
    text_dp = jnp.einsum(
        "qhd,khd->hqk",
        text_heads,
        split_heads(text_three[:, 2]),
        preferred_element_type=jnp.float32,
    )
    layout_dp = jnp.einsum(
        "qhd,khd->hqk",
        layout_heads,
        split_heads(layout_three[:, 2]),
        preferred_element_type=jnp.float32,
    )
    text_dv = jnp.einsum("hqk,qhd->khd", weights, text_heads, preferred_element_type=jnp.float32)
    layout_dv = jnp.einsum(
        "hqk,qhd->khd", weights, layout_heads, preferred_element_type=jnp.float32
    )
    text_ds = probs * (text_dp - jnp.sum(probs * text_dp, -1, keepdims=True))
    layout_ds = probs * (layout_dp - jnp.sum(probs * layout_dp, -1, keepdims=True))
    text_only = text_ds.astype(jnp.bfloat16)
    joint_ds = (text_ds + layout_ds).astype(jnp.bfloat16)
    text_dq = jnp.einsum(
        "hqk,khd->qhd", text_only, split_heads(text_three[:, 1]), preferred_element_type=jnp.float32
    ) * HD ** (-0.5)
    text_dk = jnp.einsum(
        "hqk,qhd->khd", text_only, split_heads(text_three[:, 0]), preferred_element_type=jnp.float32
    ) * HD ** (-0.5)
    layout_dq = jnp.einsum(
        "hqk,khd->qhd",
        joint_ds,
        split_heads(layout_three[:, 1]),
        preferred_element_type=jnp.float32,
    ) * LHD ** (-0.5)
    layout_dk = jnp.einsum(
        "hqk,qhd->khd",
        joint_ds,
        split_heads(layout_three[:, 0]),
        preferred_element_type=jnp.float32,
    ) * LHD ** (-0.5)
    slots = text_three.shape[0]
    text_all = jnp.stack([text_dq, text_dk, text_dv], 1).reshape(slots, 3, -1)
    layout_all = jnp.stack([layout_dq, layout_dk, layout_dv], 1).reshape(slots, 3, -1)
    return (text_all, layout_all)


def project_back(attn, width, columns, three_grad, first_grad):
    rounded_grad = three_grad.astype(jnp.bfloat16)
    if columns:
        three = attn[:, 0 : 3 * width].reshape(width, 3, width)
        input_grad = first_grad + jnp.einsum(
            "sje,dje->sd", rounded_grad, three, preferred_element_type=jnp.float32
        )
    else:
        three = attn[0 : 3 * width].reshape(3, width, width)
        input_grad = first_grad + jnp.einsum(
            "sje,jde->sd", rounded_grad, three, preferred_element_type=jnp.float32
        )
    column_sums = jnp.sum(rounded_grad.astype(jnp.float32), 0)
    return (input_grad, rounded_grad, column_sums[0], column_sums[2])


def branch_forward(inputs, context, attn, packed, first, second, width, columns):
    pieces = vector_parts(packed.astype(jnp.float32), width)
    out_block = block_of(attn, 3, width, columns)
    first_res = inputs.astype(jnp.float32) + (
        jnp.dot(context, out_block, preferred_element_type=jnp.float32) + pieces[2]
    )
    hidden = normalize(first_res, pieces[3], pieces[4])
    inner = (
        jnp.dot(hidden.astype(jnp.bfloat16), first, preferred_element_type=jnp.float32) + pieces[8]
    )
    activated = gelu_exact(inner).astype(jnp.bfloat16)
    second_res = hidden + (
        jnp.dot(activated, second, preferred_element_type=jnp.float32) + pieces[5]
    )
    result = normalize(second_res, pieces[6], pieces[7])
    return (result, (first_res, inner, second_res))


def branch_backward(attn, packed, first, second, width, columns, kept_rows, grad_out):
    first_res, inner, second_res = kept_rows
    pieces = vector_parts(packed.astype(jnp.float32), width)
    hidden, first_pull = jax.vjp(normalize, first_res, pieces[3], pieces[4])
    unused, second_pull = jax.vjp(normalize, second_res, pieces[6], pieces[7])
    grad_second, late_scale, late_shift = second_pull(grad_out)
    round_second = grad_second.astype(jnp.bfloat16)
    activated, gelu_pull = jax.vjp(gelu_exact, inner)
    (grad_inner,) = gelu_pull(jnp.dot(round_second, second.T, preferred_element_type=jnp.float32))
    round_inner = grad_inner.astype(jnp.bfloat16)
    grad_hidden = grad_second + jnp.dot(round_inner, first.T, preferred_element_type=jnp.float32)
    grad_first, early_scale, early_shift = first_pull(grad_hidden)
    round_first = grad_first.astype(jnp.bfloat16)
    out_block = block_of(attn, 3, width, columns)
    grad_ctx = jnp.dot(round_first, out_block.T, preferred_element_type=jnp.float32).astype(
        jnp.bfloat16
    )
    operands = (
        hidden.astype(jnp.bfloat16),
        activated.astype(jnp.bfloat16),
        round_first,
        round_second,
        round_inner,
    )
    vector_sums = (
        jnp.sum(grad_first, 0),
        early_scale,
        early_shift,
        jnp.sum(grad_second, 0),
        late_scale,
        late_shift,
        jnp.sum(grad_inner, 0),
    )
    return (grad_first, grad_ctx, operands, vector_sums)


def page_forward(text_rows, layout_rows, length, weights):
    (
        text_attn,
        text_first,
        text_second,
        text_packed,
        layout_attn,
        layout_first,
        layout_second,
        layout_packed,
    ) = weights
    width = text_rows.shape[1]
    narrow = layout_rows.shape[1]
    valid = jnp.arange(text_rows.shape[0], dtype=jnp.int32) < length
    text_three = project_three(text_rows, text_attn, text_packed, width, True)
    layout_three = project_three(layout_rows, layout_attn, layout_packed, narrow, False)
    text_ctx, layout_ctx, log_total = attend(text_three, layout_three, valid)
    text_out, text_kept = branch_forward(
        text_rows, text_ctx, text_attn, text_packed, text_first, text_second, width, True
    )
    layout_out, layout_kept = branch_forward(
        layout_rows,
        layout_ctx,
        layout_attn,
        layout_packed,
        layout_first,
        layout_second,
        narrow,
        False,
    )
    mask = valid[:, None].astype(jnp.float32)
    outputs = ((text_out * mask).astype(jnp.bfloat16), (layout_out * mask).astype(jnp.bfloat16))
    kept_page = (text_three, layout_three, text_ctx, layout_ctx, log_total, text_kept, layout_kept)
    return (outputs, kept_page)


def page_backward(text_rows, layout_rows, length, kept_page, text_cot, layout_cot, weights):
    (
        text_attn,
        text_first,
        text_second,
        text_packed,
        layout_attn,
        layout_first,
        layout_second,
        layout_packed,
    ) = weights
    text_three, layout_three, text_ctx, layout_ctx, log_total, text_kept, layout_kept = kept_page
    width = text_rows.shape[1]
    narrow = layout_rows.shape[1]
    slots = text_rows.shape[0]
    valid = jnp.arange(slots, dtype=jnp.int32) < length
    mask = valid[:, None].astype(jnp.float32)
    text_res_grad, text_ctx_grad, text_ops, text_sums = branch_backward(
        text_attn,
        text_packed,
        text_first,
        text_second,
        width,
        True,
        text_kept,
        text_cot.astype(jnp.float32) * mask,
    )
    layout_res_grad, layout_ctx_grad, layout_ops, layout_sums = branch_backward(
        layout_attn,
        layout_packed,
        layout_first,
        layout_second,
        narrow,
        False,
        layout_kept,
        layout_cot.astype(jnp.float32) * mask,
    )
    text_three_grad, layout_three_grad = attend_back(
        text_three, layout_three, valid, log_total, text_ctx_grad, layout_ctx_grad
    )
    text_in_grad, text_rounded, text_query_bias, text_value_bias = project_back(
        text_attn, width, True, text_three_grad, text_res_grad
    )
    layout_in_grad, layout_rounded, layout_query_bias, layout_value_bias = project_back(
        layout_attn, narrow, False, layout_three_grad, layout_res_grad
    )
    hidden_low, active_low, first_low, second_low, inner_low = layout_ops
    three_w = jnp.einsum(
        "sd,sje->jde", layout_rows, layout_rounded, preferred_element_type=jnp.float32
    ).reshape(3 * narrow, narrow)
    out_w = jnp.einsum("sd,se->de", layout_ctx, first_low, preferred_element_type=jnp.float32)
    layout_attn_grad = jnp.concatenate([three_w, out_w], 0)
    layout_first_grad = jnp.einsum(
        "sd,sf->df", hidden_low, inner_low, preferred_element_type=jnp.float32
    )
    layout_second_grad = jnp.einsum(
        "sf,sd->fd", active_low, second_low, preferred_element_type=jnp.float32
    )
    layout_vec_grad = jnp.concatenate([layout_query_bias, layout_value_bias] + list(layout_sums))
    text_vec_grad = jnp.concatenate([text_query_bias, text_value_bias] + list(text_sums))
    text_hidden, text_active, text_first_low, text_second_low, text_inner_low = text_ops
    text_operands = (
        text_rounded.reshape(slots, 3 * width),
        text_first_low,
        text_hidden,
        text_inner_low,
        text_active,
        text_second_low,
    )
    small_terms = (
        text_vec_grad,
        layout_attn_grad,
        layout_first_grad,
        layout_second_grad,
        layout_vec_grad,
    )
    return ((text_in_grad, layout_in_grad), small_terms, text_operands)


def add_all(running, terms):
    return tuple((before + addend for before, addend in zip(running, terms)))


def flat_rows(values):
    return values.reshape(-1, values.shape[-1])


AXES = ("dp", "shard")


def small_layout(pieces):
    flat = jnp.concatenate([piece.reshape(-1) for piece in pieces])
    rows = -(-flat.shape[0] // 1024) * 8
    return jnp.pad(flat, (0, rows * 128 - flat.shape[0])).reshape(rows, 128)


def gather_small(text_vectors, layout_attn, layout_w1, layout_w2, layout_vectors):
    pieces = (text_vectors, layout_attn, layout_w1, layout_w2, layout_vectors)
    packed = small_layout(pieces)
    rows = packed.shape[0]
    gathered = lax.all_gather(packed, AXES, axis=0, tiled=True)
    count = gathered.shape[0] // rows
    flat = gathered.reshape(count, rows * 128)
    sizes = [piece.size for piece in pieces]
    offsets = [sum(sizes[:index]) for index in range(len(sizes))]
    parts = [flat[:, offset : offset + size] for offset, size in zip(offsets, sizes)]
    full_text_vectors = parts[0].reshape(-1)
    full_layout_attn = parts[1].reshape(count * layout_attn.shape[0], layout_attn.shape[1])
    full_layout_w1 = (
        parts[2]
        .reshape(count, layout_w1.shape[0], layout_w1.shape[1])
        .transpose(1, 0, 2)
        .reshape(layout_w1.shape[0], count * layout_w1.shape[1])
    )
    full_layout_w2 = parts[3].reshape(count * layout_w2.shape[0], layout_w2.shape[1])
    full_layout_vectors = parts[4].reshape(-1)
    return (
        full_text_vectors,
        full_layout_attn,
        full_layout_w1,
        full_layout_w2,
        full_layout_vectors,
    )


def scatter_small(count, text_vec_grad, layout_attn_grad, layout_w1_grad, layout_w2_grad, layout_vec_grad):
    local_w1_cols = layout_w1_grad.shape[1] // count
    blocks = (
        text_vec_grad.reshape(count, -1),
        layout_attn_grad.reshape(count, -1),
        layout_w1_grad.reshape(layout_w1_grad.shape[0], count, local_w1_cols)
        .transpose(1, 0, 2)
        .reshape(count, -1),
        layout_w2_grad.reshape(count, -1),
        layout_vec_grad.reshape(count, -1),
    )
    joined = jnp.concatenate(blocks, 1)
    width = joined.shape[1]
    rows = -(-width // 1024) * 8
    joined = jnp.pad(joined, ((0, 0), (0, rows * 128 - width))).reshape(count * rows, 128)
    summed = lax.psum_scatter(joined, AXES, scatter_dimension=0, tiled=True).reshape(-1)
    sizes = [block.shape[1] for block in blocks]
    offsets = [sum(sizes[:index]) for index in range(len(sizes))]
    parts = [summed[offset : offset + size] for offset, size in zip(offsets, sizes)]
    return (
        parts[0],
        parts[1].reshape(layout_attn_grad.shape[0] // count, layout_attn_grad.shape[1]),
        parts[2].reshape(layout_w1_grad.shape[0], local_w1_cols),
        parts[3].reshape(layout_w2_grad.shape[0] // count, layout_w2_grad.shape[1]),
        parts[4],
    )


def body(
    text_in,
    layout_in,
    lengths,
    text_attn,
    text_w1,
    text_w2,
    text_vectors,
    layout_attn,
    layout_w1,
    layout_w2,
    layout_vectors,
    cot_text,
    cot_layout,
):
    count = lax.psum(1, AXES)
    full_text_vectors, full_layout_attn, full_layout_w1, full_layout_w2, full_layout_vectors = (
        gather_small(text_vectors, layout_attn, layout_w1, layout_w2, layout_vectors)
    )
    weights = (
        lax.all_gather(text_attn, AXES, axis=0, tiled=True),
        lax.all_gather(text_w1, AXES, axis=0, tiled=True),
        lax.all_gather(text_w2, AXES, axis=0, tiled=True),
        full_text_vectors,
        full_layout_attn,
        full_layout_w1,
        full_layout_w2,
        full_layout_vectors,
    )

    def forward_step(carry, page):
        text_rows, layout_rows, length = page
        outputs, kept_page = page_forward(text_rows, layout_rows, length, weights)
        return (carry, (outputs, kept_page))

    unused, (outputs, kept_all) = lax.scan(forward_step, None, (text_in, layout_in, lengths))
    out_text, out_layout = outputs
    zeros = (
        jnp.zeros(weights[3].shape, jnp.float32),
        jnp.zeros(weights[4].shape, jnp.float32),
        jnp.zeros(weights[5].shape, jnp.float32),
        jnp.zeros(weights[6].shape, jnp.float32),
        jnp.zeros(weights[7].shape, jnp.float32),
    )

    def backward_step(running, page):
        text_rows, layout_rows, length, kept_page, text_cot, layout_cot = page
        in_grads, small_terms, text_operands = page_backward(
            text_rows, layout_rows, length, kept_page, text_cot, layout_cot, weights
        )
        return (add_all(running, small_terms), (in_grads, text_operands))

    totals, ((text_grad, layout_grad), text_operands) = lax.scan(
        backward_step, zeros, (text_in, layout_in, lengths, kept_all, cot_text, cot_layout)
    )
    inputs_all = flat_rows(text_in)
    context_all = flat_rows(kept_all[2])
    three_all, first_all, hidden_all, inner_all, active_all, second_all = tuple(
        (flat_rows(values) for values in text_operands)
    )
    grad_second = lax.psum_scatter(
        jnp.einsum("sf,sd->fd", active_all, second_all, preferred_element_type=jnp.float32),
        AXES,
        scatter_dimension=0,
        tiled=True,
    )
    grad_first = lax.psum_scatter(
        jnp.einsum("sd,sf->df", hidden_all, inner_all, preferred_element_type=jnp.float32),
        AXES,
        scatter_dimension=0,
        tiled=True,
    )
    three_part = jnp.einsum("sd,se->de", inputs_all, three_all, preferred_element_type=jnp.float32)
    out_part = jnp.einsum("sd,se->de", context_all, first_all, preferred_element_type=jnp.float32)
    grad_attn = lax.psum_scatter(
        jnp.concatenate([three_part, out_part], 1), AXES, scatter_dimension=0, tiled=True
    )
    summed = scatter_small(count, *totals)
    return (
        out_text,
        out_layout,
        text_grad,
        layout_grad,
        grad_attn,
        grad_first,
        grad_second,
        summed[0],
        summed[1],
        summed[2],
        summed[3],
        summed[4],
    )


def solution(mesh):
    placed = (
        P(("dp", "shard"), None, None),
        P(("dp", "shard"), None, None),
        P(("dp", "shard")),
        P(("dp", "shard"), None),
        P(("dp", "shard"), None),
        P(("dp", "shard"), None),
        P(("dp", "shard")),
        P(("dp", "shard"), None),
        P(None, ("dp", "shard")),
        P(("dp", "shard"), None),
        P(("dp", "shard")),
        P(("dp", "shard"), None, None),
        P(("dp", "shard"), None, None),
    )
    return jax.shard_map(
        body,
        mesh=mesh,
        in_specs=placed,
        out_specs=(
            P(("dp", "shard"), None, None),
            P(("dp", "shard"), None, None),
            P(("dp", "shard"), None, None),
            P(("dp", "shard"), None, None),
            P(("dp", "shard"), None),
            P(("dp", "shard"), None),
            P(("dp", "shard"), None),
            P(("dp", "shard")),
            P(("dp", "shard"), None),
            P(None, ("dp", "shard")),
            P(("dp", "shard"), None),
            P(("dp", "shard")),
        ),
        check_vma=False,
    )
```

```python
import jax
import jax.numpy as jnp
from jax import lax
from jax.sharding import PartitionSpec as P


H = 12
HD = 64
LHD = 16


EPS = 1e-05
NEG = -1000000000.0


def normalize(values, scale_row, shift_row):
    centered = values - jnp.mean(values, -1, keepdims=True)
    variance = jnp.mean(centered * centered, -1, keepdims=True)
    return centered * lax.rsqrt(variance + EPS) * scale_row + shift_row


def gelu_exact(values):
    return jax.nn.gelu(values, approximate=False)


def vector_parts(packed, width):
    pieces = [packed[index * width : (index + 1) * width] for index in range(8)]
    return pieces + [packed[8 * width :]]


def split_heads(values):
    return values.reshape(values.shape[0], H, -1)


def block_of(attn, index, width, columns):
    if columns:
        return attn[:, index * width : (index + 1) * width]
    return attn[index * width : (index + 1) * width]


def project_three(inputs, attn, packed, width, columns):
    if columns:
        three = attn[:, 0 : 3 * width].reshape(width, 3, width)
        mixed = jnp.einsum("sd,dje->sje", inputs, three, preferred_element_type=jnp.float32)
    else:
        three = attn[0 : 3 * width].reshape(3, width, width)
        mixed = jnp.einsum("sd,jde->sje", inputs, three, preferred_element_type=jnp.float32)
    pieces = vector_parts(packed.astype(jnp.float32), width)
    offsets = jnp.stack([pieces[0], jnp.zeros_like(pieces[0]), pieces[1]])
    return (mixed + offsets[None]).astype(jnp.bfloat16)


def score_table(text_three, layout_three, valid):
    text_part = jnp.einsum(
        "qhd,khd->hqk",
        split_heads(text_three[:, 0]),
        split_heads(text_three[:, 1]),
        preferred_element_type=jnp.float32,
    )
    layout_part = jnp.einsum(
        "qhd,khd->hqk",
        split_heads(layout_three[:, 0]),
        split_heads(layout_three[:, 1]),
        preferred_element_type=jnp.float32,
    )
    joined = text_part * HD ** (-0.5) + layout_part * LHD ** (-0.5)
    return jnp.where(valid[None, None, :], joined, NEG)


def attend(text_three, layout_three, valid):
    scores = score_table(text_three, layout_three, valid)
    row_max = jnp.max(scores, -1, keepdims=True)
    exponent = jnp.exp(scores - row_max)
    row_total = jnp.sum(exponent, -1, keepdims=True)
    weights = (exponent / row_total).astype(jnp.bfloat16)
    slots = text_three.shape[0]
    text_ctx = jnp.einsum(
        "hqk,khd->qhd", weights, split_heads(text_three[:, 2]), preferred_element_type=jnp.float32
    )
    layout_ctx = jnp.einsum(
        "hqk,khd->qhd", weights, split_heads(layout_three[:, 2]), preferred_element_type=jnp.float32
    )
    log_total = (row_max + jnp.log(row_total))[..., 0]
    return (
        text_ctx.reshape(slots, -1).astype(jnp.bfloat16),
        layout_ctx.reshape(slots, -1).astype(jnp.bfloat16),
        log_total,
    )


def attend_back(text_three, layout_three, valid, log_total, text_grad, layout_grad):
    scores = score_table(text_three, layout_three, valid)
    probs = jnp.exp(scores - log_total[..., None])
    weights = probs.astype(jnp.bfloat16)
    text_heads = split_heads(text_grad)
    layout_heads = split_heads(layout_grad)
    text_dp = jnp.einsum(
        "qhd,khd->hqk",
        text_heads,
        split_heads(text_three[:, 2]),
        preferred_element_type=jnp.float32,
    )
    layout_dp = jnp.einsum(
        "qhd,khd->hqk",
        layout_heads,
        split_heads(layout_three[:, 2]),
        preferred_element_type=jnp.float32,
    )
    text_dv = jnp.einsum("hqk,qhd->khd", weights, text_heads, preferred_element_type=jnp.float32)
    layout_dv = jnp.einsum(
        "hqk,qhd->khd", weights, layout_heads, preferred_element_type=jnp.float32
    )
    text_ds = probs * (text_dp - jnp.sum(probs * text_dp, -1, keepdims=True))
    layout_ds = probs * (layout_dp - jnp.sum(probs * layout_dp, -1, keepdims=True))
    text_only = text_ds.astype(jnp.bfloat16)
    joint_ds = (text_ds + layout_ds).astype(jnp.bfloat16)
    text_dq = jnp.einsum(
        "hqk,khd->qhd", text_only, split_heads(text_three[:, 1]), preferred_element_type=jnp.float32
    ) * HD ** (-0.5)
    text_dk = jnp.einsum(
        "hqk,qhd->khd", text_only, split_heads(text_three[:, 0]), preferred_element_type=jnp.float32
    ) * HD ** (-0.5)
    layout_dq = jnp.einsum(
        "hqk,khd->qhd",
        joint_ds,
        split_heads(layout_three[:, 1]),
        preferred_element_type=jnp.float32,
    ) * LHD ** (-0.5)
    layout_dk = jnp.einsum(
        "hqk,qhd->khd",
        joint_ds,
        split_heads(layout_three[:, 0]),
        preferred_element_type=jnp.float32,
    ) * LHD ** (-0.5)
    slots = text_three.shape[0]
    text_all = jnp.stack([text_dq, text_dk, text_dv], 1).reshape(slots, 3, -1)
    layout_all = jnp.stack([layout_dq, layout_dk, layout_dv], 1).reshape(slots, 3, -1)
    return (text_all, layout_all)


def project_back(attn, width, columns, three_grad, first_grad):
    rounded_grad = three_grad.astype(jnp.bfloat16)
    if columns:
        three = attn[:, 0 : 3 * width].reshape(width, 3, width)
        input_grad = first_grad + jnp.einsum(
            "sje,dje->sd", rounded_grad, three, preferred_element_type=jnp.float32
        )
    else:
        three = attn[0 : 3 * width].reshape(3, width, width)
        input_grad = first_grad + jnp.einsum(
            "sje,jde->sd", rounded_grad, three, preferred_element_type=jnp.float32
        )
    column_sums = jnp.sum(rounded_grad.astype(jnp.float32), 0)
    return (input_grad, rounded_grad, column_sums[0], column_sums[2])


def branch_forward(inputs, context, attn, packed, first, second, width, columns):
    pieces = vector_parts(packed.astype(jnp.float32), width)
    out_block = block_of(attn, 3, width, columns)
    first_res = inputs.astype(jnp.float32) + (
        jnp.dot(context, out_block, preferred_element_type=jnp.float32) + pieces[2]
    )
    hidden = normalize(first_res, pieces[3], pieces[4])
    inner = (
        jnp.dot(hidden.astype(jnp.bfloat16), first, preferred_element_type=jnp.float32) + pieces[8]
    )
    activated = gelu_exact(inner).astype(jnp.bfloat16)
    second_res = hidden + (
        jnp.dot(activated, second, preferred_element_type=jnp.float32) + pieces[5]
    )
    result = normalize(second_res, pieces[6], pieces[7])
    return (result, (first_res, inner, second_res))


def branch_backward(attn, packed, first, second, width, columns, kept_rows, grad_out):
    first_res, inner, second_res = kept_rows
    pieces = vector_parts(packed.astype(jnp.float32), width)
    hidden, first_pull = jax.vjp(normalize, first_res, pieces[3], pieces[4])
    _, second_pull = jax.vjp(normalize, second_res, pieces[6], pieces[7])
    grad_second, late_scale, late_shift = second_pull(grad_out)
    round_second = grad_second.astype(jnp.bfloat16)
    activated, gelu_pull = jax.vjp(gelu_exact, inner)
    (grad_inner,) = gelu_pull(jnp.dot(round_second, second.T, preferred_element_type=jnp.float32))
    round_inner = grad_inner.astype(jnp.bfloat16)
    grad_hidden = grad_second + jnp.dot(round_inner, first.T, preferred_element_type=jnp.float32)
    grad_first, early_scale, early_shift = first_pull(grad_hidden)
    round_first = grad_first.astype(jnp.bfloat16)
    out_block = block_of(attn, 3, width, columns)
    grad_ctx = jnp.dot(round_first, out_block.T, preferred_element_type=jnp.float32).astype(
        jnp.bfloat16
    )
    operands = (
        hidden.astype(jnp.bfloat16),
        activated.astype(jnp.bfloat16),
        round_first,
        round_second,
        round_inner,
    )
    vector_sums = (
        jnp.sum(grad_first, 0),
        early_scale,
        early_shift,
        jnp.sum(grad_second, 0),
        late_scale,
        late_shift,
        jnp.sum(grad_inner, 0),
    )
    return (grad_first, grad_ctx, operands, vector_sums)


def page_forward(text_rows, layout_rows, length, weights):
    (
        text_attn,
        text_first,
        text_second,
        text_packed,
        layout_attn,
        layout_first,
        layout_second,
        layout_packed,
    ) = weights
    width = text_rows.shape[1]
    narrow = layout_rows.shape[1]
    valid = jnp.arange(text_rows.shape[0], dtype=jnp.int32) < length
    text_three = project_three(text_rows, text_attn, text_packed, width, True)
    layout_three = project_three(layout_rows, layout_attn, layout_packed, narrow, False)
    text_ctx, layout_ctx, log_total = attend(text_three, layout_three, valid)
    text_out, text_kept = branch_forward(
        text_rows, text_ctx, text_attn, text_packed, text_first, text_second, width, True
    )
    layout_out, layout_kept = branch_forward(
        layout_rows,
        layout_ctx,
        layout_attn,
        layout_packed,
        layout_first,
        layout_second,
        narrow,
        False,
    )
    mask = valid[:, None].astype(jnp.float32)
    outputs = ((text_out * mask).astype(jnp.bfloat16), (layout_out * mask).astype(jnp.bfloat16))
    kept_page = (text_three, layout_three, text_ctx, layout_ctx, log_total, text_kept, layout_kept)
    return (outputs, kept_page)


def page_back_ffn(length, kept_page, text_cot, layout_cot, weights):
    (
        text_attn,
        text_first,
        text_second,
        text_packed,
        layout_attn,
        layout_first,
        layout_second,
        layout_packed,
    ) = weights
    _, _, _, _, _, text_kept, layout_kept = kept_page
    width = text_attn.shape[0]
    narrow = layout_attn.shape[1]
    slots = text_cot.shape[0]
    valid = jnp.arange(slots, dtype=jnp.int32) < length
    mask = valid[:, None].astype(jnp.float32)
    text_back = branch_backward(
        text_attn,
        text_packed,
        text_first,
        text_second,
        width,
        True,
        text_kept,
        text_cot.astype(jnp.float32) * mask,
    )
    layout_back = branch_backward(
        layout_attn,
        layout_packed,
        layout_first,
        layout_second,
        narrow,
        False,
        layout_kept,
        layout_cot.astype(jnp.float32) * mask,
    )
    return (text_back, layout_back)


def page_back_attn(text_rows, layout_rows, length, kept_page, text_back, layout_back, weights):
    (text_attn, _, _, _, layout_attn, _, _, _) = weights
    text_three, layout_three, _, layout_ctx, log_total, _, _ = kept_page
    width = text_rows.shape[1]
    narrow = layout_rows.shape[1]
    slots = text_rows.shape[0]
    valid = jnp.arange(slots, dtype=jnp.int32) < length
    text_res_grad, text_ctx_grad, _, text_sums = text_back
    layout_res_grad, layout_ctx_grad, layout_ops, layout_sums = layout_back
    text_three_grad, layout_three_grad = attend_back(
        text_three, layout_three, valid, log_total, text_ctx_grad, layout_ctx_grad
    )
    text_in_grad, text_rounded, text_query_bias, text_value_bias = project_back(
        text_attn, width, True, text_three_grad, text_res_grad
    )
    layout_in_grad, layout_rounded, layout_query_bias, layout_value_bias = project_back(
        layout_attn, narrow, False, layout_three_grad, layout_res_grad
    )
    hidden_low, active_low, first_low, second_low, inner_low = layout_ops
    three_w = jnp.einsum(
        "sd,sje->jde", layout_rows, layout_rounded, preferred_element_type=jnp.float32
    ).reshape(3 * narrow, narrow)
    out_w = jnp.einsum("sd,se->de", layout_ctx, first_low, preferred_element_type=jnp.float32)
    layout_attn_grad = jnp.concatenate([three_w, out_w], 0)
    layout_first_grad = jnp.einsum(
        "sd,sf->df", hidden_low, inner_low, preferred_element_type=jnp.float32
    )
    layout_second_grad = jnp.einsum(
        "sf,sd->fd", active_low, second_low, preferred_element_type=jnp.float32
    )
    layout_vec_grad = jnp.concatenate([layout_query_bias, layout_value_bias] + list(layout_sums))
    text_vec_grad = jnp.concatenate([text_query_bias, text_value_bias] + list(text_sums))
    small_terms = (
        text_vec_grad,
        layout_attn_grad,
        layout_first_grad,
        layout_second_grad,
        layout_vec_grad,
    )
    return ((text_in_grad, layout_in_grad), small_terms, text_rounded.reshape(slots, 3 * width))


def flat_rows(values):
    return values.reshape(-1, values.shape[-1])


AXES = ("dp", "shard")


def rows_for(size, width, aligned):
    rows = -(-size // width)
    if aligned:
        rows = -(-rows // 8) * 8
    return rows


def pack_rows(pieces, width, aligned):
    flat = jnp.concatenate([piece.reshape(-1) for piece in pieces])
    rows = rows_for(flat.shape[0], width, aligned)
    return jnp.pad(flat, (0, rows * width - flat.shape[0])).reshape(rows, width)


def unpack_small(flat, count, shapes):
    sizes = [rows * cols for rows, cols in shapes]
    offsets = [sum(sizes[:index]) for index in range(len(sizes))]
    parts = [flat[:, offset : offset + size] for offset, size in zip(offsets, sizes)]
    (attn_rows, attn_cols), (w1_rows, w1_cols), (w2_rows, w2_cols) = shapes[1:4]
    return (
        parts[0].reshape(-1),
        parts[1].reshape(count * attn_rows, attn_cols),
        parts[2].reshape(count, w1_rows, w1_cols).transpose(1, 0, 2).reshape(w1_rows, count * w1_cols),
        parts[3].reshape(count * w2_rows, w2_cols),
        parts[4].reshape(-1),
    )


def gather_weights(text_attn, text_w1, text_w2, text_vectors, layout_attn, layout_w1, layout_w2, layout_vectors):
    rows, width = text_attn.shape
    aligned = rows % 8 == 0
    small = (text_vectors, layout_attn, layout_w1, layout_w2, layout_vectors)
    small_rows = pack_rows(small, width, aligned)
    first = jnp.concatenate([text_attn, small_rows], 0)
    first_all = lax.all_gather(first, AXES, axis=0, tiled=True)
    count = first_all.shape[0] // first.shape[0]
    first_all = first_all.reshape(count, first.shape[0], width)
    full_attn = first_all[:, :rows].reshape(count * rows, width)
    small_flat = first_all[:, rows:].reshape(count, -1)
    shapes = [(1, text_vectors.shape[0]), layout_attn.shape, layout_w1.shape, layout_w2.shape, (1, layout_vectors.shape[0])]
    full_small = unpack_small(small_flat, count, shapes)
    w2_rows = text_w2.shape[0]
    second = jnp.concatenate([text_w1, text_w2.reshape(rows, -1)], 0)
    second_all = lax.all_gather(second, AXES, axis=0, tiled=True).reshape(count, 2 * rows, width)
    full_w1 = second_all[:, :rows].reshape(count * rows, width)
    full_w2 = second_all[:, rows:].reshape(count * w2_rows, text_w2.shape[1])
    return (full_attn, full_w1, full_w2) + full_small


def small_blocks(count, text_vec_grad, layout_attn_grad, layout_w1_grad, layout_w2_grad, layout_vec_grad):
    local_w1_cols = layout_w1_grad.shape[1] // count
    return (
        text_vec_grad.reshape(count, -1),
        layout_attn_grad.reshape(count, -1),
        layout_w1_grad.reshape(layout_w1_grad.shape[0], count, local_w1_cols)
        .transpose(1, 0, 2)
        .reshape(count, -1),
        layout_w2_grad.reshape(count, -1),
        layout_vec_grad.reshape(count, -1),
    )


def scatter_late(count, grad_attn, small_grads):
    width = grad_attn.shape[1]
    rows = grad_attn.shape[0] // count
    blocks = small_blocks(count, *small_grads)
    joined = jnp.concatenate(blocks, 1)
    size = joined.shape[1]
    small_rows = rows_for(size, width, rows % 8 == 0)
    joined = jnp.pad(joined, ((0, 0), (0, small_rows * width - size))).reshape(count, small_rows, width)
    packed = jnp.concatenate([grad_attn.reshape(count, rows, width), joined], 1)
    summed = lax.psum_scatter(packed.reshape(-1, width), AXES, scatter_dimension=0, tiled=True)
    attn_part = summed[:rows]
    flat = summed[rows:].reshape(-1)
    sizes = [block.shape[1] for block in blocks]
    offsets = [sum(sizes[:index]) for index in range(len(sizes))]
    parts = [flat[offset : offset + size] for offset, size in zip(offsets, sizes)]
    _, layout_attn_grad, layout_w1_grad, layout_w2_grad, _ = small_grads
    local_w1_cols = layout_w1_grad.shape[1] // count
    return (
        attn_part,
        parts[0],
        parts[1].reshape(layout_attn_grad.shape[0] // count, layout_attn_grad.shape[1]),
        parts[2].reshape(layout_w1_grad.shape[0], local_w1_cols),
        parts[3].reshape(layout_w2_grad.shape[0] // count, layout_w2_grad.shape[1]),
        parts[4],
    )


def scatter_early(count, grad_first, grad_second):
    width = grad_first.shape[1]
    rows = grad_first.shape[0] // count
    packed = jnp.concatenate(
        [grad_first.reshape(count, rows, width), grad_second.reshape(count, rows, width)], 1
    )
    summed = lax.psum_scatter(packed.reshape(-1, width), AXES, scatter_dimension=0, tiled=True)
    return (summed[:rows], summed[rows:].reshape(-1, grad_second.shape[1]))


def body(
    text_in,
    layout_in,
    lengths,
    text_attn,
    text_w1,
    text_w2,
    text_vectors,
    layout_attn,
    layout_w1,
    layout_w2,
    layout_vectors,
    cot_text,
    cot_layout,
):
    count = lax.psum(1, AXES)
    weights = gather_weights(
        text_attn, text_w1, text_w2, text_vectors, layout_attn, layout_w1, layout_w2, layout_vectors
    )

    page_weights = (None,) * len(weights)
    outputs, kept_all = jax.vmap(page_forward, in_axes=(0, 0, 0, page_weights))(
        text_in, layout_in, lengths, weights
    )
    out_text, out_layout = outputs
    text_back, layout_back = jax.vmap(page_back_ffn, in_axes=(0, 0, 0, 0, page_weights))(
        lengths, kept_all, cot_text, cot_layout, weights
    )
    text_hidden, text_active, text_first_low, text_second_low, text_inner_low = text_back[2]
    early = (
        jnp.einsum("sd,sf->df", flat_rows(text_hidden), flat_rows(text_inner_low), preferred_element_type=jnp.float32),
        jnp.einsum("sf,sd->fd", flat_rows(text_active), flat_rows(text_second_low), preferred_element_type=jnp.float32),
    )
    early, text_back, layout_back = lax.optimization_barrier((early, text_back, layout_back))
    grad_first, grad_second = scatter_early(count, *early)
    (text_grad, layout_grad), small_terms, text_rounded = jax.vmap(
        page_back_attn, in_axes=(0, 0, 0, 0, 0, 0, page_weights)
    )(text_in, layout_in, lengths, kept_all, text_back, layout_back, weights)
    totals = tuple(jnp.sum(term, 0) for term in small_terms)
    three_part = jnp.einsum(
        "sd,se->de", flat_rows(text_in), flat_rows(text_rounded), preferred_element_type=jnp.float32
    )
    out_part = jnp.einsum(
        "sd,se->de", flat_rows(kept_all[2]), flat_rows(text_first_low), preferred_element_type=jnp.float32
    )
    summed = scatter_late(count, jnp.concatenate([three_part, out_part], 1), totals)
    return (
        out_text,
        out_layout,
        text_grad,
        layout_grad,
        summed[0],
        grad_first,
        grad_second,
        summed[1],
        summed[2],
        summed[3],
        summed[4],
        summed[5],
    )


def solution(mesh):
    placed = (
        P(("dp", "shard"), None, None),
        P(("dp", "shard"), None, None),
        P(("dp", "shard")),
        P(("dp", "shard"), None),
        P(("dp", "shard"), None),
        P(("dp", "shard"), None),
        P(("dp", "shard")),
        P(("dp", "shard"), None),
        P(None, ("dp", "shard")),
        P(("dp", "shard"), None),
        P(("dp", "shard")),
        P(("dp", "shard"), None, None),
        P(("dp", "shard"), None, None),
    )
    return jax.shard_map(
        body,
        mesh=mesh,
        in_specs=placed,
        out_specs=(
            P(("dp", "shard"), None, None),
            P(("dp", "shard"), None, None),
            P(("dp", "shard"), None, None),
            P(("dp", "shard"), None, None),
            P(("dp", "shard"), None),
            P(("dp", "shard"), None),
            P(("dp", "shard"), None),
            P(("dp", "shard")),
            P(("dp", "shard"), None),
            P(None, ("dp", "shard")),
            P(("dp", "shard"), None),
            P(("dp", "shard")),
        ),
        check_vma=False,
    )
```

```python
import jax
import jax.numpy as jnp
from jax import lax
from jax.sharding import PartitionSpec as P


H = 12
HD = 64
LHD = 16


EPS = 1e-05
NEG = -1000000000.0


def normalize(values, scale_row, shift_row):
    centered = values - jnp.mean(values, -1, keepdims=True)
    variance = jnp.mean(centered * centered, -1, keepdims=True)
    return centered * lax.rsqrt(variance + EPS) * scale_row + shift_row


def gelu_exact(values):
    return jax.nn.gelu(values, approximate=False)


def vector_parts(packed, width):
    pieces = [packed[index * width : (index + 1) * width] for index in range(8)]
    return pieces + [packed[8 * width :]]


def split_heads(values):
    return values.reshape(values.shape[0], H, -1)


def block_of(attn, index, width, columns):
    if columns:
        return attn[:, index * width : (index + 1) * width]
    return attn[index * width : (index + 1) * width]


def project_three(inputs, attn, packed, width, columns):
    if columns:
        three = attn[:, 0 : 3 * width].reshape(width, 3, width)
        mixed = jnp.einsum("sd,dje->sje", inputs, three, preferred_element_type=jnp.float32)
    else:
        three = attn[0 : 3 * width].reshape(3, width, width)
        mixed = jnp.einsum("sd,jde->sje", inputs, three, preferred_element_type=jnp.float32)
    pieces = vector_parts(packed.astype(jnp.float32), width)
    offsets = jnp.stack([pieces[0], jnp.zeros_like(pieces[0]), pieces[1]])
    return (mixed + offsets[None]).astype(jnp.bfloat16)


def score_table(text_three, layout_three, valid):
    text_part = jnp.einsum(
        "qhd,khd->hqk",
        split_heads(text_three[:, 0]),
        split_heads(text_three[:, 1]),
        preferred_element_type=jnp.float32,
    )
    layout_part = jnp.einsum(
        "qhd,khd->hqk",
        split_heads(layout_three[:, 0]),
        split_heads(layout_three[:, 1]),
        preferred_element_type=jnp.float32,
    )
    joined = text_part * HD ** (-0.5) + layout_part * LHD ** (-0.5)
    return jnp.where(valid[None, None, :], joined, NEG)


def attend(text_three, layout_three, valid):
    scores = score_table(text_three, layout_three, valid)
    row_max = jnp.max(scores, -1, keepdims=True)
    exponent = jnp.exp(scores - row_max)
    row_total = jnp.sum(exponent, -1, keepdims=True)
    weights = (exponent / row_total).astype(jnp.bfloat16)
    slots = text_three.shape[0]
    text_ctx = jnp.einsum(
        "hqk,khd->qhd", weights, split_heads(text_three[:, 2]), preferred_element_type=jnp.float32
    )
    layout_ctx = jnp.einsum(
        "hqk,khd->qhd", weights, split_heads(layout_three[:, 2]), preferred_element_type=jnp.float32
    )
    log_total = (row_max + jnp.log(row_total))[..., 0]
    return (
        text_ctx.reshape(slots, -1).astype(jnp.bfloat16),
        layout_ctx.reshape(slots, -1).astype(jnp.bfloat16),
        log_total,
    )


def attend_back(text_three, layout_three, valid, log_total, text_grad, layout_grad):
    scores = score_table(text_three, layout_three, valid)
    probs = jnp.exp(scores - log_total[..., None])
    weights = probs.astype(jnp.bfloat16)
    text_heads = split_heads(text_grad)
    layout_heads = split_heads(layout_grad)
    text_dp = jnp.einsum(
        "qhd,khd->hqk",
        text_heads,
        split_heads(text_three[:, 2]),
        preferred_element_type=jnp.float32,
    )
    layout_dp = jnp.einsum(
        "qhd,khd->hqk",
        layout_heads,
        split_heads(layout_three[:, 2]),
        preferred_element_type=jnp.float32,
    )
    text_dv = jnp.einsum("hqk,qhd->khd", weights, text_heads, preferred_element_type=jnp.float32)
    layout_dv = jnp.einsum(
        "hqk,qhd->khd", weights, layout_heads, preferred_element_type=jnp.float32
    )
    text_ds = probs * (text_dp - jnp.sum(probs * text_dp, -1, keepdims=True))
    layout_ds = probs * (layout_dp - jnp.sum(probs * layout_dp, -1, keepdims=True))
    text_only = text_ds.astype(jnp.bfloat16)
    joint_ds = (text_ds + layout_ds).astype(jnp.bfloat16)
    text_dq = jnp.einsum(
        "hqk,khd->qhd", text_only, split_heads(text_three[:, 1]), preferred_element_type=jnp.float32
    ) * HD ** (-0.5)
    text_dk = jnp.einsum(
        "hqk,qhd->khd", text_only, split_heads(text_three[:, 0]), preferred_element_type=jnp.float32
    ) * HD ** (-0.5)
    layout_dq = jnp.einsum(
        "hqk,khd->qhd",
        joint_ds,
        split_heads(layout_three[:, 1]),
        preferred_element_type=jnp.float32,
    ) * LHD ** (-0.5)
    layout_dk = jnp.einsum(
        "hqk,qhd->khd",
        joint_ds,
        split_heads(layout_three[:, 0]),
        preferred_element_type=jnp.float32,
    ) * LHD ** (-0.5)
    slots = text_three.shape[0]
    text_all = jnp.stack([text_dq, text_dk, text_dv], 1).reshape(slots, 3, -1)
    layout_all = jnp.stack([layout_dq, layout_dk, layout_dv], 1).reshape(slots, 3, -1)
    return (text_all, layout_all)


def project_back(attn, width, columns, three_grad, first_grad):
    rounded_grad = three_grad.astype(jnp.bfloat16)
    if columns:
        three = attn[:, 0 : 3 * width].reshape(width, 3, width)
        input_grad = first_grad + jnp.einsum(
            "sje,dje->sd", rounded_grad, three, preferred_element_type=jnp.float32
        )
    else:
        three = attn[0 : 3 * width].reshape(3, width, width)
        input_grad = first_grad + jnp.einsum(
            "sje,jde->sd", rounded_grad, three, preferred_element_type=jnp.float32
        )
    column_sums = jnp.sum(rounded_grad.astype(jnp.float32), 0)
    return (input_grad, rounded_grad, column_sums[0], column_sums[2])


def branch_forward(inputs, context, attn, packed, first, second, width, columns):
    pieces = vector_parts(packed.astype(jnp.float32), width)
    out_block = block_of(attn, 3, width, columns)
    first_res = inputs.astype(jnp.float32) + (
        jnp.dot(context, out_block, preferred_element_type=jnp.float32) + pieces[2]
    )
    hidden = normalize(first_res, pieces[3], pieces[4])
    inner = (
        jnp.dot(hidden.astype(jnp.bfloat16), first, preferred_element_type=jnp.float32) + pieces[8]
    )
    activated = gelu_exact(inner).astype(jnp.bfloat16)
    second_res = hidden + (
        jnp.dot(activated, second, preferred_element_type=jnp.float32) + pieces[5]
    )
    result = normalize(second_res, pieces[6], pieces[7])
    return (result, (first_res, inner, second_res))


def branch_backward(attn, packed, first, second, width, columns, kept_rows, grad_out):
    first_res, inner, second_res = kept_rows
    pieces = vector_parts(packed.astype(jnp.float32), width)
    hidden, first_pull = jax.vjp(normalize, first_res, pieces[3], pieces[4])
    _, second_pull = jax.vjp(normalize, second_res, pieces[6], pieces[7])
    grad_second, late_scale, late_shift = second_pull(grad_out)
    round_second = grad_second.astype(jnp.bfloat16)
    activated, gelu_pull = jax.vjp(gelu_exact, inner)
    (grad_inner,) = gelu_pull(jnp.dot(round_second, second.T, preferred_element_type=jnp.float32))
    round_inner = grad_inner.astype(jnp.bfloat16)
    grad_hidden = grad_second + jnp.dot(round_inner, first.T, preferred_element_type=jnp.float32)
    grad_first, early_scale, early_shift = first_pull(grad_hidden)
    round_first = grad_first.astype(jnp.bfloat16)
    out_block = block_of(attn, 3, width, columns)
    grad_ctx = jnp.dot(round_first, out_block.T, preferred_element_type=jnp.float32).astype(
        jnp.bfloat16
    )
    operands = (
        hidden.astype(jnp.bfloat16),
        activated.astype(jnp.bfloat16),
        round_first,
        round_second,
        round_inner,
    )
    vector_sums = (
        jnp.sum(grad_first, 0),
        early_scale,
        early_shift,
        jnp.sum(grad_second, 0),
        late_scale,
        late_shift,
        jnp.sum(grad_inner, 0),
    )
    return (grad_first, grad_ctx, operands, vector_sums)


def page_forward(text_rows, layout_rows, length, weights):
    (
        text_attn,
        text_first,
        text_second,
        text_packed,
        layout_attn,
        layout_first,
        layout_second,
        layout_packed,
    ) = weights
    width = text_rows.shape[1]
    narrow = layout_rows.shape[1]
    valid = jnp.arange(text_rows.shape[0], dtype=jnp.int32) < length
    text_three = project_three(text_rows, text_attn, text_packed, width, True)
    layout_three = project_three(layout_rows, layout_attn, layout_packed, narrow, False)
    text_ctx, layout_ctx, log_total = attend(text_three, layout_three, valid)
    text_out, text_kept = branch_forward(
        text_rows, text_ctx, text_attn, text_packed, text_first, text_second, width, True
    )
    layout_out, layout_kept = branch_forward(
        layout_rows,
        layout_ctx,
        layout_attn,
        layout_packed,
        layout_first,
        layout_second,
        narrow,
        False,
    )
    mask = valid[:, None].astype(jnp.float32)
    outputs = ((text_out * mask).astype(jnp.bfloat16), (layout_out * mask).astype(jnp.bfloat16))
    kept_page = (text_three, layout_three, text_ctx, layout_ctx, log_total, text_kept, layout_kept)
    return (outputs, kept_page)


def page_back_ffn(length, kept_page, text_cot, layout_cot, weights):
    (
        text_attn,
        text_first,
        text_second,
        text_packed,
        layout_attn,
        layout_first,
        layout_second,
        layout_packed,
    ) = weights
    _, _, _, _, _, text_kept, layout_kept = kept_page
    width = text_attn.shape[0]
    narrow = layout_attn.shape[1]
    slots = text_cot.shape[0]
    valid = jnp.arange(slots, dtype=jnp.int32) < length
    mask = valid[:, None].astype(jnp.float32)
    text_back = branch_backward(
        text_attn,
        text_packed,
        text_first,
        text_second,
        width,
        True,
        text_kept,
        text_cot.astype(jnp.float32) * mask,
    )
    layout_back = branch_backward(
        layout_attn,
        layout_packed,
        layout_first,
        layout_second,
        narrow,
        False,
        layout_kept,
        layout_cot.astype(jnp.float32) * mask,
    )
    return (text_back, layout_back)


def page_back_attn(text_rows, layout_rows, length, kept_page, text_back, layout_back, weights):
    (text_attn, _, _, _, layout_attn, _, _, _) = weights
    text_three, layout_three, _, layout_ctx, log_total, _, _ = kept_page
    width = text_rows.shape[1]
    narrow = layout_rows.shape[1]
    slots = text_rows.shape[0]
    valid = jnp.arange(slots, dtype=jnp.int32) < length
    text_res_grad, text_ctx_grad, _, text_sums = text_back
    layout_res_grad, layout_ctx_grad, layout_ops, layout_sums = layout_back
    text_three_grad, layout_three_grad = attend_back(
        text_three, layout_three, valid, log_total, text_ctx_grad, layout_ctx_grad
    )
    text_in_grad, text_rounded, text_query_bias, text_value_bias = project_back(
        text_attn, width, True, text_three_grad, text_res_grad
    )
    layout_in_grad, layout_rounded, layout_query_bias, layout_value_bias = project_back(
        layout_attn, narrow, False, layout_three_grad, layout_res_grad
    )
    hidden_low, active_low, first_low, second_low, inner_low = layout_ops
    three_w = jnp.einsum(
        "sd,sje->jde", layout_rows, layout_rounded, preferred_element_type=jnp.float32
    ).reshape(3 * narrow, narrow)
    out_w = jnp.einsum("sd,se->de", layout_ctx, first_low, preferred_element_type=jnp.float32)
    layout_attn_grad = jnp.concatenate([three_w, out_w], 0)
    layout_first_grad = jnp.einsum(
        "sd,sf->df", hidden_low, inner_low, preferred_element_type=jnp.float32
    )
    layout_second_grad = jnp.einsum(
        "sf,sd->fd", active_low, second_low, preferred_element_type=jnp.float32
    )
    layout_vec_grad = jnp.concatenate([layout_query_bias, layout_value_bias] + list(layout_sums))
    text_vec_grad = jnp.concatenate([text_query_bias, text_value_bias] + list(text_sums))
    small_terms = (
        text_vec_grad,
        layout_attn_grad,
        layout_first_grad,
        layout_second_grad,
        layout_vec_grad,
    )
    return ((text_in_grad, layout_in_grad), small_terms, text_rounded.reshape(slots, 3 * width))


def flat_rows(values):
    return values.reshape(-1, values.shape[-1])


AXES = ("dp", "shard")


def rows_for(size, width, aligned):
    rows = -(-size // width)
    if aligned:
        rows = -(-rows // 8) * 8
    return rows


def pack_rows(pieces, width, aligned):
    flat = jnp.concatenate([piece.reshape(-1) for piece in pieces])
    rows = rows_for(flat.shape[0], width, aligned)
    return jnp.pad(flat, (0, rows * width - flat.shape[0])).reshape(rows, width)


def unpack_small(flat, count, shapes):
    sizes = [rows * cols for rows, cols in shapes]
    offsets = [sum(sizes[:index]) for index in range(len(sizes))]
    parts = [flat[:, offset : offset + size] for offset, size in zip(offsets, sizes)]
    (attn_rows, attn_cols), (w1_rows, w1_cols), (w2_rows, w2_cols) = shapes[1:4]
    return (
        parts[0].reshape(-1),
        parts[1].reshape(count * attn_rows, attn_cols),
        parts[2].reshape(count, w1_rows, w1_cols).transpose(1, 0, 2).reshape(w1_rows, count * w1_cols),
        parts[3].reshape(count * w2_rows, w2_cols),
        parts[4].reshape(-1),
    )


def gather_weights(text_attn, text_w1, text_w2, text_vectors, layout_attn, layout_w1, layout_w2, layout_vectors):
    rows, width = text_attn.shape
    aligned = rows % 8 == 0
    small = (text_vectors, layout_attn, layout_w1, layout_w2, layout_vectors)
    small_rows = pack_rows(small, width, aligned)
    first = jnp.concatenate([text_attn, small_rows], 0)
    first_all = lax.all_gather(first, AXES, axis=0, tiled=True)
    count = first_all.shape[0] // first.shape[0]
    first_all = first_all.reshape(count, first.shape[0], width)
    full_attn = first_all[:, :rows].reshape(count * rows, width)
    small_flat = first_all[:, rows:].reshape(count, -1)
    shapes = [(1, text_vectors.shape[0]), layout_attn.shape, layout_w1.shape, layout_w2.shape, (1, layout_vectors.shape[0])]
    full_small = unpack_small(small_flat, count, shapes)
    w2_rows = text_w2.shape[0]
    second = jnp.concatenate([text_w1, text_w2.reshape(rows, -1)], 0)
    second_all = lax.all_gather(second, AXES, axis=0, tiled=True).reshape(count, 2 * rows, width)
    full_w1 = second_all[:, :rows].reshape(count * rows, width)
    full_w2 = second_all[:, rows:].reshape(count * w2_rows, text_w2.shape[1])
    return (full_attn, full_w1, full_w2) + full_small


def small_blocks(count, text_vec_grad, layout_attn_grad, layout_w1_grad, layout_w2_grad, layout_vec_grad):
    local_w1_cols = layout_w1_grad.shape[1] // count
    return (
        text_vec_grad.reshape(count, -1),
        layout_attn_grad.reshape(count, -1),
        layout_w1_grad.reshape(layout_w1_grad.shape[0], count, local_w1_cols)
        .transpose(1, 0, 2)
        .reshape(count, -1),
        layout_w2_grad.reshape(count, -1),
        layout_vec_grad.reshape(count, -1),
    )


def scatter_late(count, grad_attn, small_grads):
    width = grad_attn.shape[1]
    rows = grad_attn.shape[0] // count
    blocks = small_blocks(count, *small_grads)
    joined = jnp.concatenate(blocks, 1)
    size = joined.shape[1]
    small_rows = rows_for(size, width, rows % 8 == 0)
    joined = jnp.pad(joined, ((0, 0), (0, small_rows * width - size))).reshape(count, small_rows, width)
    packed = jnp.concatenate([grad_attn.reshape(count, rows, width), joined], 1)
    summed = lax.psum_scatter(
        packed.reshape(-1, width).astype(jnp.bfloat16), AXES, scatter_dimension=0, tiled=True
    ).astype(jnp.float32)
    attn_part = summed[:rows]
    flat = summed[rows:].reshape(-1)
    sizes = [block.shape[1] for block in blocks]
    offsets = [sum(sizes[:index]) for index in range(len(sizes))]
    parts = [flat[offset : offset + size] for offset, size in zip(offsets, sizes)]
    _, layout_attn_grad, layout_w1_grad, layout_w2_grad, _ = small_grads
    local_w1_cols = layout_w1_grad.shape[1] // count
    return (
        attn_part,
        parts[0],
        parts[1].reshape(layout_attn_grad.shape[0] // count, layout_attn_grad.shape[1]),
        parts[2].reshape(layout_w1_grad.shape[0], local_w1_cols),
        parts[3].reshape(layout_w2_grad.shape[0] // count, layout_w2_grad.shape[1]),
        parts[4],
    )


def scatter_early(count, grad_first, grad_second):
    width = grad_first.shape[1]
    rows = grad_first.shape[0] // count
    packed = jnp.concatenate(
        [grad_first.reshape(count, rows, width), grad_second.reshape(count, rows, width)], 1
    )
    summed = lax.psum_scatter(
        packed.reshape(-1, width).astype(jnp.bfloat16), AXES, scatter_dimension=0, tiled=True
    ).astype(jnp.float32)
    return (summed[:rows], summed[rows:].reshape(-1, grad_second.shape[1]))


def body(
    text_in,
    layout_in,
    lengths,
    text_attn,
    text_w1,
    text_w2,
    text_vectors,
    layout_attn,
    layout_w1,
    layout_w2,
    layout_vectors,
    cot_text,
    cot_layout,
):
    count = lax.psum(1, AXES)
    weights = gather_weights(
        text_attn, text_w1, text_w2, text_vectors, layout_attn, layout_w1, layout_w2, layout_vectors
    )

    page_weights = (None,) * len(weights)
    outputs, kept_all = jax.vmap(page_forward, in_axes=(0, 0, 0, page_weights))(
        text_in, layout_in, lengths, weights
    )
    out_text, out_layout = outputs
    text_back, layout_back = jax.vmap(page_back_ffn, in_axes=(0, 0, 0, 0, page_weights))(
        lengths, kept_all, cot_text, cot_layout, weights
    )
    text_hidden, text_active, text_first_low, text_second_low, text_inner_low = text_back[2]
    early = (
        jnp.einsum("sd,sf->df", flat_rows(text_hidden), flat_rows(text_inner_low), preferred_element_type=jnp.float32),
        jnp.einsum("sf,sd->fd", flat_rows(text_active), flat_rows(text_second_low), preferred_element_type=jnp.float32),
    )
    early, text_back, layout_back = lax.optimization_barrier((early, text_back, layout_back))
    grad_first, grad_second = scatter_early(count, *early)
    (text_grad, layout_grad), small_terms, text_rounded = jax.vmap(
        page_back_attn, in_axes=(0, 0, 0, 0, 0, 0, page_weights)
    )(text_in, layout_in, lengths, kept_all, text_back, layout_back, weights)
    totals = tuple(jnp.sum(term, 0) for term in small_terms)
    three_part = jnp.einsum(
        "sd,se->de", flat_rows(text_in), flat_rows(text_rounded), preferred_element_type=jnp.float32
    )
    out_part = jnp.einsum(
        "sd,se->de", flat_rows(kept_all[2]), flat_rows(text_first_low), preferred_element_type=jnp.float32
    )
    summed = scatter_late(count, jnp.concatenate([three_part, out_part], 1), totals)
    return (
        out_text,
        out_layout,
        text_grad,
        layout_grad,
        summed[0],
        grad_first,
        grad_second,
        summed[1],
        summed[2],
        summed[3],
        summed[4],
        summed[5],
    )


def solution(mesh):
    placed = (
        P(("dp", "shard"), None, None),
        P(("dp", "shard"), None, None),
        P(("dp", "shard")),
        P(("dp", "shard"), None),
        P(("dp", "shard"), None),
        P(("dp", "shard"), None),
        P(("dp", "shard")),
        P(("dp", "shard"), None),
        P(None, ("dp", "shard")),
        P(("dp", "shard"), None),
        P(("dp", "shard")),
        P(("dp", "shard"), None, None),
        P(("dp", "shard"), None, None),
    )
    return jax.shard_map(
        body,
        mesh=mesh,
        in_specs=placed,
        out_specs=(
            P(("dp", "shard"), None, None),
            P(("dp", "shard"), None, None),
            P(("dp", "shard"), None, None),
            P(("dp", "shard"), None, None),
            P(("dp", "shard"), None),
            P(("dp", "shard"), None),
            P(("dp", "shard"), None),
            P(("dp", "shard")),
            P(("dp", "shard"), None),
            P(None, ("dp", "shard")),
            P(("dp", "shard"), None),
            P(("dp", "shard")),
        ),
        check_vma=False,
    )
```

```python
import jax
import jax.numpy as jnp
from jax import lax
from jax.sharding import PartitionSpec as P


H = 12
HD = 64
LHD = 16


EPS = 1e-05
NEG = -1000000000.0


def normalize(values, scale_row, shift_row):
    centered = values - jnp.mean(values, -1, keepdims=True)
    variance = jnp.mean(centered * centered, -1, keepdims=True)
    return centered * lax.rsqrt(variance + EPS) * scale_row + shift_row


def gelu_exact(values):
    return jax.nn.gelu(values, approximate=False)


def vector_parts(packed, width):
    pieces = [packed[index * width : (index + 1) * width] for index in range(8)]
    return pieces + [packed[8 * width :]]


def split_heads(values):
    return values.reshape(values.shape[0], H, -1)


def block_of(attn, index, width, columns):
    if columns:
        return attn[:, index * width : (index + 1) * width]
    return attn[index * width : (index + 1) * width]


def project_three(inputs, attn, packed, width, columns):
    if columns:
        three = attn[:, 0 : 3 * width].reshape(width, 3, width)
        mixed = jnp.einsum("sd,dje->sje", inputs, three, preferred_element_type=jnp.float32)
    else:
        three = attn[0 : 3 * width].reshape(3, width, width)
        mixed = jnp.einsum("sd,jde->sje", inputs, three, preferred_element_type=jnp.float32)
    pieces = vector_parts(packed.astype(jnp.float32), width)
    offsets = jnp.stack([pieces[0], jnp.zeros_like(pieces[0]), pieces[1]])
    return (mixed + offsets[None]).astype(jnp.bfloat16)


def score_table(text_three, layout_three, valid):
    text_part = jnp.einsum(
        "qhd,khd->hqk",
        split_heads(text_three[:, 0]),
        split_heads(text_three[:, 1]),
        preferred_element_type=jnp.float32,
    )
    layout_part = jnp.einsum(
        "qhd,khd->hqk",
        split_heads(layout_three[:, 0]),
        split_heads(layout_three[:, 1]),
        preferred_element_type=jnp.float32,
    )
    joined = text_part * HD ** (-0.5) + layout_part * LHD ** (-0.5)
    return jnp.where(valid[None, None, :], joined, NEG)


def attend(text_three, layout_three, valid):
    scores = score_table(text_three, layout_three, valid)
    row_max = jnp.max(scores, -1, keepdims=True)
    exponent = jnp.exp(scores - row_max)
    row_total = jnp.sum(exponent, -1, keepdims=True)
    weights = (exponent / row_total).astype(jnp.bfloat16)
    slots = text_three.shape[0]
    text_ctx = jnp.einsum(
        "hqk,khd->qhd", weights, split_heads(text_three[:, 2]), preferred_element_type=jnp.float32
    )
    layout_ctx = jnp.einsum(
        "hqk,khd->qhd", weights, split_heads(layout_three[:, 2]), preferred_element_type=jnp.float32
    )
    log_total = (row_max + jnp.log(row_total))[..., 0]
    return (
        text_ctx.reshape(slots, -1).astype(jnp.bfloat16),
        layout_ctx.reshape(slots, -1).astype(jnp.bfloat16),
        log_total,
    )


def attend_back(text_three, layout_three, valid, log_total, text_grad, layout_grad):
    scores = score_table(text_three, layout_three, valid)
    probs = jnp.exp(scores - log_total[..., None])
    weights = probs.astype(jnp.bfloat16)
    text_heads = split_heads(text_grad)
    layout_heads = split_heads(layout_grad)
    text_dp = jnp.einsum(
        "qhd,khd->hqk",
        text_heads,
        split_heads(text_three[:, 2]),
        preferred_element_type=jnp.float32,
    )
    layout_dp = jnp.einsum(
        "qhd,khd->hqk",
        layout_heads,
        split_heads(layout_three[:, 2]),
        preferred_element_type=jnp.float32,
    )
    text_dv = jnp.einsum("hqk,qhd->khd", weights, text_heads, preferred_element_type=jnp.float32)
    layout_dv = jnp.einsum(
        "hqk,qhd->khd", weights, layout_heads, preferred_element_type=jnp.float32
    )
    text_ds = probs * (text_dp - jnp.sum(probs * text_dp, -1, keepdims=True))
    layout_ds = probs * (layout_dp - jnp.sum(probs * layout_dp, -1, keepdims=True))
    text_only, joint_ds = lax.optimization_barrier(
        (text_ds.astype(jnp.bfloat16), (text_ds + layout_ds).astype(jnp.bfloat16))
    )
    text_dq = jnp.einsum(
        "hqk,khd->qhd", text_only, split_heads(text_three[:, 1]), preferred_element_type=jnp.float32
    ) * HD ** (-0.5)
    text_dk = jnp.einsum(
        "hqk,qhd->khd", text_only, split_heads(text_three[:, 0]), preferred_element_type=jnp.float32
    ) * HD ** (-0.5)
    layout_dq = jnp.einsum(
        "hqk,khd->qhd",
        joint_ds,
        split_heads(layout_three[:, 1]),
        preferred_element_type=jnp.float32,
    ) * LHD ** (-0.5)
    layout_dk = jnp.einsum(
        "hqk,qhd->khd",
        joint_ds,
        split_heads(layout_three[:, 0]),
        preferred_element_type=jnp.float32,
    ) * LHD ** (-0.5)
    slots = text_three.shape[0]
    text_all = jnp.stack([text_dq, text_dk, text_dv], 1).reshape(slots, 3, -1)
    layout_all = jnp.stack([layout_dq, layout_dk, layout_dv], 1).reshape(slots, 3, -1)
    return (text_all, layout_all)


def project_back(attn, width, columns, three_grad, first_grad):
    rounded_grad = three_grad.astype(jnp.bfloat16)
    if columns:
        three = attn[:, 0 : 3 * width].reshape(width, 3, width)
        input_grad = first_grad + jnp.einsum(
            "sje,dje->sd", rounded_grad, three, preferred_element_type=jnp.float32
        )
    else:
        three = attn[0 : 3 * width].reshape(3, width, width)
        input_grad = first_grad + jnp.einsum(
            "sje,jde->sd", rounded_grad, three, preferred_element_type=jnp.float32
        )
    column_sums = jnp.sum(rounded_grad.astype(jnp.float32), 0)
    return (input_grad, rounded_grad, column_sums[0], column_sums[2])


def branch_forward(inputs, context, attn, packed, first, second, width, columns):
    pieces = vector_parts(packed.astype(jnp.float32), width)
    out_block = block_of(attn, 3, width, columns)
    first_res = inputs.astype(jnp.float32) + (
        jnp.dot(context, out_block, preferred_element_type=jnp.float32) + pieces[2]
    )
    hidden = normalize(first_res, pieces[3], pieces[4])
    inner = (
        jnp.dot(hidden.astype(jnp.bfloat16), first, preferred_element_type=jnp.float32) + pieces[8]
    )
    activated = gelu_exact(inner).astype(jnp.bfloat16)
    second_res = hidden + (
        jnp.dot(activated, second, preferred_element_type=jnp.float32) + pieces[5]
    )
    result = normalize(second_res, pieces[6], pieces[7])
    return (result, (first_res, inner, second_res))


def branch_backward(attn, packed, first, second, width, columns, kept_rows, grad_out):
    first_res, inner, second_res = kept_rows
    pieces = vector_parts(packed.astype(jnp.float32), width)
    hidden, first_pull = jax.vjp(normalize, first_res, pieces[3], pieces[4])
    _, second_pull = jax.vjp(normalize, second_res, pieces[6], pieces[7])
    grad_second, late_scale, late_shift = second_pull(grad_out)
    round_second = grad_second.astype(jnp.bfloat16)
    activated, gelu_pull = jax.vjp(gelu_exact, inner)
    (grad_inner,) = gelu_pull(jnp.dot(round_second, second.T, preferred_element_type=jnp.float32))
    round_inner = grad_inner.astype(jnp.bfloat16)
    grad_hidden = grad_second + jnp.dot(round_inner, first.T, preferred_element_type=jnp.float32)
    grad_first, early_scale, early_shift = first_pull(grad_hidden)
    round_first = grad_first.astype(jnp.bfloat16)
    out_block = block_of(attn, 3, width, columns)
    grad_ctx = jnp.dot(round_first, out_block.T, preferred_element_type=jnp.float32).astype(
        jnp.bfloat16
    )
    operands = (
        hidden.astype(jnp.bfloat16),
        activated.astype(jnp.bfloat16),
        round_first,
        round_second,
        round_inner,
    )
    vector_sums = (
        jnp.sum(grad_first, 0),
        early_scale,
        early_shift,
        jnp.sum(grad_second, 0),
        late_scale,
        late_shift,
        jnp.sum(grad_inner, 0),
    )
    return (grad_first, grad_ctx, operands, vector_sums)


def page_forward(text_rows, layout_rows, length, weights):
    (
        text_attn,
        text_first,
        text_second,
        text_packed,
        layout_attn,
        layout_first,
        layout_second,
        layout_packed,
    ) = weights
    width = text_rows.shape[1]
    narrow = layout_rows.shape[1]
    valid = jnp.arange(text_rows.shape[0], dtype=jnp.int32) < length
    text_three = project_three(text_rows, text_attn, text_packed, width, True)
    layout_three = project_three(layout_rows, layout_attn, layout_packed, narrow, False)
    text_ctx, layout_ctx, log_total = attend(text_three, layout_three, valid)
    text_out, text_kept = branch_forward(
        text_rows, text_ctx, text_attn, text_packed, text_first, text_second, width, True
    )
    layout_out, layout_kept = branch_forward(
        layout_rows,
        layout_ctx,
        layout_attn,
        layout_packed,
        layout_first,
        layout_second,
        narrow,
        False,
    )
    mask = valid[:, None].astype(jnp.float32)
    outputs = ((text_out * mask).astype(jnp.bfloat16), (layout_out * mask).astype(jnp.bfloat16))
    kept_page = (text_three, layout_three, text_ctx, layout_ctx, log_total, text_kept, layout_kept)
    return (outputs, kept_page)


def page_back_ffn(length, kept_page, text_cot, layout_cot, weights):
    (
        text_attn,
        text_first,
        text_second,
        text_packed,
        layout_attn,
        layout_first,
        layout_second,
        layout_packed,
    ) = weights
    _, _, _, _, _, text_kept, layout_kept = kept_page
    width = text_attn.shape[0]
    narrow = layout_attn.shape[1]
    slots = text_cot.shape[0]
    valid = jnp.arange(slots, dtype=jnp.int32) < length
    mask = valid[:, None].astype(jnp.float32)
    text_back = branch_backward(
        text_attn,
        text_packed,
        text_first,
        text_second,
        width,
        True,
        text_kept,
        text_cot.astype(jnp.float32) * mask,
    )
    layout_back = branch_backward(
        layout_attn,
        layout_packed,
        layout_first,
        layout_second,
        narrow,
        False,
        layout_kept,
        layout_cot.astype(jnp.float32) * mask,
    )
    return (text_back, layout_back)


def page_back_attn(text_rows, layout_rows, length, kept_page, text_back, layout_back, weights):
    (text_attn, _, _, _, layout_attn, _, _, _) = weights
    text_three, layout_three, _, layout_ctx, log_total, _, _ = kept_page
    width = text_rows.shape[1]
    narrow = layout_rows.shape[1]
    slots = text_rows.shape[0]
    valid = jnp.arange(slots, dtype=jnp.int32) < length
    text_res_grad, text_ctx_grad, _, text_sums = text_back
    layout_res_grad, layout_ctx_grad, layout_ops, layout_sums = layout_back
    text_three_grad, layout_three_grad = attend_back(
        text_three, layout_three, valid, log_total, text_ctx_grad, layout_ctx_grad
    )
    text_in_grad, text_rounded, text_query_bias, text_value_bias = project_back(
        text_attn, width, True, text_three_grad, text_res_grad
    )
    layout_in_grad, layout_rounded, layout_query_bias, layout_value_bias = project_back(
        layout_attn, narrow, False, layout_three_grad, layout_res_grad
    )
    hidden_low, active_low, first_low, second_low, inner_low = layout_ops
    three_w = jnp.einsum(
        "sd,sje->jde", layout_rows, layout_rounded, preferred_element_type=jnp.float32
    ).reshape(3 * narrow, narrow)
    out_w = jnp.einsum("sd,se->de", layout_ctx, first_low, preferred_element_type=jnp.float32)
    layout_attn_grad = jnp.concatenate([three_w, out_w], 0)
    layout_first_grad = jnp.einsum(
        "sd,sf->df", hidden_low, inner_low, preferred_element_type=jnp.float32
    )
    layout_second_grad = jnp.einsum(
        "sf,sd->fd", active_low, second_low, preferred_element_type=jnp.float32
    )
    layout_vec_grad = jnp.concatenate([layout_query_bias, layout_value_bias] + list(layout_sums))
    text_vec_grad = jnp.concatenate([text_query_bias, text_value_bias] + list(text_sums))
    small_terms = (
        text_vec_grad,
        layout_attn_grad,
        layout_first_grad,
        layout_second_grad,
        layout_vec_grad,
    )
    return ((text_in_grad, layout_in_grad), small_terms, text_rounded.reshape(slots, 3 * width))


def flat_rows(values):
    return values.reshape(-1, values.shape[-1])


AXES = ("dp", "shard")


def rows_for(size, width, aligned):
    rows = -(-size // width)
    if aligned:
        rows = -(-rows // 8) * 8
    return rows


def pack_rows(pieces, width, aligned):
    flat = jnp.concatenate([piece.reshape(-1) for piece in pieces])
    rows = rows_for(flat.shape[0], width, aligned)
    return jnp.pad(flat, (0, rows * width - flat.shape[0])).reshape(rows, width)


def unpack_small(flat, count, shapes):
    sizes = [rows * cols for rows, cols in shapes]
    offsets = [sum(sizes[:index]) for index in range(len(sizes))]
    parts = [flat[:, offset : offset + size] for offset, size in zip(offsets, sizes)]
    (attn_rows, attn_cols), (w1_rows, w1_cols), (w2_rows, w2_cols) = shapes[1:4]
    return (
        parts[0].reshape(-1),
        parts[1].reshape(count * attn_rows, attn_cols),
        parts[2].reshape(count, w1_rows, w1_cols).transpose(1, 0, 2).reshape(w1_rows, count * w1_cols),
        parts[3].reshape(count * w2_rows, w2_cols),
        parts[4].reshape(-1),
    )


def gather_weights(text_attn, text_w1, text_w2, text_vectors, layout_attn, layout_w1, layout_w2, layout_vectors):
    rows, width = text_attn.shape
    aligned = rows % 8 == 0
    small = (text_vectors, layout_attn, layout_w1, layout_w2, layout_vectors)
    small_rows = pack_rows(small, width, aligned)
    first = jnp.concatenate([text_attn, small_rows], 0)
    first_all = lax.all_gather(first, AXES, axis=0, tiled=True)
    count = first_all.shape[0] // first.shape[0]
    first_all = first_all.reshape(count, first.shape[0], width)
    full_attn = first_all[:, :rows].reshape(count * rows, width)
    small_flat = first_all[:, rows:].reshape(count, -1)
    shapes = [(1, text_vectors.shape[0]), layout_attn.shape, layout_w1.shape, layout_w2.shape, (1, layout_vectors.shape[0])]
    full_small = unpack_small(small_flat, count, shapes)
    full_w1 = lax.all_gather(text_w1, AXES, axis=0, tiled=True)
    full_w2 = lax.all_gather(text_w2, AXES, axis=0, tiled=True)
    return (full_attn, full_w1, full_w2) + full_small


def small_blocks(count, text_vec_grad, layout_attn_grad, layout_w1_grad, layout_w2_grad, layout_vec_grad):
    local_w1_cols = layout_w1_grad.shape[1] // count
    return (
        text_vec_grad.reshape(count, -1),
        layout_attn_grad.reshape(count, -1),
        layout_w1_grad.reshape(layout_w1_grad.shape[0], count, local_w1_cols)
        .transpose(1, 0, 2)
        .reshape(count, -1),
        layout_w2_grad.reshape(count, -1),
        layout_vec_grad.reshape(count, -1),
    )


def scatter_late(count, grad_attn, small_grads):
    width = grad_attn.shape[1]
    rows = grad_attn.shape[0] // count
    blocks = small_blocks(count, *small_grads)
    joined = jnp.concatenate(blocks, 1)
    size = joined.shape[1]
    small_rows = rows_for(size, width, rows % 8 == 0)
    joined = jnp.pad(joined, ((0, 0), (0, small_rows * width - size))).reshape(count, small_rows, width)
    packed = jnp.concatenate([grad_attn.reshape(count, rows, width), joined], 1)
    summed = lax.psum_scatter(
        packed.reshape(-1, width).astype(jnp.bfloat16), AXES, scatter_dimension=0, tiled=True
    ).astype(jnp.float32)
    attn_part = summed[:rows]
    flat = summed[rows:].reshape(-1)
    sizes = [block.shape[1] for block in blocks]
    offsets = [sum(sizes[:index]) for index in range(len(sizes))]
    parts = [flat[offset : offset + size] for offset, size in zip(offsets, sizes)]
    _, layout_attn_grad, layout_w1_grad, layout_w2_grad, _ = small_grads
    local_w1_cols = layout_w1_grad.shape[1] // count
    return (
        attn_part,
        parts[0],
        parts[1].reshape(layout_attn_grad.shape[0] // count, layout_attn_grad.shape[1]),
        parts[2].reshape(layout_w1_grad.shape[0], local_w1_cols),
        parts[3].reshape(layout_w2_grad.shape[0] // count, layout_w2_grad.shape[1]),
        parts[4],
    )


def pack_early(count, grad_first, grad_second):
    width = grad_first.shape[1]
    rows = grad_first.shape[0] // count
    packed = jnp.concatenate(
        [grad_first.reshape(count, rows, width), grad_second.reshape(count, rows, width)], 1
    )
    return packed.reshape(-1, width).astype(jnp.bfloat16)


def scatter_early(count, packed, second_shape):
    rows = packed.shape[0] // (2 * count)
    summed = lax.psum_scatter(packed, AXES, scatter_dimension=0, tiled=True).astype(jnp.float32)
    return (summed[:rows], summed[rows:].reshape(-1, second_shape[1]))


def body(
    text_in,
    layout_in,
    lengths,
    text_attn,
    text_w1,
    text_w2,
    text_vectors,
    layout_attn,
    layout_w1,
    layout_w2,
    layout_vectors,
    cot_text,
    cot_layout,
):
    count = lax.psum(1, AXES)
    weights = gather_weights(
        text_attn, text_w1, text_w2, text_vectors, layout_attn, layout_w1, layout_w2, layout_vectors
    )

    page_weights = (None,) * len(weights)
    outputs, kept_all = jax.vmap(page_forward, in_axes=(0, 0, 0, page_weights))(
        text_in, layout_in, lengths, weights
    )
    out_text, out_layout = outputs
    text_back, layout_back = jax.vmap(page_back_ffn, in_axes=(0, 0, 0, 0, page_weights))(
        lengths, kept_all, cot_text, cot_layout, weights
    )
    text_hidden, text_active, text_first_low, text_second_low, text_inner_low = text_back[2]
    early = (
        jnp.einsum("sd,sf->df", flat_rows(text_hidden), flat_rows(text_inner_low), preferred_element_type=jnp.float32),
        jnp.einsum("sf,sd->fd", flat_rows(text_active), flat_rows(text_second_low), preferred_element_type=jnp.float32),
    )
    packed = pack_early(count, *early)
    packed, text_back, layout_back = lax.optimization_barrier((packed, text_back, layout_back))
    grad_first, grad_second = scatter_early(count, packed, early[1].shape)
    (text_grad, layout_grad), small_terms, text_rounded = jax.vmap(
        page_back_attn, in_axes=(0, 0, 0, 0, 0, 0, page_weights)
    )(text_in, layout_in, lengths, kept_all, text_back, layout_back, weights)
    totals = tuple(jnp.sum(term, 0) for term in small_terms)
    three_part = jnp.einsum(
        "sd,se->de", flat_rows(text_in), flat_rows(text_rounded), preferred_element_type=jnp.float32
    )
    out_part = jnp.einsum(
        "sd,se->de", flat_rows(kept_all[2]), flat_rows(text_first_low), preferred_element_type=jnp.float32
    )
    summed = scatter_late(count, jnp.concatenate([three_part, out_part], 1), totals)
    return (
        out_text,
        out_layout,
        text_grad,
        layout_grad,
        summed[0],
        grad_first,
        grad_second,
        summed[1],
        summed[2],
        summed[3],
        summed[4],
        summed[5],
    )


def solution(mesh):
    placed = (
        P(("dp", "shard"), None, None),
        P(("dp", "shard"), None, None),
        P(("dp", "shard")),
        P(("dp", "shard"), None),
        P(("dp", "shard"), None),
        P(("dp", "shard"), None),
        P(("dp", "shard")),
        P(("dp", "shard"), None),
        P(None, ("dp", "shard")),
        P(("dp", "shard"), None),
        P(("dp", "shard")),
        P(("dp", "shard"), None, None),
        P(("dp", "shard"), None, None),
    )
    return jax.shard_map(
        body,
        mesh=mesh,
        in_specs=placed,
        out_specs=(
            P(("dp", "shard"), None, None),
            P(("dp", "shard"), None, None),
            P(("dp", "shard"), None, None),
            P(("dp", "shard"), None, None),
            P(("dp", "shard"), None),
            P(("dp", "shard"), None),
            P(("dp", "shard"), None),
            P(("dp", "shard")),
            P(("dp", "shard"), None),
            P(None, ("dp", "shard")),
            P(("dp", "shard"), None),
            P(("dp", "shard")),
        ),
        check_vma=False,
    )
```

```python
import jax
import jax.numpy as jnp
from jax import lax
from jax.sharding import PartitionSpec as P


H = 12
HD = 64
LHD = 16


EPS = 1e-05
NEG = -1000000000.0


def normalize(values, scale_row, shift_row):
    centered = values - jnp.mean(values, -1, keepdims=True)
    variance = jnp.mean(centered * centered, -1, keepdims=True)
    return centered * lax.rsqrt(variance + EPS) * scale_row + shift_row


def gelu_exact(values):
    return jax.nn.gelu(values, approximate=False)


def vector_parts(packed, width):
    pieces = [packed[index * width : (index + 1) * width] for index in range(8)]
    return pieces + [packed[8 * width :]]


def split_heads(values):
    return values.reshape(values.shape[0], H, -1)


def block_of(attn, index, width, columns):
    if columns:
        return attn[:, index * width : (index + 1) * width]
    return attn[index * width : (index + 1) * width]


def project_three(inputs, attn, packed, width, columns):
    if columns:
        three = attn[:, 0 : 3 * width].reshape(width, 3, width)
        mixed = jnp.einsum("sd,dje->sje", inputs, three, preferred_element_type=jnp.float32)
    else:
        three = attn[0 : 3 * width].reshape(3, width, width)
        mixed = jnp.einsum("sd,jde->sje", inputs, three, preferred_element_type=jnp.float32)
    pieces = vector_parts(packed.astype(jnp.float32), width)
    offsets = jnp.stack([pieces[0], jnp.zeros_like(pieces[0]), pieces[1]])
    return (mixed + offsets[None]).astype(jnp.bfloat16)


def score_table(text_three, layout_three, valid):
    text_part = jnp.einsum(
        "qhd,khd->hqk",
        split_heads(text_three[:, 0]),
        split_heads(text_three[:, 1]),
        preferred_element_type=jnp.float32,
    )
    layout_part = jnp.einsum(
        "qhd,khd->hqk",
        split_heads(layout_three[:, 0]),
        split_heads(layout_three[:, 1]),
        preferred_element_type=jnp.float32,
    )
    joined = text_part * HD ** (-0.5) + layout_part * LHD ** (-0.5)
    return jnp.where(valid[None, None, :], joined, NEG)


def attend(text_three, layout_three, valid):
    scores = score_table(text_three, layout_three, valid)
    row_max = jnp.max(scores, -1, keepdims=True)
    exponent = jnp.exp(scores - row_max)
    row_total = jnp.sum(exponent, -1, keepdims=True)
    weights = (exponent / row_total).astype(jnp.bfloat16)
    slots = text_three.shape[0]
    text_ctx = jnp.einsum(
        "hqk,khd->qhd", weights, split_heads(text_three[:, 2]), preferred_element_type=jnp.float32
    )
    layout_ctx = jnp.einsum(
        "hqk,khd->qhd", weights, split_heads(layout_three[:, 2]), preferred_element_type=jnp.float32
    )
    log_total = (row_max + jnp.log(row_total))[..., 0]
    return (
        text_ctx.reshape(slots, -1).astype(jnp.bfloat16),
        layout_ctx.reshape(slots, -1).astype(jnp.bfloat16),
        log_total,
    )


def attend_back(text_three, layout_three, valid, log_total, text_grad, layout_grad):
    scores = score_table(text_three, layout_three, valid)
    probs = jnp.exp(scores - log_total[..., None])
    weights = probs.astype(jnp.bfloat16)
    text_heads = split_heads(text_grad)
    layout_heads = split_heads(layout_grad)
    text_dp = jnp.einsum(
        "qhd,khd->hqk",
        text_heads,
        split_heads(text_three[:, 2]),
        preferred_element_type=jnp.float32,
    )
    layout_dp = jnp.einsum(
        "qhd,khd->hqk",
        layout_heads,
        split_heads(layout_three[:, 2]),
        preferred_element_type=jnp.float32,
    )
    text_dv = jnp.einsum("hqk,qhd->khd", weights, text_heads, preferred_element_type=jnp.float32)
    layout_dv = jnp.einsum(
        "hqk,qhd->khd", weights, layout_heads, preferred_element_type=jnp.float32
    )
    text_ds = probs * (text_dp - jnp.sum(probs * text_dp, -1, keepdims=True))
    layout_ds = probs * (layout_dp - jnp.sum(probs * layout_dp, -1, keepdims=True))
    text_only, joint_ds = lax.optimization_barrier(
        (text_ds.astype(jnp.bfloat16), (text_ds + layout_ds).astype(jnp.bfloat16))
    )
    text_dq = jnp.einsum(
        "hqk,khd->qhd", text_only, split_heads(text_three[:, 1]), preferred_element_type=jnp.float32
    ) * HD ** (-0.5)
    text_dk = jnp.einsum(
        "hqk,qhd->khd", text_only, split_heads(text_three[:, 0]), preferred_element_type=jnp.float32
    ) * HD ** (-0.5)
    layout_dq = jnp.einsum(
        "hqk,khd->qhd",
        joint_ds,
        split_heads(layout_three[:, 1]),
        preferred_element_type=jnp.float32,
    ) * LHD ** (-0.5)
    layout_dk = jnp.einsum(
        "hqk,qhd->khd",
        joint_ds,
        split_heads(layout_three[:, 0]),
        preferred_element_type=jnp.float32,
    ) * LHD ** (-0.5)
    slots = text_three.shape[0]
    text_all = jnp.stack([text_dq, text_dk, text_dv], 1).reshape(slots, 3, -1)
    layout_all = jnp.stack([layout_dq, layout_dk, layout_dv], 1).reshape(slots, 3, -1)
    return (text_all, layout_all)


def project_back(attn, width, columns, three_grad, first_grad):
    rounded_grad = three_grad.astype(jnp.bfloat16)
    if columns:
        three = attn[:, 0 : 3 * width].reshape(width, 3, width)
        input_grad = first_grad + jnp.einsum(
            "sje,dje->sd", rounded_grad, three, preferred_element_type=jnp.float32
        )
    else:
        three = attn[0 : 3 * width].reshape(3, width, width)
        input_grad = first_grad + jnp.einsum(
            "sje,jde->sd", rounded_grad, three, preferred_element_type=jnp.float32
        )
    column_sums = jnp.sum(rounded_grad.astype(jnp.float32), 0)
    return (input_grad, rounded_grad, column_sums[0], column_sums[2])


def branch_forward(inputs, context, attn, packed, first, second, width, columns):
    pieces = vector_parts(packed.astype(jnp.float32), width)
    out_block = block_of(attn, 3, width, columns)
    first_res = inputs.astype(jnp.float32) + (
        jnp.dot(context, out_block, preferred_element_type=jnp.float32) + pieces[2]
    )
    hidden = normalize(first_res, pieces[3], pieces[4])
    inner = (
        jnp.dot(hidden.astype(jnp.bfloat16), first, preferred_element_type=jnp.float32) + pieces[8]
    )
    activated = gelu_exact(inner).astype(jnp.bfloat16)
    second_res = hidden + (
        jnp.dot(activated, second, preferred_element_type=jnp.float32) + pieces[5]
    )
    result = normalize(second_res, pieces[6], pieces[7])
    return (result, (first_res, inner, second_res))


def branch_backward(attn, packed, first, second, width, columns, kept_rows, grad_out):
    first_res, inner, second_res = kept_rows
    pieces = vector_parts(packed.astype(jnp.float32), width)
    hidden, first_pull = jax.vjp(normalize, first_res, pieces[3], pieces[4])
    _, second_pull = jax.vjp(normalize, second_res, pieces[6], pieces[7])
    grad_second, late_scale, late_shift = second_pull(grad_out)
    round_second = grad_second.astype(jnp.bfloat16)
    activated, gelu_pull = jax.vjp(gelu_exact, inner)
    (grad_inner,) = gelu_pull(jnp.dot(round_second, second.T, preferred_element_type=jnp.float32))
    round_inner = grad_inner.astype(jnp.bfloat16)
    grad_hidden = grad_second + jnp.dot(round_inner, first.T, preferred_element_type=jnp.float32)
    grad_first, early_scale, early_shift = first_pull(grad_hidden)
    round_first = grad_first.astype(jnp.bfloat16)
    out_block = block_of(attn, 3, width, columns)
    grad_ctx = jnp.dot(round_first, out_block.T, preferred_element_type=jnp.float32).astype(
        jnp.bfloat16
    )
    operands = (
        hidden.astype(jnp.bfloat16),
        activated.astype(jnp.bfloat16),
        round_first,
        round_second,
        round_inner,
    )
    vector_sums = (
        jnp.sum(grad_first, 0),
        early_scale,
        early_shift,
        jnp.sum(grad_second, 0),
        late_scale,
        late_shift,
        jnp.sum(grad_inner, 0),
    )
    return (grad_first, grad_ctx, operands, vector_sums)


def page_forward(text_rows, layout_rows, length, weights):
    (
        text_attn,
        text_first,
        text_second,
        text_packed,
        layout_attn,
        layout_first,
        layout_second,
        layout_packed,
    ) = weights
    width = text_rows.shape[1]
    narrow = layout_rows.shape[1]
    valid = jnp.arange(text_rows.shape[0], dtype=jnp.int32) < length
    text_three = project_three(text_rows, text_attn, text_packed, width, True)
    layout_three = project_three(layout_rows, layout_attn, layout_packed, narrow, False)
    text_ctx, layout_ctx, log_total = attend(text_three, layout_three, valid)
    text_out, text_kept = branch_forward(
        text_rows, text_ctx, text_attn, text_packed, text_first, text_second, width, True
    )
    layout_out, layout_kept = branch_forward(
        layout_rows,
        layout_ctx,
        layout_attn,
        layout_packed,
        layout_first,
        layout_second,
        narrow,
        False,
    )
    mask = valid[:, None].astype(jnp.float32)
    outputs = ((text_out * mask).astype(jnp.bfloat16), (layout_out * mask).astype(jnp.bfloat16))
    kept_page = (text_three, layout_three, text_ctx, layout_ctx, log_total, text_kept, layout_kept)
    return (outputs, kept_page)


def page_back_ffn(length, kept_page, text_cot, layout_cot, weights):
    (
        text_attn,
        text_first,
        text_second,
        text_packed,
        layout_attn,
        layout_first,
        layout_second,
        layout_packed,
    ) = weights
    _, _, _, _, _, text_kept, layout_kept = kept_page
    width = text_attn.shape[0]
    narrow = layout_attn.shape[1]
    slots = text_cot.shape[0]
    valid = jnp.arange(slots, dtype=jnp.int32) < length
    mask = valid[:, None].astype(jnp.float32)
    text_back = branch_backward(
        text_attn,
        text_packed,
        text_first,
        text_second,
        width,
        True,
        text_kept,
        text_cot.astype(jnp.float32) * mask,
    )
    layout_back = branch_backward(
        layout_attn,
        layout_packed,
        layout_first,
        layout_second,
        narrow,
        False,
        layout_kept,
        layout_cot.astype(jnp.float32) * mask,
    )
    return (text_back, layout_back)


def page_back_attn(text_rows, layout_rows, length, kept_page, text_back, layout_back, weights):
    (text_attn, _, _, _, layout_attn, _, _, _) = weights
    text_three, layout_three, _, layout_ctx, log_total, _, _ = kept_page
    width = text_rows.shape[1]
    narrow = layout_rows.shape[1]
    slots = text_rows.shape[0]
    valid = jnp.arange(slots, dtype=jnp.int32) < length
    text_res_grad, text_ctx_grad, _, text_sums = text_back
    layout_res_grad, layout_ctx_grad, layout_ops, layout_sums = layout_back
    text_three_grad, layout_three_grad = attend_back(
        text_three, layout_three, valid, log_total, text_ctx_grad, layout_ctx_grad
    )
    text_in_grad, text_rounded, text_query_bias, text_value_bias = project_back(
        text_attn, width, True, text_three_grad, text_res_grad
    )
    layout_in_grad, layout_rounded, layout_query_bias, layout_value_bias = project_back(
        layout_attn, narrow, False, layout_three_grad, layout_res_grad
    )
    hidden_low, active_low, first_low, second_low, inner_low = layout_ops
    three_w = jnp.einsum(
        "sd,sje->jde", layout_rows, layout_rounded, preferred_element_type=jnp.float32
    ).reshape(3 * narrow, narrow)
    out_w = jnp.einsum("sd,se->de", layout_ctx, first_low, preferred_element_type=jnp.float32)
    layout_attn_grad = jnp.concatenate([three_w, out_w], 0)
    layout_first_grad = jnp.einsum(
        "sd,sf->df", hidden_low, inner_low, preferred_element_type=jnp.float32
    )
    layout_second_grad = jnp.einsum(
        "sf,sd->fd", active_low, second_low, preferred_element_type=jnp.float32
    )
    layout_vec_grad = jnp.concatenate([layout_query_bias, layout_value_bias] + list(layout_sums))
    text_vec_grad = jnp.concatenate([text_query_bias, text_value_bias] + list(text_sums))
    small_terms = (
        text_vec_grad,
        layout_attn_grad,
        layout_first_grad,
        layout_second_grad,
        layout_vec_grad,
    )
    return ((text_in_grad, layout_in_grad), small_terms, text_rounded.reshape(slots, 3 * width))


def flat_rows(values):
    return values.reshape(-1, values.shape[-1])


AXES = ("dp", "shard")


def rows_for(size, width, aligned):
    rows = -(-size // width)
    if aligned:
        rows = -(-rows // 8) * 8
    return rows


def pack_rows(pieces, width, aligned):
    flat = jnp.concatenate([piece.reshape(-1) for piece in pieces])
    rows = rows_for(flat.shape[0], width, aligned)
    return jnp.pad(flat, (0, rows * width - flat.shape[0])).reshape(rows, width)


def unpack_small(flat, count, shapes):
    sizes = [rows * cols for rows, cols in shapes]
    offsets = [sum(sizes[:index]) for index in range(len(sizes))]
    parts = [flat[:, offset : offset + size] for offset, size in zip(offsets, sizes)]
    (attn_rows, attn_cols), (w1_rows, w1_cols), (w2_rows, w2_cols) = shapes[1:4]
    return (
        parts[0].reshape(-1),
        parts[1].reshape(count * attn_rows, attn_cols),
        parts[2].reshape(count, w1_rows, w1_cols).transpose(1, 0, 2).reshape(w1_rows, count * w1_cols),
        parts[3].reshape(count * w2_rows, w2_cols),
        parts[4].reshape(-1),
    )


def gather_weights(text_attn, text_w1, text_w2, text_vectors, layout_attn, layout_w1, layout_w2, layout_vectors):
    rows, width = text_attn.shape
    aligned = rows % 8 == 0
    small = (text_vectors, layout_attn, layout_w1, layout_w2, layout_vectors)
    small_rows = pack_rows(small, width, aligned)
    first = jnp.concatenate([text_attn, small_rows], 0)
    first_all = lax.all_gather(first, AXES, axis=0, tiled=True)
    count = first_all.shape[0] // first.shape[0]
    first_all = first_all.reshape(count, first.shape[0], width)
    full_attn = first_all[:, :rows].reshape(count * rows, width)
    small_flat = first_all[:, rows:].reshape(count, -1)
    shapes = [(1, text_vectors.shape[0]), layout_attn.shape, layout_w1.shape, layout_w2.shape, (1, layout_vectors.shape[0])]
    full_small = unpack_small(small_flat, count, shapes)
    w2_rows = text_w2.shape[0]
    second = jnp.concatenate([text_w1, text_w2.reshape(rows, -1)], 0)
    second_all = lax.all_gather(second, AXES, axis=0, tiled=True).reshape(count, 2 * rows, width)
    full_w1 = second_all[:, :rows].reshape(count * rows, width)
    full_w2 = second_all[:, rows:].reshape(count * w2_rows, text_w2.shape[1])
    return (full_attn, full_w1, full_w2) + full_small


def small_blocks(count, text_vec_grad, layout_attn_grad, layout_w1_grad, layout_w2_grad, layout_vec_grad):
    local_w1_cols = layout_w1_grad.shape[1] // count
    return (
        text_vec_grad.reshape(count, -1),
        layout_attn_grad.reshape(count, -1),
        layout_w1_grad.reshape(layout_w1_grad.shape[0], count, local_w1_cols)
        .transpose(1, 0, 2)
        .reshape(count, -1),
        layout_w2_grad.reshape(count, -1),
        layout_vec_grad.reshape(count, -1),
    )


def scatter_late(count, grad_attn, small_grads):
    width = grad_attn.shape[1]
    rows = grad_attn.shape[0] // count
    blocks = small_blocks(count, *small_grads)
    joined = jnp.concatenate(blocks, 1)
    size = joined.shape[1]
    small_rows = rows_for(size, width, rows % 8 == 0)
    joined = jnp.pad(joined, ((0, 0), (0, small_rows * width - size))).reshape(count, small_rows, width)
    packed = jnp.concatenate([grad_attn.reshape(count, rows, width), joined], 1)
    summed = lax.psum_scatter(
        packed.reshape(-1, width).astype(jnp.bfloat16), AXES, scatter_dimension=0, tiled=True
    ).astype(jnp.float32)
    attn_part = summed[:rows]
    flat = summed[rows:].reshape(-1)
    sizes = [block.shape[1] for block in blocks]
    offsets = [sum(sizes[:index]) for index in range(len(sizes))]
    parts = [flat[offset : offset + size] for offset, size in zip(offsets, sizes)]
    _, layout_attn_grad, layout_w1_grad, layout_w2_grad, _ = small_grads
    local_w1_cols = layout_w1_grad.shape[1] // count
    return (
        attn_part,
        parts[0],
        parts[1].reshape(layout_attn_grad.shape[0] // count, layout_attn_grad.shape[1]),
        parts[2].reshape(layout_w1_grad.shape[0], local_w1_cols),
        parts[3].reshape(layout_w2_grad.shape[0] // count, layout_w2_grad.shape[1]),
        parts[4],
    )


def pack_early(count, grad_first, grad_second):
    width = grad_first.shape[1]
    rows = grad_first.shape[0] // count
    packed = jnp.concatenate(
        [grad_first.reshape(count, rows, width), grad_second.reshape(count, rows, width)], 1
    )
    return packed.reshape(-1, width).astype(jnp.bfloat16)


def scatter_early(count, packed, second_shape):
    rows = packed.shape[0] // (2 * count)
    summed = lax.psum_scatter(packed, AXES, scatter_dimension=0, tiled=True).astype(jnp.float32)
    return (summed[:rows], summed[rows:].reshape(-1, second_shape[1]))


def body(
    text_in,
    layout_in,
    lengths,
    text_attn,
    text_w1,
    text_w2,
    text_vectors,
    layout_attn,
    layout_w1,
    layout_w2,
    layout_vectors,
    cot_text,
    cot_layout,
):
    count = lax.psum(1, AXES)
    weights = gather_weights(
        text_attn, text_w1, text_w2, text_vectors, layout_attn, layout_w1, layout_w2, layout_vectors
    )

    page_weights = (None,) * len(weights)
    outputs, kept_all = jax.vmap(page_forward, in_axes=(0, 0, 0, page_weights))(
        text_in, layout_in, lengths, weights
    )
    out_text, out_layout = outputs
    text_back, layout_back = jax.vmap(page_back_ffn, in_axes=(0, 0, 0, 0, page_weights))(
        lengths, kept_all, cot_text, cot_layout, weights
    )
    text_hidden, text_active, text_first_low, text_second_low, text_inner_low = text_back[2]
    early = (
        jnp.einsum("sd,sf->df", flat_rows(text_hidden), flat_rows(text_inner_low), preferred_element_type=jnp.float32),
        jnp.einsum("sf,sd->fd", flat_rows(text_active), flat_rows(text_second_low), preferred_element_type=jnp.float32),
    )
    packed = pack_early(count, *early)
    packed, text_back, layout_back = lax.optimization_barrier((packed, text_back, layout_back))
    grad_first, grad_second = scatter_early(count, packed, early[1].shape)
    (text_grad, layout_grad), small_terms, text_rounded = jax.vmap(
        page_back_attn, in_axes=(0, 0, 0, 0, 0, 0, page_weights)
    )(text_in, layout_in, lengths, kept_all, text_back, layout_back, weights)
    totals = tuple(jnp.sum(term, 0) for term in small_terms)
    three_part = jnp.einsum(
        "sd,se->de", flat_rows(text_in), flat_rows(text_rounded), preferred_element_type=jnp.float32
    )
    out_part = jnp.einsum(
        "sd,se->de", flat_rows(kept_all[2]), flat_rows(text_first_low), preferred_element_type=jnp.float32
    )
    summed = scatter_late(count, jnp.concatenate([three_part, out_part], 1), totals)
    return (
        out_text,
        out_layout,
        text_grad,
        layout_grad,
        summed[0],
        grad_first,
        grad_second,
        summed[1],
        summed[2],
        summed[3],
        summed[4],
        summed[5],
    )


def solution(mesh):
    placed = (
        P(("dp", "shard"), None, None),
        P(("dp", "shard"), None, None),
        P(("dp", "shard")),
        P(("dp", "shard"), None),
        P(("dp", "shard"), None),
        P(("dp", "shard"), None),
        P(("dp", "shard")),
        P(("dp", "shard"), None),
        P(None, ("dp", "shard")),
        P(("dp", "shard"), None),
        P(("dp", "shard")),
        P(("dp", "shard"), None, None),
        P(("dp", "shard"), None, None),
    )
    return jax.shard_map(
        body,
        mesh=mesh,
        in_specs=placed,
        out_specs=(
            P(("dp", "shard"), None, None),
            P(("dp", "shard"), None, None),
            P(("dp", "shard"), None, None),
            P(("dp", "shard"), None, None),
            P(("dp", "shard"), None),
            P(("dp", "shard"), None),
            P(("dp", "shard"), None),
            P(("dp", "shard")),
            P(("dp", "shard"), None),
            P(None, ("dp", "shard")),
            P(("dp", "shard"), None),
            P(("dp", "shard")),
        ),
        check_vma=False,
    )
```

```python
import jax
import jax.numpy as jnp
from jax import lax
from jax.sharding import PartitionSpec as P


H = 12
HD = 64
LHD = 16


EPS = 1e-05
NEG = -1000000000.0


def normalize(values, scale_row, shift_row):
    centered = values - jnp.mean(values, -1, keepdims=True)
    variance = jnp.mean(centered * centered, -1, keepdims=True)
    return centered * lax.rsqrt(variance + EPS) * scale_row + shift_row


def gelu_exact(values):
    return jax.nn.gelu(values, approximate=False)


def vector_parts(packed, width):
    pieces = [packed[index * width : (index + 1) * width] for index in range(8)]
    return pieces + [packed[8 * width :]]


def split_heads(values):
    return values.reshape(values.shape[0], H, -1)


def block_of(attn, index, width, columns):
    if columns:
        return attn[:, index * width : (index + 1) * width]
    return attn[index * width : (index + 1) * width]


def project_three(inputs, attn, packed, width, columns):
    if columns:
        three = attn[:, 0 : 3 * width].reshape(width, 3, width)
        mixed = jnp.einsum("sd,dje->sje", inputs, three, preferred_element_type=jnp.float32)
    else:
        three = attn[0 : 3 * width].reshape(3, width, width)
        mixed = jnp.einsum("sd,jde->sje", inputs, three, preferred_element_type=jnp.float32)
    pieces = vector_parts(packed.astype(jnp.float32), width)
    offsets = jnp.stack([pieces[0], jnp.zeros_like(pieces[0]), pieces[1]])
    return (mixed + offsets[None]).astype(jnp.bfloat16)


def score_table(text_three, layout_three, valid):
    text_part = jnp.einsum(
        "qhd,khd->hqk",
        split_heads(text_three[:, 0]),
        split_heads(text_three[:, 1]),
        preferred_element_type=jnp.float32,
    )
    layout_part = jnp.einsum(
        "qhd,khd->hqk",
        split_heads(layout_three[:, 0]),
        split_heads(layout_three[:, 1]),
        preferred_element_type=jnp.float32,
    )
    joined = text_part * HD ** (-0.5) + layout_part * LHD ** (-0.5)
    return jnp.where(valid[None, None, :], joined, NEG)


def attend(text_three, layout_three, valid):
    scores = score_table(text_three, layout_three, valid)
    row_max = jnp.max(scores, -1, keepdims=True)
    exponent = jnp.exp(scores - row_max)
    row_total = jnp.sum(exponent, -1, keepdims=True)
    weights = (exponent / row_total).astype(jnp.bfloat16)
    slots = text_three.shape[0]
    text_ctx = jnp.einsum(
        "hqk,khd->qhd", weights, split_heads(text_three[:, 2]), preferred_element_type=jnp.float32
    )
    layout_ctx = jnp.einsum(
        "hqk,khd->qhd", weights, split_heads(layout_three[:, 2]), preferred_element_type=jnp.float32
    )
    log_total = (row_max + jnp.log(row_total))[..., 0]
    return (
        text_ctx.reshape(slots, -1).astype(jnp.bfloat16),
        layout_ctx.reshape(slots, -1).astype(jnp.bfloat16),
        log_total,
    )


def attend_back(text_three, layout_three, valid, log_total, text_grad, layout_grad):
    scores = score_table(text_three, layout_three, valid)
    probs = jnp.exp(scores - log_total[..., None])
    weights = probs.astype(jnp.bfloat16)
    text_heads = split_heads(text_grad)
    layout_heads = split_heads(layout_grad)
    text_dp = jnp.einsum(
        "qhd,khd->hqk",
        text_heads,
        split_heads(text_three[:, 2]),
        preferred_element_type=jnp.float32,
    )
    layout_dp = jnp.einsum(
        "qhd,khd->hqk",
        layout_heads,
        split_heads(layout_three[:, 2]),
        preferred_element_type=jnp.float32,
    )
    text_dv = jnp.einsum("hqk,qhd->khd", weights, text_heads, preferred_element_type=jnp.float32)
    layout_dv = jnp.einsum(
        "hqk,qhd->khd", weights, layout_heads, preferred_element_type=jnp.float32
    )
    text_ds = probs * (text_dp - jnp.sum(probs * text_dp, -1, keepdims=True))
    layout_ds = probs * (layout_dp - jnp.sum(probs * layout_dp, -1, keepdims=True))
    text_only, joint_ds = lax.optimization_barrier(
        (text_ds.astype(jnp.bfloat16), (text_ds + layout_ds).astype(jnp.bfloat16))
    )
    text_dq = jnp.einsum(
        "hqk,khd->qhd", text_only, split_heads(text_three[:, 1]), preferred_element_type=jnp.float32
    ) * HD ** (-0.5)
    text_dk = jnp.einsum(
        "hqk,qhd->khd", text_only, split_heads(text_three[:, 0]), preferred_element_type=jnp.float32
    ) * HD ** (-0.5)
    layout_dq = jnp.einsum(
        "hqk,khd->qhd",
        joint_ds,
        split_heads(layout_three[:, 1]),
        preferred_element_type=jnp.float32,
    ) * LHD ** (-0.5)
    layout_dk = jnp.einsum(
        "hqk,qhd->khd",
        joint_ds,
        split_heads(layout_three[:, 0]),
        preferred_element_type=jnp.float32,
    ) * LHD ** (-0.5)
    slots = text_three.shape[0]
    text_all = jnp.stack([text_dq, text_dk, text_dv], 1).reshape(slots, 3, -1)
    layout_all = jnp.stack([layout_dq, layout_dk, layout_dv], 1).reshape(slots, 3, -1)
    return (text_all, layout_all)


def project_back(attn, width, columns, three_grad, first_grad):
    rounded_grad = three_grad.astype(jnp.bfloat16)
    if columns:
        three = attn[:, 0 : 3 * width].reshape(width, 3, width)
        input_grad = first_grad + jnp.einsum(
            "sje,dje->sd", rounded_grad, three, preferred_element_type=jnp.float32
        )
    else:
        three = attn[0 : 3 * width].reshape(3, width, width)
        input_grad = first_grad + jnp.einsum(
            "sje,jde->sd", rounded_grad, three, preferred_element_type=jnp.float32
        )
    column_sums = jnp.sum(rounded_grad.astype(jnp.float32), 0)
    return (input_grad, rounded_grad, column_sums[0], column_sums[2])


def branch_forward(inputs, context, attn, packed, first, second, width, columns):
    pieces = vector_parts(packed.astype(jnp.float32), width)
    out_block = block_of(attn, 3, width, columns)
    first_res = inputs.astype(jnp.float32) + (
        jnp.dot(context, out_block, preferred_element_type=jnp.float32) + pieces[2]
    )
    hidden = normalize(first_res, pieces[3], pieces[4])
    inner = (
        jnp.dot(hidden.astype(jnp.bfloat16), first, preferred_element_type=jnp.float32) + pieces[8]
    )
    activated = gelu_exact(inner).astype(jnp.bfloat16)
    second_res = hidden + (
        jnp.dot(activated, second, preferred_element_type=jnp.float32) + pieces[5]
    )
    result = normalize(second_res, pieces[6], pieces[7])
    return (result, (first_res, inner, second_res))


def branch_backward(attn, packed, first, second, width, columns, kept_rows, grad_out):
    first_res, inner, second_res = kept_rows
    pieces = vector_parts(packed.astype(jnp.float32), width)
    hidden, first_pull = jax.vjp(normalize, first_res, pieces[3], pieces[4])
    _, second_pull = jax.vjp(normalize, second_res, pieces[6], pieces[7])
    grad_second, late_scale, late_shift = second_pull(grad_out)
    round_second = grad_second.astype(jnp.bfloat16)
    activated, gelu_pull = jax.vjp(gelu_exact, inner)
    (grad_inner,) = gelu_pull(jnp.dot(round_second, second.T, preferred_element_type=jnp.float32))
    round_inner = grad_inner.astype(jnp.bfloat16)
    grad_hidden = grad_second + jnp.dot(round_inner, first.T, preferred_element_type=jnp.float32)
    grad_first, early_scale, early_shift = first_pull(grad_hidden)
    round_first = grad_first.astype(jnp.bfloat16)
    out_block = block_of(attn, 3, width, columns)
    grad_ctx = jnp.dot(round_first, out_block.T, preferred_element_type=jnp.float32).astype(
        jnp.bfloat16
    )
    operands = (
        hidden.astype(jnp.bfloat16),
        activated.astype(jnp.bfloat16),
        round_first,
        round_second,
        round_inner,
    )
    vector_sums = (
        jnp.sum(grad_first, 0),
        early_scale,
        early_shift,
        jnp.sum(grad_second, 0),
        late_scale,
        late_shift,
        jnp.sum(grad_inner, 0),
    )
    return (grad_first, grad_ctx, operands, vector_sums)


def branch_back_a(packed, second, width, kept_rows, grad_out):
    first_res, inner, second_res = kept_rows
    pieces = vector_parts(packed.astype(jnp.float32), width)
    hidden = normalize(first_res, pieces[3], pieces[4])
    _, second_pull = jax.vjp(normalize, second_res, pieces[6], pieces[7])
    grad_second, late_scale, late_shift = second_pull(grad_out)
    round_second = grad_second.astype(jnp.bfloat16)
    activated, gelu_pull = jax.vjp(gelu_exact, inner)
    (grad_inner,) = gelu_pull(jnp.dot(round_second, second.T, preferred_element_type=jnp.float32))
    round_inner = grad_inner.astype(jnp.bfloat16)
    return (
        grad_second,
        round_second,
        grad_inner,
        round_inner,
        hidden.astype(jnp.bfloat16),
        activated.astype(jnp.bfloat16),
        late_scale,
        late_shift,
    )


def branch_back_b(attn, packed, first, width, columns, kept_rows, part_a):
    first_res, _, _ = kept_rows
    grad_second, round_second, grad_inner, round_inner, hidden_low, active_low, late_scale, late_shift = part_a
    pieces = vector_parts(packed.astype(jnp.float32), width)
    _, first_pull = jax.vjp(normalize, first_res, pieces[3], pieces[4])
    grad_hidden = grad_second + jnp.dot(round_inner, first.T, preferred_element_type=jnp.float32)
    grad_first, early_scale, early_shift = first_pull(grad_hidden)
    round_first = grad_first.astype(jnp.bfloat16)
    out_block = block_of(attn, 3, width, columns)
    grad_ctx = jnp.dot(round_first, out_block.T, preferred_element_type=jnp.float32).astype(
        jnp.bfloat16
    )
    operands = (hidden_low, active_low, round_first, round_second, round_inner)
    vector_sums = (
        jnp.sum(grad_first, 0),
        early_scale,
        early_shift,
        jnp.sum(grad_second, 0),
        late_scale,
        late_shift,
        jnp.sum(grad_inner, 0),
    )
    return (grad_first, grad_ctx, operands, vector_sums)


def page_forward(text_rows, layout_rows, length, weights):
    (text_attn, text_first, text_second, text_packed, layout_attn, _, _, layout_packed) = weights
    width = text_rows.shape[1]
    narrow = layout_rows.shape[1]
    valid = jnp.arange(text_rows.shape[0], dtype=jnp.int32) < length
    text_three = project_three(text_rows, text_attn, text_packed, width, True)
    layout_three = project_three(layout_rows, layout_attn, layout_packed, narrow, False)
    text_ctx, layout_ctx, log_total = attend(text_three, layout_three, valid)
    text_out, text_kept = branch_forward(
        text_rows, text_ctx, text_attn, text_packed, text_first, text_second, width, True
    )
    mask = valid[:, None].astype(jnp.float32)
    kept_page = (text_three, layout_three, text_ctx, layout_ctx, log_total, text_kept)
    return ((text_out * mask).astype(jnp.bfloat16), kept_page)


def page_back_ffn(length, kept_page, text_cot, weights):
    text_attn, _, text_second, text_packed = weights[:4]
    text_kept = kept_page[5]
    width = text_attn.shape[0]
    slots = text_cot.shape[0]
    valid = jnp.arange(slots, dtype=jnp.int32) < length
    mask = valid[:, None].astype(jnp.float32)
    return branch_back_a(
        text_packed, text_second, width, text_kept, text_cot.astype(jnp.float32) * mask
    )


def page_back_attn(text_rows, layout_rows, length, kept_page, text_a, layout_cot, weights):
    (
        text_attn,
        text_first,
        _,
        text_packed,
        layout_attn,
        layout_first,
        layout_second,
        layout_packed,
    ) = weights
    text_three, layout_three, _, layout_ctx, log_total, text_kept = kept_page
    width = text_rows.shape[1]
    narrow = layout_rows.shape[1]
    slots = text_rows.shape[0]
    valid = jnp.arange(slots, dtype=jnp.int32) < length
    mask = valid[:, None].astype(jnp.float32)
    layout_out, layout_kept = branch_forward(
        layout_rows,
        layout_ctx,
        layout_attn,
        layout_packed,
        layout_first,
        layout_second,
        narrow,
        False,
    )
    layout_back = branch_backward(
        layout_attn,
        layout_packed,
        layout_first,
        layout_second,
        narrow,
        False,
        layout_kept,
        layout_cot.astype(jnp.float32) * mask,
    )
    text_back = branch_back_b(text_attn, text_packed, text_first, width, True, text_kept, text_a)
    text_res_grad, text_ctx_grad, text_ops, text_sums = text_back
    layout_res_grad, layout_ctx_grad, layout_ops, layout_sums = layout_back
    text_three_grad, layout_three_grad = attend_back(
        text_three, layout_three, valid, log_total, text_ctx_grad, layout_ctx_grad
    )
    text_in_grad, text_rounded, text_query_bias, text_value_bias = project_back(
        text_attn, width, True, text_three_grad, text_res_grad
    )
    layout_in_grad, layout_rounded, layout_query_bias, layout_value_bias = project_back(
        layout_attn, narrow, False, layout_three_grad, layout_res_grad
    )
    hidden_low, active_low, first_low, second_low, inner_low = layout_ops
    three_w = jnp.einsum(
        "sd,sje->jde", layout_rows, layout_rounded, preferred_element_type=jnp.float32
    ).reshape(3 * narrow, narrow)
    out_w = jnp.einsum("sd,se->de", layout_ctx, first_low, preferred_element_type=jnp.float32)
    layout_attn_grad = jnp.concatenate([three_w, out_w], 0)
    layout_first_grad = jnp.einsum(
        "sd,sf->df", hidden_low, inner_low, preferred_element_type=jnp.float32
    )
    layout_second_grad = jnp.einsum(
        "sf,sd->fd", active_low, second_low, preferred_element_type=jnp.float32
    )
    layout_vec_grad = jnp.concatenate([layout_query_bias, layout_value_bias] + list(layout_sums))
    text_vec_grad = jnp.concatenate([text_query_bias, text_value_bias] + list(text_sums))
    small_terms = (
        text_vec_grad,
        layout_attn_grad,
        layout_first_grad,
        layout_second_grad,
        layout_vec_grad,
    )
    layout_low = (layout_out * mask).astype(jnp.bfloat16)
    grads = (text_in_grad, layout_in_grad)
    return (layout_low, grads, small_terms, text_rounded.reshape(slots, 3 * width), text_ops[2])


def flat_rows(values):
    return values.reshape(-1, values.shape[-1])


AXES = ("dp", "shard")


def rows_for(size, width, aligned):
    rows = -(-size // width)
    if aligned:
        rows = -(-rows // 8) * 8
    return rows


def pack_rows(pieces, width, aligned):
    flat = jnp.concatenate([piece.reshape(-1) for piece in pieces])
    rows = rows_for(flat.shape[0], width, aligned)
    return jnp.pad(flat, (0, rows * width - flat.shape[0])).reshape(rows, width)


def unpack_small(flat, count, shapes):
    sizes = [rows * cols for rows, cols in shapes]
    offsets = [sum(sizes[:index]) for index in range(len(sizes))]
    parts = [flat[:, offset : offset + size] for offset, size in zip(offsets, sizes)]
    (attn_rows, attn_cols), (w1_rows, w1_cols), (w2_rows, w2_cols) = shapes[1:4]
    return (
        parts[0].reshape(-1),
        parts[1].reshape(count * attn_rows, attn_cols),
        parts[2].reshape(count, w1_rows, w1_cols).transpose(1, 0, 2).reshape(w1_rows, count * w1_cols),
        parts[3].reshape(count * w2_rows, w2_cols),
        parts[4].reshape(-1),
    )


def gather_weights(text_attn, text_w1, text_w2, text_vectors, layout_attn, layout_w1, layout_w2, layout_vectors):
    rows, width = text_attn.shape
    aligned = rows % 8 == 0
    small = (text_vectors, layout_attn, layout_w1, layout_w2, layout_vectors)
    small_rows = pack_rows(small, width, aligned)
    first = jnp.concatenate([text_attn, small_rows], 0)
    first_all = lax.all_gather(first, AXES, axis=0, tiled=True)
    count = first_all.shape[0] // first.shape[0]
    first_all = first_all.reshape(count, first.shape[0], width)
    full_attn = first_all[:, :rows].reshape(count * rows, width)
    small_flat = first_all[:, rows:].reshape(count, -1)
    shapes = [(1, text_vectors.shape[0]), layout_attn.shape, layout_w1.shape, layout_w2.shape, (1, layout_vectors.shape[0])]
    full_small = unpack_small(small_flat, count, shapes)
    w2_rows = text_w2.shape[0]
    second = jnp.concatenate([text_w1, text_w2.reshape(rows, -1)], 0)
    second_all = lax.all_gather(second, AXES, axis=0, tiled=True).reshape(count, 2 * rows, width)
    full_w1 = second_all[:, :rows].reshape(count * rows, width)
    full_w2 = second_all[:, rows:].reshape(count * w2_rows, text_w2.shape[1])
    return (full_attn, full_w1, full_w2) + full_small


def small_blocks(count, text_vec_grad, layout_attn_grad, layout_w1_grad, layout_w2_grad, layout_vec_grad):
    local_w1_cols = layout_w1_grad.shape[1] // count
    return (
        text_vec_grad.reshape(count, -1),
        layout_attn_grad.reshape(count, -1),
        layout_w1_grad.reshape(layout_w1_grad.shape[0], count, local_w1_cols)
        .transpose(1, 0, 2)
        .reshape(count, -1),
        layout_w2_grad.reshape(count, -1),
        layout_vec_grad.reshape(count, -1),
    )


def scatter_late(count, grad_attn, small_grads):
    width = grad_attn.shape[1]
    rows = grad_attn.shape[0] // count
    blocks = small_blocks(count, *small_grads)
    joined = jnp.concatenate(blocks, 1)
    size = joined.shape[1]
    small_rows = rows_for(size, width, rows % 8 == 0)
    joined = jnp.pad(joined, ((0, 0), (0, small_rows * width - size))).reshape(count, small_rows, width)
    packed = jnp.concatenate([grad_attn.reshape(count, rows, width), joined], 1)
    summed = lax.psum_scatter(
        packed.reshape(-1, width).astype(jnp.bfloat16), AXES, scatter_dimension=0, tiled=True
    ).astype(jnp.float32)
    attn_part = summed[:rows]
    flat = summed[rows:].reshape(-1)
    sizes = [block.shape[1] for block in blocks]
    offsets = [sum(sizes[:index]) for index in range(len(sizes))]
    parts = [flat[offset : offset + size] for offset, size in zip(offsets, sizes)]
    _, layout_attn_grad, layout_w1_grad, layout_w2_grad, _ = small_grads
    local_w1_cols = layout_w1_grad.shape[1] // count
    return (
        attn_part,
        parts[0],
        parts[1].reshape(layout_attn_grad.shape[0] // count, layout_attn_grad.shape[1]),
        parts[2].reshape(layout_w1_grad.shape[0], local_w1_cols),
        parts[3].reshape(layout_w2_grad.shape[0] // count, layout_w2_grad.shape[1]),
        parts[4],
    )


def pack_early(count, grad_first, grad_second):
    width = grad_first.shape[1]
    rows = grad_first.shape[0] // count
    packed = jnp.concatenate(
        [grad_first.reshape(count, rows, width), grad_second.reshape(count, rows, width)], 1
    )
    return packed.reshape(-1, width).astype(jnp.bfloat16)


def scatter_early(count, packed, second_shape):
    rows = packed.shape[0] // (2 * count)
    summed = lax.psum_scatter(packed, AXES, scatter_dimension=0, tiled=True).astype(jnp.float32)
    return (summed[:rows], summed[rows:].reshape(-1, second_shape[1]))


def body(
    text_in,
    layout_in,
    lengths,
    text_attn,
    text_w1,
    text_w2,
    text_vectors,
    layout_attn,
    layout_w1,
    layout_w2,
    layout_vectors,
    cot_text,
    cot_layout,
):
    count = lax.psum(1, AXES)
    weights = gather_weights(
        text_attn, text_w1, text_w2, text_vectors, layout_attn, layout_w1, layout_w2, layout_vectors
    )

    page_weights = (None,) * len(weights)
    out_text, kept_all = jax.vmap(page_forward, in_axes=(0, 0, 0, page_weights))(
        text_in, layout_in, lengths, weights
    )
    text_a = jax.vmap(page_back_ffn, in_axes=(0, 0, 0, page_weights))(
        lengths, kept_all, cot_text, weights
    )
    round_second, round_inner, text_hidden, text_active = text_a[1], text_a[3], text_a[4], text_a[5]
    early = (
        jnp.einsum("sd,sf->df", flat_rows(text_hidden), flat_rows(round_inner), preferred_element_type=jnp.float32),
        jnp.einsum("sf,sd->fd", flat_rows(text_active), flat_rows(round_second), preferred_element_type=jnp.float32),
    )
    packed = pack_early(count, *early)
    packed, text_a, kept_all = lax.optimization_barrier((packed, text_a, kept_all))
    grad_first, grad_second = scatter_early(count, packed, early[1].shape)
    out_layout, (text_grad, layout_grad), small_terms, text_rounded, text_first_low = jax.vmap(
        page_back_attn, in_axes=(0, 0, 0, 0, 0, 0, page_weights)
    )(text_in, layout_in, lengths, kept_all, text_a, cot_layout, weights)
    totals = tuple(jnp.sum(term, 0) for term in small_terms)
    three_part = jnp.einsum(
        "sd,se->de", flat_rows(text_in), flat_rows(text_rounded), preferred_element_type=jnp.float32
    )
    out_part = jnp.einsum(
        "sd,se->de", flat_rows(kept_all[2]), flat_rows(text_first_low), preferred_element_type=jnp.float32
    )
    summed = scatter_late(count, jnp.concatenate([three_part, out_part], 1), totals)
    return (
        out_text,
        out_layout,
        text_grad,
        layout_grad,
        summed[0],
        grad_first,
        grad_second,
        summed[1],
        summed[2],
        summed[3],
        summed[4],
        summed[5],
    )


def solution(mesh):
    placed = (
        P(("dp", "shard"), None, None),
        P(("dp", "shard"), None, None),
        P(("dp", "shard")),
        P(("dp", "shard"), None),
        P(("dp", "shard"), None),
        P(("dp", "shard"), None),
        P(("dp", "shard")),
        P(("dp", "shard"), None),
        P(None, ("dp", "shard")),
        P(("dp", "shard"), None),
        P(("dp", "shard")),
        P(("dp", "shard"), None, None),
        P(("dp", "shard"), None, None),
    )
    return jax.shard_map(
        body,
        mesh=mesh,
        in_specs=placed,
        out_specs=(
            P(("dp", "shard"), None, None),
            P(("dp", "shard"), None, None),
            P(("dp", "shard"), None, None),
            P(("dp", "shard"), None, None),
            P(("dp", "shard"), None),
            P(("dp", "shard"), None),
            P(("dp", "shard"), None),
            P(("dp", "shard")),
            P(("dp", "shard"), None),
            P(None, ("dp", "shard")),
            P(("dp", "shard"), None),
            P(("dp", "shard")),
        ),
        check_vma=False,
    )
```

```python
import jax
import jax.numpy as jnp
from jax import lax
from jax.sharding import PartitionSpec as P


H = 12
HD = 64
LHD = 16


EPS = 1e-05
NEG = -1000000000.0


def normalize(values, scale_row, shift_row):
    centered = values - jnp.mean(values, -1, keepdims=True)
    variance = jnp.mean(centered * centered, -1, keepdims=True)
    return centered * lax.rsqrt(variance + EPS) * scale_row + shift_row


def gelu_exact(values):
    return jax.nn.gelu(values, approximate=False)


def vector_parts(packed, width):
    pieces = [packed[index * width : (index + 1) * width] for index in range(8)]
    return pieces + [packed[8 * width :]]


def split_heads(values):
    return values.reshape(values.shape[0], H, -1)


def block_of(attn, index, width, columns):
    if columns:
        return attn[:, index * width : (index + 1) * width]
    return attn[index * width : (index + 1) * width]


def project_three(inputs, attn, packed, width, columns):
    if columns:
        three = attn[:, 0 : 3 * width].reshape(width, 3, width)
        mixed = jnp.einsum("sd,dje->sje", inputs, three, preferred_element_type=jnp.float32)
    else:
        three = attn[0 : 3 * width].reshape(3, width, width)
        mixed = jnp.einsum("sd,jde->sje", inputs, three, preferred_element_type=jnp.float32)
    pieces = vector_parts(packed.astype(jnp.float32), width)
    offsets = jnp.stack([pieces[0], jnp.zeros_like(pieces[0]), pieces[1]])
    return (mixed + offsets[None]).astype(jnp.bfloat16)


def score_table(text_three, layout_three, valid):
    text_part = jnp.einsum(
        "qhd,khd->hqk",
        split_heads(text_three[:, 0]),
        split_heads(text_three[:, 1]),
        preferred_element_type=jnp.float32,
    )
    layout_part = jnp.einsum(
        "qhd,khd->hqk",
        split_heads(layout_three[:, 0]),
        split_heads(layout_three[:, 1]),
        preferred_element_type=jnp.float32,
    )
    joined = text_part * HD ** (-0.5) + layout_part * LHD ** (-0.5)
    return jnp.where(valid[None, None, :], joined, NEG)


def attend(text_three, layout_three, valid):
    scores = score_table(text_three, layout_three, valid)
    row_max = jnp.max(scores, -1, keepdims=True)
    exponent = jnp.exp(scores - row_max)
    row_total = jnp.sum(exponent, -1, keepdims=True)
    weights = (exponent / row_total).astype(jnp.bfloat16)
    slots = text_three.shape[0]
    text_ctx = jnp.einsum(
        "hqk,khd->qhd", weights, split_heads(text_three[:, 2]), preferred_element_type=jnp.float32
    )
    layout_ctx = jnp.einsum(
        "hqk,khd->qhd", weights, split_heads(layout_three[:, 2]), preferred_element_type=jnp.float32
    )
    log_total = (row_max + jnp.log(row_total))[..., 0]
    return (
        text_ctx.reshape(slots, -1).astype(jnp.bfloat16),
        layout_ctx.reshape(slots, -1).astype(jnp.bfloat16),
        log_total,
    )


def attend_back(text_three, layout_three, valid, log_total, text_grad, layout_grad):
    scores = score_table(text_three, layout_three, valid)
    probs = jnp.exp(scores - log_total[..., None])
    weights = probs.astype(jnp.bfloat16)
    text_heads = split_heads(text_grad)
    layout_heads = split_heads(layout_grad)
    text_dp = jnp.einsum(
        "qhd,khd->hqk",
        text_heads,
        split_heads(text_three[:, 2]),
        preferred_element_type=jnp.float32,
    )
    layout_dp = jnp.einsum(
        "qhd,khd->hqk",
        layout_heads,
        split_heads(layout_three[:, 2]),
        preferred_element_type=jnp.float32,
    )
    text_dv = jnp.einsum("hqk,qhd->khd", weights, text_heads, preferred_element_type=jnp.float32)
    layout_dv = jnp.einsum(
        "hqk,qhd->khd", weights, layout_heads, preferred_element_type=jnp.float32
    )
    text_ds = probs * (text_dp - jnp.sum(probs * text_dp, -1, keepdims=True))
    layout_ds = probs * (layout_dp - jnp.sum(probs * layout_dp, -1, keepdims=True))
    text_only, joint_ds = lax.optimization_barrier(
        (text_ds.astype(jnp.bfloat16), (text_ds + layout_ds).astype(jnp.bfloat16))
    )
    text_dq = jnp.einsum(
        "hqk,khd->qhd", text_only, split_heads(text_three[:, 1]), preferred_element_type=jnp.float32
    ) * HD ** (-0.5)
    text_dk = jnp.einsum(
        "hqk,qhd->khd", text_only, split_heads(text_three[:, 0]), preferred_element_type=jnp.float32
    ) * HD ** (-0.5)
    layout_dq = jnp.einsum(
        "hqk,khd->qhd",
        joint_ds,
        split_heads(layout_three[:, 1]),
        preferred_element_type=jnp.float32,
    ) * LHD ** (-0.5)
    layout_dk = jnp.einsum(
        "hqk,qhd->khd",
        joint_ds,
        split_heads(layout_three[:, 0]),
        preferred_element_type=jnp.float32,
    ) * LHD ** (-0.5)
    slots = text_three.shape[0]
    text_all = jnp.stack([text_dq, text_dk, text_dv], 1).reshape(slots, 3, -1)
    layout_all = jnp.stack([layout_dq, layout_dk, layout_dv], 1).reshape(slots, 3, -1)
    return (text_all, layout_all)


def project_back(attn, width, columns, three_grad, first_grad):
    rounded_grad = three_grad.astype(jnp.bfloat16)
    if columns:
        three = attn[:, 0 : 3 * width].reshape(width, 3, width)
        input_grad = first_grad + jnp.einsum(
            "sje,dje->sd", rounded_grad, three, preferred_element_type=jnp.float32
        )
    else:
        three = attn[0 : 3 * width].reshape(3, width, width)
        input_grad = first_grad + jnp.einsum(
            "sje,jde->sd", rounded_grad, three, preferred_element_type=jnp.float32
        )
    column_sums = jnp.sum(rounded_grad.astype(jnp.float32), 0)
    return (input_grad, rounded_grad, column_sums[0], column_sums[2])


def branch_forward(inputs, context, attn, packed, first, second, width, columns):
    pieces = vector_parts(packed.astype(jnp.float32), width)
    out_block = block_of(attn, 3, width, columns)
    first_res = inputs.astype(jnp.float32) + (
        jnp.dot(context, out_block, preferred_element_type=jnp.float32) + pieces[2]
    )
    hidden = normalize(first_res, pieces[3], pieces[4])
    inner = (
        jnp.dot(hidden.astype(jnp.bfloat16), first, preferred_element_type=jnp.float32) + pieces[8]
    )
    activated = gelu_exact(inner).astype(jnp.bfloat16)
    second_res = hidden + (
        jnp.dot(activated, second, preferred_element_type=jnp.float32) + pieces[5]
    )
    result = normalize(second_res, pieces[6], pieces[7])
    return (result, (first_res, inner, second_res))


def branch_backward(attn, packed, first, second, width, columns, kept_rows, grad_out):
    first_res, inner, second_res = kept_rows
    pieces = vector_parts(packed.astype(jnp.float32), width)
    hidden, first_pull = jax.vjp(normalize, first_res, pieces[3], pieces[4])
    _, second_pull = jax.vjp(normalize, second_res, pieces[6], pieces[7])
    grad_second, late_scale, late_shift = second_pull(grad_out)
    round_second = grad_second.astype(jnp.bfloat16)
    activated, gelu_pull = jax.vjp(gelu_exact, inner)
    (grad_inner,) = gelu_pull(jnp.dot(round_second, second.T, preferred_element_type=jnp.float32))
    round_inner = grad_inner.astype(jnp.bfloat16)
    grad_hidden = grad_second + jnp.dot(round_inner, first.T, preferred_element_type=jnp.float32)
    grad_first, early_scale, early_shift = first_pull(grad_hidden)
    round_first = grad_first.astype(jnp.bfloat16)
    out_block = block_of(attn, 3, width, columns)
    grad_ctx = jnp.dot(round_first, out_block.T, preferred_element_type=jnp.float32).astype(
        jnp.bfloat16
    )
    operands = (
        hidden.astype(jnp.bfloat16),
        activated.astype(jnp.bfloat16),
        round_first,
        round_second,
        round_inner,
    )
    vector_sums = (
        jnp.sum(grad_first, 0),
        early_scale,
        early_shift,
        jnp.sum(grad_second, 0),
        late_scale,
        late_shift,
        jnp.sum(grad_inner, 0),
    )
    return (grad_first, grad_ctx, operands, vector_sums)


def branch_back_a(packed, second, width, kept_rows, grad_out):
    first_res, inner, second_res = kept_rows
    pieces = vector_parts(packed.astype(jnp.float32), width)
    hidden = normalize(first_res, pieces[3], pieces[4])
    _, second_pull = jax.vjp(normalize, second_res, pieces[6], pieces[7])
    grad_second, late_scale, late_shift = second_pull(grad_out)
    round_second = grad_second.astype(jnp.bfloat16)
    activated, gelu_pull = jax.vjp(gelu_exact, inner)
    (grad_inner,) = gelu_pull(jnp.dot(round_second, second.T, preferred_element_type=jnp.float32))
    round_inner = grad_inner.astype(jnp.bfloat16)
    return (
        grad_second,
        round_second,
        grad_inner,
        round_inner,
        hidden.astype(jnp.bfloat16),
        activated.astype(jnp.bfloat16),
        late_scale,
        late_shift,
    )


def branch_back_b(attn, packed, first, width, columns, kept_rows, part_a):
    first_res, _, _ = kept_rows
    grad_second, round_second, grad_inner, round_inner, hidden_low, active_low, late_scale, late_shift = part_a
    pieces = vector_parts(packed.astype(jnp.float32), width)
    _, first_pull = jax.vjp(normalize, first_res, pieces[3], pieces[4])
    grad_hidden = grad_second + jnp.dot(round_inner, first.T, preferred_element_type=jnp.float32)
    grad_first, early_scale, early_shift = first_pull(grad_hidden)
    round_first = grad_first.astype(jnp.bfloat16)
    out_block = block_of(attn, 3, width, columns)
    grad_ctx = jnp.dot(round_first, out_block.T, preferred_element_type=jnp.float32).astype(
        jnp.bfloat16
    )
    operands = (hidden_low, active_low, round_first, round_second, round_inner)
    vector_sums = (
        jnp.sum(grad_first, 0),
        early_scale,
        early_shift,
        jnp.sum(grad_second, 0),
        late_scale,
        late_shift,
        jnp.sum(grad_inner, 0),
    )
    return (grad_first, grad_ctx, operands, vector_sums)


def page_forward(text_rows, layout_rows, length, weights):
    (text_attn, text_first, text_second, text_packed, layout_attn, _, _, layout_packed) = weights
    width = text_rows.shape[1]
    narrow = layout_rows.shape[1]
    valid = jnp.arange(text_rows.shape[0], dtype=jnp.int32) < length
    text_three = project_three(text_rows, text_attn, text_packed, width, True)
    layout_three = project_three(layout_rows, layout_attn, layout_packed, narrow, False)
    text_ctx, layout_ctx, log_total = attend(text_three, layout_three, valid)
    text_out, text_kept = branch_forward(
        text_rows, text_ctx, text_attn, text_packed, text_first, text_second, width, True
    )
    mask = valid[:, None].astype(jnp.float32)
    kept_page = (text_three, layout_three, text_ctx, layout_ctx, log_total, text_kept)
    return ((text_out * mask).astype(jnp.bfloat16), kept_page)


def page_back_ffn(length, kept_page, text_cot, weights):
    text_attn, _, text_second, text_packed = weights[:4]
    text_kept = kept_page[5]
    width = text_attn.shape[0]
    slots = text_cot.shape[0]
    valid = jnp.arange(slots, dtype=jnp.int32) < length
    mask = valid[:, None].astype(jnp.float32)
    return branch_back_a(
        text_packed, text_second, width, text_kept, text_cot.astype(jnp.float32) * mask
    )


def page_back_attn(text_rows, layout_rows, length, kept_page, text_a, layout_cot, weights):
    (
        text_attn,
        text_first,
        _,
        text_packed,
        layout_attn,
        layout_first,
        layout_second,
        layout_packed,
    ) = weights
    text_three, layout_three, _, layout_ctx, log_total, text_kept = kept_page
    width = text_rows.shape[1]
    narrow = layout_rows.shape[1]
    slots = text_rows.shape[0]
    valid = jnp.arange(slots, dtype=jnp.int32) < length
    mask = valid[:, None].astype(jnp.float32)
    layout_out, layout_kept = branch_forward(
        layout_rows,
        layout_ctx,
        layout_attn,
        layout_packed,
        layout_first,
        layout_second,
        narrow,
        False,
    )
    layout_back = branch_backward(
        layout_attn,
        layout_packed,
        layout_first,
        layout_second,
        narrow,
        False,
        layout_kept,
        layout_cot.astype(jnp.float32) * mask,
    )
    text_back = branch_back_b(text_attn, text_packed, text_first, width, True, text_kept, text_a)
    text_res_grad, text_ctx_grad, text_ops, text_sums = text_back
    layout_res_grad, layout_ctx_grad, layout_ops, layout_sums = layout_back
    text_three_grad, layout_three_grad = attend_back(
        text_three, layout_three, valid, log_total, text_ctx_grad, layout_ctx_grad
    )
    text_in_grad, text_rounded, text_query_bias, text_value_bias = project_back(
        text_attn, width, True, text_three_grad, text_res_grad
    )
    layout_in_grad, layout_rounded, layout_query_bias, layout_value_bias = project_back(
        layout_attn, narrow, False, layout_three_grad, layout_res_grad
    )
    hidden_low, active_low, first_low, second_low, inner_low = layout_ops
    three_w = jnp.einsum(
        "sd,sje->jde", layout_rows, layout_rounded, preferred_element_type=jnp.float32
    ).reshape(3 * narrow, narrow)
    out_w = jnp.einsum("sd,se->de", layout_ctx, first_low, preferred_element_type=jnp.float32)
    layout_attn_grad = jnp.concatenate([three_w, out_w], 0)
    layout_first_grad = jnp.einsum(
        "sd,sf->df", hidden_low, inner_low, preferred_element_type=jnp.float32
    )
    layout_second_grad = jnp.einsum(
        "sf,sd->fd", active_low, second_low, preferred_element_type=jnp.float32
    )
    layout_vec_grad = jnp.concatenate([layout_query_bias, layout_value_bias] + list(layout_sums))
    text_vec_grad = jnp.concatenate([text_query_bias, text_value_bias] + list(text_sums))
    small_terms = (
        text_vec_grad,
        layout_attn_grad,
        layout_first_grad,
        layout_second_grad,
        layout_vec_grad,
    )
    layout_low = (layout_out * mask).astype(jnp.bfloat16)
    grads = (text_in_grad, layout_in_grad)
    return (layout_low, grads, small_terms, text_rounded.reshape(slots, 3 * width), text_ops[2])


def flat_rows(values):
    return values.reshape(-1, values.shape[-1])


AXES = ("dp", "shard")


def rows_for(size, width, aligned):
    rows = -(-size // width)
    if aligned:
        rows = -(-rows // 8) * 8
    return rows


def pack_rows(pieces, width, aligned):
    flat = jnp.concatenate([piece.reshape(-1) for piece in pieces])
    rows = rows_for(flat.shape[0], width, aligned)
    return jnp.pad(flat, (0, rows * width - flat.shape[0])).reshape(rows, width)


def unpack_small(flat, count, shapes):
    sizes = [rows * cols for rows, cols in shapes]
    offsets = [sum(sizes[:index]) for index in range(len(sizes))]
    parts = [flat[:, offset : offset + size] for offset, size in zip(offsets, sizes)]
    (attn_rows, attn_cols), (w1_rows, w1_cols), (w2_rows, w2_cols) = shapes[1:4]
    return (
        parts[0].reshape(-1),
        parts[1].reshape(count * attn_rows, attn_cols),
        parts[2].reshape(count, w1_rows, w1_cols).transpose(1, 0, 2).reshape(w1_rows, count * w1_cols),
        parts[3].reshape(count * w2_rows, w2_cols),
        parts[4].reshape(-1),
    )


def gather_weights(text_attn, text_w1, text_w2, text_vectors, layout_attn, layout_w1, layout_w2, layout_vectors):
    rows, width = text_attn.shape
    aligned = rows % 8 == 0
    small = (text_vectors, layout_attn, layout_w1, layout_w2, layout_vectors)
    small_rows = pack_rows(small, width, aligned)
    first = jnp.concatenate([text_attn, text_w1, small_rows], 0)
    first_all = lax.all_gather(first, AXES, axis=0, tiled=True)
    count = first_all.shape[0] // first.shape[0]
    first_all = first_all.reshape(count, first.shape[0], width)
    full_attn = first_all[:, :rows].reshape(count * rows, width)
    full_w1 = first_all[:, rows : 2 * rows].reshape(count * rows, width)
    small_flat = first_all[:, 2 * rows :].reshape(count, -1)
    shapes = [(1, text_vectors.shape[0]), layout_attn.shape, layout_w1.shape, layout_w2.shape, (1, layout_vectors.shape[0])]
    full_small = unpack_small(small_flat, count, shapes)
    full_w2 = lax.all_gather(text_w2, AXES, axis=0, tiled=True)
    return (full_attn, full_w1, full_w2) + full_small


def small_blocks(count, text_vec_grad, layout_attn_grad, layout_w1_grad, layout_w2_grad, layout_vec_grad):
    local_w1_cols = layout_w1_grad.shape[1] // count
    return (
        text_vec_grad.reshape(count, -1),
        layout_attn_grad.reshape(count, -1),
        layout_w1_grad.reshape(layout_w1_grad.shape[0], count, local_w1_cols)
        .transpose(1, 0, 2)
        .reshape(count, -1),
        layout_w2_grad.reshape(count, -1),
        layout_vec_grad.reshape(count, -1),
    )


def scatter_late(count, grad_attn, small_grads):
    width = grad_attn.shape[1]
    rows = grad_attn.shape[0] // count
    blocks = small_blocks(count, *small_grads)
    joined = jnp.concatenate(blocks, 1)
    size = joined.shape[1]
    small_rows = rows_for(size, width, rows % 8 == 0)
    joined = jnp.pad(joined, ((0, 0), (0, small_rows * width - size))).reshape(count, small_rows, width)
    packed = jnp.concatenate([grad_attn.reshape(count, rows, width), joined], 1)
    summed = lax.psum_scatter(
        packed.reshape(-1, width).astype(jnp.bfloat16), AXES, scatter_dimension=0, tiled=True
    ).astype(jnp.float32)
    attn_part = summed[:rows]
    flat = summed[rows:].reshape(-1)
    sizes = [block.shape[1] for block in blocks]
    offsets = [sum(sizes[:index]) for index in range(len(sizes))]
    parts = [flat[offset : offset + size] for offset, size in zip(offsets, sizes)]
    _, layout_attn_grad, layout_w1_grad, layout_w2_grad, _ = small_grads
    local_w1_cols = layout_w1_grad.shape[1] // count
    return (
        attn_part,
        parts[0],
        parts[1].reshape(layout_attn_grad.shape[0] // count, layout_attn_grad.shape[1]),
        parts[2].reshape(layout_w1_grad.shape[0], local_w1_cols),
        parts[3].reshape(layout_w2_grad.shape[0] // count, layout_w2_grad.shape[1]),
        parts[4],
    )


def pack_early(count, grad_first, grad_second):
    width = grad_first.shape[1]
    rows = grad_first.shape[0] // count
    packed = jnp.concatenate(
        [grad_first.reshape(count, rows, width), grad_second.reshape(count, rows, width)], 1
    )
    return packed.reshape(-1, width).astype(jnp.bfloat16)


def scatter_early(count, packed, second_shape):
    rows = packed.shape[0] // (2 * count)
    summed = lax.psum_scatter(packed, AXES, scatter_dimension=0, tiled=True).astype(jnp.float32)
    return (summed[:rows], summed[rows:].reshape(-1, second_shape[1]))


def body(
    text_in,
    layout_in,
    lengths,
    text_attn,
    text_w1,
    text_w2,
    text_vectors,
    layout_attn,
    layout_w1,
    layout_w2,
    layout_vectors,
    cot_text,
    cot_layout,
):
    count = lax.psum(1, AXES)
    weights = gather_weights(
        text_attn, text_w1, text_w2, text_vectors, layout_attn, layout_w1, layout_w2, layout_vectors
    )

    page_weights = (None,) * len(weights)
    out_text, kept_all = jax.vmap(page_forward, in_axes=(0, 0, 0, page_weights))(
        text_in, layout_in, lengths, weights
    )
    text_a = jax.vmap(page_back_ffn, in_axes=(0, 0, 0, page_weights))(
        lengths, kept_all, cot_text, weights
    )
    round_second, round_inner, text_hidden, text_active = text_a[1], text_a[3], text_a[4], text_a[5]
    early = (
        jnp.einsum("sd,sf->df", flat_rows(text_hidden), flat_rows(round_inner), preferred_element_type=jnp.float32),
        jnp.einsum("sf,sd->fd", flat_rows(text_active), flat_rows(round_second), preferred_element_type=jnp.float32),
    )
    packed = pack_early(count, *early)
    packed, text_a, kept_all = lax.optimization_barrier((packed, text_a, kept_all))
    grad_first, grad_second = scatter_early(count, packed, early[1].shape)
    out_layout, (text_grad, layout_grad), small_terms, text_rounded, text_first_low = jax.vmap(
        page_back_attn, in_axes=(0, 0, 0, 0, 0, 0, page_weights)
    )(text_in, layout_in, lengths, kept_all, text_a, cot_layout, weights)
    totals = tuple(jnp.sum(term, 0) for term in small_terms)
    three_part = jnp.einsum(
        "sd,se->de", flat_rows(text_in), flat_rows(text_rounded), preferred_element_type=jnp.float32
    )
    out_part = jnp.einsum(
        "sd,se->de", flat_rows(kept_all[2]), flat_rows(text_first_low), preferred_element_type=jnp.float32
    )
    summed = scatter_late(count, jnp.concatenate([three_part, out_part], 1), totals)
    return (
        out_text,
        out_layout,
        text_grad,
        layout_grad,
        summed[0],
        grad_first,
        grad_second,
        summed[1],
        summed[2],
        summed[3],
        summed[4],
        summed[5],
    )


def solution(mesh):
    placed = (
        P(("dp", "shard"), None, None),
        P(("dp", "shard"), None, None),
        P(("dp", "shard")),
        P(("dp", "shard"), None),
        P(("dp", "shard"), None),
        P(("dp", "shard"), None),
        P(("dp", "shard")),
        P(("dp", "shard"), None),
        P(None, ("dp", "shard")),
        P(("dp", "shard"), None),
        P(("dp", "shard")),
        P(("dp", "shard"), None, None),
        P(("dp", "shard"), None, None),
    )
    return jax.shard_map(
        body,
        mesh=mesh,
        in_specs=placed,
        out_specs=(
            P(("dp", "shard"), None, None),
            P(("dp", "shard"), None, None),
            P(("dp", "shard"), None, None),
            P(("dp", "shard"), None, None),
            P(("dp", "shard"), None),
            P(("dp", "shard"), None),
            P(("dp", "shard"), None),
            P(("dp", "shard")),
            P(("dp", "shard"), None),
            P(None, ("dp", "shard")),
            P(("dp", "shard"), None),
            P(("dp", "shard")),
        ),
        check_vma=False,
    )
```

```python
import functools

import jax
import jax.numpy as jnp
from jax import lax
from jax.experimental import pallas as pl
from jax.experimental.pallas import tpu as pltpu
from jax.sharding import PartitionSpec as P


H = 12
HD = 64
LHD = 16


EPS = 1e-05
NEG = -1000000000.0


def normalize(values, scale_row, shift_row):
    centered = values - jnp.mean(values, -1, keepdims=True)
    variance = jnp.mean(centered * centered, -1, keepdims=True)
    return centered * lax.rsqrt(variance + EPS) * scale_row + shift_row


def gelu_exact(values):
    return jax.nn.gelu(values, approximate=False)


def vector_parts(packed, width):
    pieces = [packed[index * width : (index + 1) * width] for index in range(8)]
    return pieces + [packed[8 * width :]]


def split_heads(values):
    return values.reshape(values.shape[0], H, -1)


def block_of(attn, index, width, columns):
    if columns:
        return attn[:, index * width : (index + 1) * width]
    return attn[index * width : (index + 1) * width]


def project_three(inputs, attn, packed, width, columns):
    if columns:
        three = attn[:, 0 : 3 * width].reshape(width, 3, width)
        mixed = jnp.einsum("sd,dje->sje", inputs, three, preferred_element_type=jnp.float32)
    else:
        three = attn[0 : 3 * width].reshape(3, width, width)
        mixed = jnp.einsum("sd,jde->sje", inputs, three, preferred_element_type=jnp.float32)
    pieces = vector_parts(packed.astype(jnp.float32), width)
    offsets = jnp.stack([pieces[0], jnp.zeros_like(pieces[0]), pieces[1]])
    return (mixed + offsets[None]).astype(jnp.bfloat16)


def score_table(text_three, layout_three, valid):
    text_part = jnp.einsum(
        "qhd,khd->hqk",
        split_heads(text_three[:, 0]),
        split_heads(text_three[:, 1]),
        preferred_element_type=jnp.float32,
    )
    layout_part = jnp.einsum(
        "qhd,khd->hqk",
        split_heads(layout_three[:, 0]),
        split_heads(layout_three[:, 1]),
        preferred_element_type=jnp.float32,
    )
    joined = text_part * HD ** (-0.5) + layout_part * LHD ** (-0.5)
    return jnp.where(valid[None, None, :], joined, NEG)


def attend(text_three, layout_three, valid):
    scores = score_table(text_three, layout_three, valid)
    row_max = jnp.max(scores, -1, keepdims=True)
    exponent = jnp.exp(scores - row_max)
    row_total = jnp.sum(exponent, -1, keepdims=True)
    weights = (exponent / row_total).astype(jnp.bfloat16)
    slots = text_three.shape[0]
    text_ctx = jnp.einsum(
        "hqk,khd->qhd", weights, split_heads(text_three[:, 2]), preferred_element_type=jnp.float32
    )
    layout_ctx = jnp.einsum(
        "hqk,khd->qhd", weights, split_heads(layout_three[:, 2]), preferred_element_type=jnp.float32
    )
    log_total = (row_max + jnp.log(row_total))[..., 0]
    return (
        text_ctx.reshape(slots, -1).astype(jnp.bfloat16),
        layout_ctx.reshape(slots, -1).astype(jnp.bfloat16),
        log_total,
    )


def _nt(a, b):
    return lax.dot_general(a, b, (((1,), (1,)), ((), ())), preferred_element_type=jnp.float32)


def _tn(a, b):
    return lax.dot_general(a, b, (((0,), (0,)), ((), ())), preferred_element_type=jnp.float32)


def _nn(a, b):
    return lax.dot_general(a, b, (((1,), (0,)), ((), ())), preferred_element_type=jnp.float32)


def attn_back_kernel(len_ref, q_ref, k_ref, v_ref, dc_ref, ql_ref, kl_ref, vl_ref, dcl_ref, lse_ref,
                     dq_ref, dk_ref, dv_ref, dql_ref, dkl_ref, dvl_ref, *, text_scale, layout_scale):
    q, k, v, dc = q_ref[0], k_ref[0], v_ref[0], dc_ref[0]
    ql, kl, vl, dcl = ql_ref[0], kl_ref[0], vl_ref[0], dcl_ref[0]
    scores = _nt(q, k) * text_scale + _nt(ql, kl) * layout_scale
    keys = lax.broadcasted_iota(jnp.int32, scores.shape, 1)
    scores = jnp.where(keys < len_ref[0], scores, NEG)
    probs = jnp.exp(scores - lse_ref[0])
    text_dp = _nt(dc, v)
    layout_dp = _nt(dcl, vl)
    text_ds = probs * (text_dp - jnp.sum(probs * text_dp, 1, keepdims=True))
    layout_ds = probs * (layout_dp - jnp.sum(probs * layout_dp, 1, keepdims=True))
    text_g = text_ds.astype(jnp.bfloat16)
    joint_g = (text_ds + layout_ds).astype(jnp.bfloat16)
    weights = probs.astype(jnp.bfloat16)
    dq_ref[0] = (_nn(text_g, k) * text_scale).astype(dq_ref.dtype)
    dk_ref[0] = (_tn(text_g, q) * text_scale).astype(dk_ref.dtype)
    dv_ref[0] = _tn(weights, dc).astype(dv_ref.dtype)
    dql_ref[0] = (_nn(joint_g, kl) * layout_scale).astype(dql_ref.dtype)
    dkl_ref[0] = (_tn(joint_g, ql) * layout_scale).astype(dkl_ref.dtype)
    dvl_ref[0] = _tn(weights, dcl).astype(dvl_ref.dtype)


def attn_back_heads(length, q, k, v, dc, ql, kl, vl, dcl, lse, text_scale, layout_scale):
    heads, slots, wide = q.shape
    narrow = ql.shape[2]
    text_spec = pl.BlockSpec((1, slots, wide), lambda h, n: (h, 0, 0))
    layout_spec = pl.BlockSpec((1, slots, narrow), lambda h, n: (h, 0, 0))
    lse_spec = pl.BlockSpec((1, slots, 1), lambda h, n: (h, 0, 0))
    text_out = jax.ShapeDtypeStruct((heads, slots, wide), jnp.bfloat16)
    layout_out = jax.ShapeDtypeStruct((heads, slots, narrow), jnp.bfloat16)
    flops = heads * slots * slots * 2 * (4 * wide + 4 * narrow)
    return pl.pallas_call(
        functools.partial(attn_back_kernel, text_scale=text_scale, layout_scale=layout_scale),
        grid_spec=pltpu.PrefetchScalarGridSpec(
            num_scalar_prefetch=1,
            grid=(heads,),
            in_specs=[text_spec] * 4 + [layout_spec] * 4 + [lse_spec],
            out_specs=[text_spec] * 3 + [layout_spec] * 3,
        ),
        out_shape=[text_out] * 3 + [layout_out] * 3,
        compiler_params=pltpu.CompilerParams(dimension_semantics=("arbitrary",)),
        cost_estimate=pl.CostEstimate(
            flops=flops,
            transcendentals=heads * slots * slots,
            bytes_accessed=heads * slots * (8 * wide + 8 * narrow + 4),
        ),
    )(length, q, k, v, dc, ql, kl, vl, dcl, lse)


def to_heads(values, size):
    return values.reshape(values.shape[0], H, size).transpose(1, 0, 2)


def from_heads(values):
    return values.transpose(1, 0, 2).reshape(values.shape[1], -1)


def attend_back(text_three, layout_three, length, log_total, text_grad, layout_grad):
    outs = attn_back_heads(
        jnp.reshape(length, (1,)).astype(jnp.int32),
        to_heads(text_three[:, 0], HD),
        to_heads(text_three[:, 1], HD),
        to_heads(text_three[:, 2], HD),
        to_heads(text_grad, HD),
        to_heads(layout_three[:, 0], LHD),
        to_heads(layout_three[:, 1], LHD),
        to_heads(layout_three[:, 2], LHD),
        to_heads(layout_grad, LHD),
        log_total[:, :, None],
        HD ** (-0.5),
        LHD ** (-0.5),
    )
    text_all = jnp.stack([from_heads(part) for part in outs[:3]], 1)
    layout_all = jnp.stack([from_heads(part) for part in outs[3:]], 1)
    return (text_all, layout_all)


def project_back(attn, width, columns, three_grad, first_grad):
    rounded_grad = three_grad.astype(jnp.bfloat16)
    if columns:
        three = attn[:, 0 : 3 * width].reshape(width, 3, width)
        input_grad = first_grad + jnp.einsum(
            "sje,dje->sd", rounded_grad, three, preferred_element_type=jnp.float32
        )
    else:
        three = attn[0 : 3 * width].reshape(3, width, width)
        input_grad = first_grad + jnp.einsum(
            "sje,jde->sd", rounded_grad, three, preferred_element_type=jnp.float32
        )
    column_sums = jnp.sum(rounded_grad.astype(jnp.float32), 0)
    return (input_grad, rounded_grad, column_sums[0], column_sums[2])


def branch_forward(inputs, context, attn, packed, first, second, width, columns):
    pieces = vector_parts(packed.astype(jnp.float32), width)
    out_block = block_of(attn, 3, width, columns)
    first_res = inputs.astype(jnp.float32) + (
        jnp.dot(context, out_block, preferred_element_type=jnp.float32) + pieces[2]
    )
    hidden = normalize(first_res, pieces[3], pieces[4])
    inner = (
        jnp.dot(hidden.astype(jnp.bfloat16), first, preferred_element_type=jnp.float32) + pieces[8]
    )
    activated = gelu_exact(inner).astype(jnp.bfloat16)
    second_res = hidden + (
        jnp.dot(activated, second, preferred_element_type=jnp.float32) + pieces[5]
    )
    result = normalize(second_res, pieces[6], pieces[7])
    return (result, (first_res, inner, second_res))


def branch_backward(attn, packed, first, second, width, columns, kept_rows, grad_out):
    first_res, inner, second_res = kept_rows
    pieces = vector_parts(packed.astype(jnp.float32), width)
    hidden, first_pull = jax.vjp(normalize, first_res, pieces[3], pieces[4])
    _, second_pull = jax.vjp(normalize, second_res, pieces[6], pieces[7])
    grad_second, late_scale, late_shift = second_pull(grad_out)
    round_second = grad_second.astype(jnp.bfloat16)
    activated, gelu_pull = jax.vjp(gelu_exact, inner)
    (grad_inner,) = gelu_pull(jnp.dot(round_second, second.T, preferred_element_type=jnp.float32))
    round_inner = grad_inner.astype(jnp.bfloat16)
    grad_hidden = grad_second + jnp.dot(round_inner, first.T, preferred_element_type=jnp.float32)
    grad_first, early_scale, early_shift = first_pull(grad_hidden)
    round_first = grad_first.astype(jnp.bfloat16)
    out_block = block_of(attn, 3, width, columns)
    grad_ctx = jnp.dot(round_first, out_block.T, preferred_element_type=jnp.float32).astype(
        jnp.bfloat16
    )
    operands = (
        hidden.astype(jnp.bfloat16),
        activated.astype(jnp.bfloat16),
        round_first,
        round_second,
        round_inner,
    )
    vector_sums = (
        jnp.sum(grad_first, 0),
        early_scale,
        early_shift,
        jnp.sum(grad_second, 0),
        late_scale,
        late_shift,
        jnp.sum(grad_inner, 0),
    )
    return (grad_first, grad_ctx, operands, vector_sums)


def branch_back_a(packed, second, width, kept_rows, grad_out):
    first_res, inner, second_res = kept_rows
    pieces = vector_parts(packed.astype(jnp.float32), width)
    hidden = normalize(first_res, pieces[3], pieces[4])
    _, second_pull = jax.vjp(normalize, second_res, pieces[6], pieces[7])
    grad_second, late_scale, late_shift = second_pull(grad_out)
    round_second = grad_second.astype(jnp.bfloat16)
    activated, gelu_pull = jax.vjp(gelu_exact, inner)
    (grad_inner,) = gelu_pull(jnp.dot(round_second, second.T, preferred_element_type=jnp.float32))
    round_inner = grad_inner.astype(jnp.bfloat16)
    return (
        grad_second,
        round_second,
        grad_inner,
        round_inner,
        hidden.astype(jnp.bfloat16),
        activated.astype(jnp.bfloat16),
        late_scale,
        late_shift,
    )


def branch_back_b(attn, packed, first, width, columns, kept_rows, part_a):
    first_res, _, _ = kept_rows
    grad_second, round_second, grad_inner, round_inner, hidden_low, active_low, late_scale, late_shift = part_a
    pieces = vector_parts(packed.astype(jnp.float32), width)
    _, first_pull = jax.vjp(normalize, first_res, pieces[3], pieces[4])
    grad_hidden = grad_second + jnp.dot(round_inner, first.T, preferred_element_type=jnp.float32)
    grad_first, early_scale, early_shift = first_pull(grad_hidden)
    round_first = grad_first.astype(jnp.bfloat16)
    out_block = block_of(attn, 3, width, columns)
    grad_ctx = jnp.dot(round_first, out_block.T, preferred_element_type=jnp.float32).astype(
        jnp.bfloat16
    )
    operands = (hidden_low, active_low, round_first, round_second, round_inner)
    vector_sums = (
        jnp.sum(grad_first, 0),
        early_scale,
        early_shift,
        jnp.sum(grad_second, 0),
        late_scale,
        late_shift,
        jnp.sum(grad_inner, 0),
    )
    return (grad_first, grad_ctx, operands, vector_sums)


def page_forward(text_rows, layout_rows, length, weights):
    (text_attn, text_first, text_second, text_packed, layout_attn, _, _, layout_packed) = weights
    width = text_rows.shape[1]
    narrow = layout_rows.shape[1]
    valid = jnp.arange(text_rows.shape[0], dtype=jnp.int32) < length
    text_three = project_three(text_rows, text_attn, text_packed, width, True)
    layout_three = project_three(layout_rows, layout_attn, layout_packed, narrow, False)
    text_ctx, layout_ctx, log_total = attend(text_three, layout_three, valid)
    text_out, text_kept = branch_forward(
        text_rows, text_ctx, text_attn, text_packed, text_first, text_second, width, True
    )
    mask = valid[:, None].astype(jnp.float32)
    kept_page = (text_three, layout_three, text_ctx, layout_ctx, log_total, text_kept)
    return ((text_out * mask).astype(jnp.bfloat16), kept_page)


def page_back_ffn(length, kept_page, text_cot, weights):
    text_attn, _, text_second, text_packed = weights[:4]
    text_kept = kept_page[5]
    width = text_attn.shape[0]
    slots = text_cot.shape[0]
    valid = jnp.arange(slots, dtype=jnp.int32) < length
    mask = valid[:, None].astype(jnp.float32)
    return branch_back_a(
        text_packed, text_second, width, text_kept, text_cot.astype(jnp.float32) * mask
    )


def page_back_attn(text_rows, layout_rows, length, kept_page, text_a, layout_cot, weights):
    (
        text_attn,
        text_first,
        _,
        text_packed,
        layout_attn,
        layout_first,
        layout_second,
        layout_packed,
    ) = weights
    text_three, layout_three, _, layout_ctx, log_total, text_kept = kept_page
    width = text_rows.shape[1]
    narrow = layout_rows.shape[1]
    slots = text_rows.shape[0]
    valid = jnp.arange(slots, dtype=jnp.int32) < length
    mask = valid[:, None].astype(jnp.float32)
    layout_out, layout_kept = branch_forward(
        layout_rows,
        layout_ctx,
        layout_attn,
        layout_packed,
        layout_first,
        layout_second,
        narrow,
        False,
    )
    layout_back = branch_backward(
        layout_attn,
        layout_packed,
        layout_first,
        layout_second,
        narrow,
        False,
        layout_kept,
        layout_cot.astype(jnp.float32) * mask,
    )
    text_back = branch_back_b(text_attn, text_packed, text_first, width, True, text_kept, text_a)
    text_res_grad, text_ctx_grad, text_ops, text_sums = text_back
    layout_res_grad, layout_ctx_grad, layout_ops, layout_sums = layout_back
    text_three_grad, layout_three_grad = attend_back(
        text_three, layout_three, length, log_total, text_ctx_grad, layout_ctx_grad
    )
    text_in_grad, text_rounded, text_query_bias, text_value_bias = project_back(
        text_attn, width, True, text_three_grad, text_res_grad
    )
    layout_in_grad, layout_rounded, layout_query_bias, layout_value_bias = project_back(
        layout_attn, narrow, False, layout_three_grad, layout_res_grad
    )
    hidden_low, active_low, first_low, second_low, inner_low = layout_ops
    three_w = jnp.einsum(
        "sd,sje->jde", layout_rows, layout_rounded, preferred_element_type=jnp.float32
    ).reshape(3 * narrow, narrow)
    out_w = jnp.einsum("sd,se->de", layout_ctx, first_low, preferred_element_type=jnp.float32)
    layout_attn_grad = jnp.concatenate([three_w, out_w], 0)
    layout_first_grad = jnp.einsum(
        "sd,sf->df", hidden_low, inner_low, preferred_element_type=jnp.float32
    )
    layout_second_grad = jnp.einsum(
        "sf,sd->fd", active_low, second_low, preferred_element_type=jnp.float32
    )
    layout_vec_grad = jnp.concatenate([layout_query_bias, layout_value_bias] + list(layout_sums))
    text_vec_grad = jnp.concatenate([text_query_bias, text_value_bias] + list(text_sums))
    small_terms = (
        text_vec_grad,
        layout_attn_grad,
        layout_first_grad,
        layout_second_grad,
        layout_vec_grad,
    )
    layout_low = (layout_out * mask).astype(jnp.bfloat16)
    grads = (text_in_grad, layout_in_grad)
    return (layout_low, grads, small_terms, text_rounded.reshape(slots, 3 * width), text_ops[2])


def flat_rows(values):
    return values.reshape(-1, values.shape[-1])


AXES = ("dp", "shard")


def rows_for(size, width, aligned):
    rows = -(-size // width)
    if aligned:
        rows = -(-rows // 8) * 8
    return rows


def pack_rows(pieces, width, aligned):
    flat = jnp.concatenate([piece.reshape(-1) for piece in pieces])
    rows = rows_for(flat.shape[0], width, aligned)
    return jnp.pad(flat, (0, rows * width - flat.shape[0])).reshape(rows, width)


def unpack_small(flat, count, shapes):
    sizes = [rows * cols for rows, cols in shapes]
    offsets = [sum(sizes[:index]) for index in range(len(sizes))]
    parts = [flat[:, offset : offset + size] for offset, size in zip(offsets, sizes)]
    (attn_rows, attn_cols), (w1_rows, w1_cols), (w2_rows, w2_cols) = shapes[1:4]
    return (
        parts[0].reshape(-1),
        parts[1].reshape(count * attn_rows, attn_cols),
        parts[2].reshape(count, w1_rows, w1_cols).transpose(1, 0, 2).reshape(w1_rows, count * w1_cols),
        parts[3].reshape(count * w2_rows, w2_cols),
        parts[4].reshape(-1),
    )


def gather_weights(text_attn, text_w1, text_w2, text_vectors, layout_attn, layout_w1, layout_w2, layout_vectors):
    rows, width = text_attn.shape
    aligned = rows % 8 == 0
    small = (text_vectors, layout_attn, layout_w1, layout_w2, layout_vectors)
    small_rows = pack_rows(small, width, aligned)
    first = jnp.concatenate([text_attn, text_w1, small_rows], 0)
    first_all = lax.all_gather(first, AXES, axis=0, tiled=True)
    count = first_all.shape[0] // first.shape[0]
    first_all = first_all.reshape(count, first.shape[0], width)
    full_attn = first_all[:, :rows].reshape(count * rows, width)
    full_w1 = first_all[:, rows : 2 * rows].reshape(count * rows, width)
    small_flat = first_all[:, 2 * rows :].reshape(count, -1)
    shapes = [(1, text_vectors.shape[0]), layout_attn.shape, layout_w1.shape, layout_w2.shape, (1, layout_vectors.shape[0])]
    full_small = unpack_small(small_flat, count, shapes)
    full_w2 = lax.all_gather(text_w2, AXES, axis=0, tiled=True)
    return (full_attn, full_w1, full_w2) + full_small


def small_blocks(count, text_vec_grad, layout_attn_grad, layout_w1_grad, layout_w2_grad, layout_vec_grad):
    local_w1_cols = layout_w1_grad.shape[1] // count
    return (
        text_vec_grad.reshape(count, -1),
        layout_attn_grad.reshape(count, -1),
        layout_w1_grad.reshape(layout_w1_grad.shape[0], count, local_w1_cols)
        .transpose(1, 0, 2)
        .reshape(count, -1),
        layout_w2_grad.reshape(count, -1),
        layout_vec_grad.reshape(count, -1),
    )


def scatter_late(count, grad_attn, small_grads):
    width = grad_attn.shape[1]
    rows = grad_attn.shape[0] // count
    blocks = small_blocks(count, *small_grads)
    joined = jnp.concatenate(blocks, 1)
    size = joined.shape[1]
    small_rows = rows_for(size, width, rows % 8 == 0)
    joined = jnp.pad(joined, ((0, 0), (0, small_rows * width - size))).reshape(count, small_rows, width)
    packed = jnp.concatenate([grad_attn.reshape(count, rows, width), joined], 1)
    summed = lax.psum_scatter(
        packed.reshape(-1, width).astype(jnp.bfloat16), AXES, scatter_dimension=0, tiled=True
    ).astype(jnp.float32)
    attn_part = summed[:rows]
    flat = summed[rows:].reshape(-1)
    sizes = [block.shape[1] for block in blocks]
    offsets = [sum(sizes[:index]) for index in range(len(sizes))]
    parts = [flat[offset : offset + size] for offset, size in zip(offsets, sizes)]
    _, layout_attn_grad, layout_w1_grad, layout_w2_grad, _ = small_grads
    local_w1_cols = layout_w1_grad.shape[1] // count
    return (
        attn_part,
        parts[0],
        parts[1].reshape(layout_attn_grad.shape[0] // count, layout_attn_grad.shape[1]),
        parts[2].reshape(layout_w1_grad.shape[0], local_w1_cols),
        parts[3].reshape(layout_w2_grad.shape[0] // count, layout_w2_grad.shape[1]),
        parts[4],
    )


def pack_early(count, grad_first, grad_second):
    width = grad_first.shape[1]
    rows = grad_first.shape[0] // count
    packed = jnp.concatenate(
        [grad_first.reshape(count, rows, width), grad_second.reshape(count, rows, width)], 1
    )
    return packed.reshape(-1, width).astype(jnp.bfloat16)


def scatter_early(count, packed, second_shape):
    rows = packed.shape[0] // (2 * count)
    summed = lax.psum_scatter(packed, AXES, scatter_dimension=0, tiled=True).astype(jnp.float32)
    return (summed[:rows], summed[rows:].reshape(-1, second_shape[1]))


def body(
    text_in,
    layout_in,
    lengths,
    text_attn,
    text_w1,
    text_w2,
    text_vectors,
    layout_attn,
    layout_w1,
    layout_w2,
    layout_vectors,
    cot_text,
    cot_layout,
):
    count = lax.psum(1, AXES)
    weights = gather_weights(
        text_attn, text_w1, text_w2, text_vectors, layout_attn, layout_w1, layout_w2, layout_vectors
    )

    page_weights = (None,) * len(weights)
    out_text, kept_all = jax.vmap(page_forward, in_axes=(0, 0, 0, page_weights))(
        text_in, layout_in, lengths, weights
    )
    text_a = jax.vmap(page_back_ffn, in_axes=(0, 0, 0, page_weights))(
        lengths, kept_all, cot_text, weights
    )
    round_second, round_inner, text_hidden, text_active = text_a[1], text_a[3], text_a[4], text_a[5]
    early = (
        jnp.einsum("sd,sf->df", flat_rows(text_hidden), flat_rows(round_inner), preferred_element_type=jnp.float32),
        jnp.einsum("sf,sd->fd", flat_rows(text_active), flat_rows(round_second), preferred_element_type=jnp.float32),
    )
    packed = pack_early(count, *early)
    packed, text_a, kept_all = lax.optimization_barrier((packed, text_a, kept_all))
    grad_first, grad_second = scatter_early(count, packed, early[1].shape)
    out_layout, (text_grad, layout_grad), small_terms, text_rounded, text_first_low = jax.vmap(
        page_back_attn, in_axes=(0, 0, 0, 0, 0, 0, page_weights)
    )(text_in, layout_in, lengths, kept_all, text_a, cot_layout, weights)
    totals = tuple(jnp.sum(term, 0) for term in small_terms)
    three_part = jnp.einsum(
        "sd,se->de", flat_rows(text_in), flat_rows(text_rounded), preferred_element_type=jnp.float32
    )
    out_part = jnp.einsum(
        "sd,se->de", flat_rows(kept_all[2]), flat_rows(text_first_low), preferred_element_type=jnp.float32
    )
    summed = scatter_late(count, jnp.concatenate([three_part, out_part], 1), totals)
    return (
        out_text,
        out_layout,
        text_grad,
        layout_grad,
        summed[0],
        grad_first,
        grad_second,
        summed[1],
        summed[2],
        summed[3],
        summed[4],
        summed[5],
    )


def solution(mesh):
    placed = (
        P(("dp", "shard"), None, None),
        P(("dp", "shard"), None, None),
        P(("dp", "shard")),
        P(("dp", "shard"), None),
        P(("dp", "shard"), None),
        P(("dp", "shard"), None),
        P(("dp", "shard")),
        P(("dp", "shard"), None),
        P(None, ("dp", "shard")),
        P(("dp", "shard"), None),
        P(("dp", "shard")),
        P(("dp", "shard"), None, None),
        P(("dp", "shard"), None, None),
    )
    return jax.shard_map(
        body,
        mesh=mesh,
        in_specs=placed,
        out_specs=(
            P(("dp", "shard"), None, None),
            P(("dp", "shard"), None, None),
            P(("dp", "shard"), None, None),
            P(("dp", "shard"), None, None),
            P(("dp", "shard"), None),
            P(("dp", "shard"), None),
            P(("dp", "shard"), None),
            P(("dp", "shard")),
            P(("dp", "shard"), None),
            P(None, ("dp", "shard")),
            P(("dp", "shard"), None),
            P(("dp", "shard")),
        ),
        check_vma=False,
    )
```

```python
import functools

import jax
import jax.numpy as jnp
from jax import lax
from jax.experimental import pallas as pl
from jax.experimental.pallas import tpu as pltpu
from jax.sharding import PartitionSpec as P


H = 12
HD = 64
LHD = 16


EPS = 1e-05
NEG = -1000000000.0


def normalize(values, scale_row, shift_row):
    centered = values - jnp.mean(values, -1, keepdims=True)
    variance = jnp.mean(centered * centered, -1, keepdims=True)
    return centered * lax.rsqrt(variance + EPS) * scale_row + shift_row


def gelu_exact(values):
    return 0.5 * values * (1.0 + lax.erf(values * (0.5 ** 0.5)))


def vector_parts(packed, width):
    pieces = [packed[index * width : (index + 1) * width] for index in range(8)]
    return pieces + [packed[8 * width :]]


def split_heads(values):
    return values.reshape(values.shape[0], H, -1)


def block_of(attn, index, width, columns):
    if columns:
        return attn[:, index * width : (index + 1) * width]
    return attn[index * width : (index + 1) * width]


def project_three(inputs, attn, packed, width, columns):
    if columns:
        three = attn[:, 0 : 3 * width].reshape(width, 3, width)
        mixed = jnp.einsum("sd,dje->sje", inputs, three, preferred_element_type=jnp.float32)
    else:
        three = attn[0 : 3 * width].reshape(3, width, width)
        mixed = jnp.einsum("sd,jde->sje", inputs, three, preferred_element_type=jnp.float32)
    pieces = vector_parts(packed.astype(jnp.float32), width)
    offsets = jnp.stack([pieces[0], jnp.zeros_like(pieces[0]), pieces[1]])
    return (mixed + offsets[None]).astype(jnp.bfloat16)


def score_table(text_three, layout_three, valid):
    text_part = jnp.einsum(
        "qhd,khd->hqk",
        split_heads(text_three[:, 0]),
        split_heads(text_three[:, 1]),
        preferred_element_type=jnp.float32,
    )
    layout_part = jnp.einsum(
        "qhd,khd->hqk",
        split_heads(layout_three[:, 0]),
        split_heads(layout_three[:, 1]),
        preferred_element_type=jnp.float32,
    )
    joined = text_part * HD ** (-0.5) + layout_part * LHD ** (-0.5)
    return jnp.where(valid[None, None, :], joined, NEG)


def attend(text_three, layout_three, valid):
    scores = score_table(text_three, layout_three, valid)
    row_max = jnp.max(scores, -1, keepdims=True)
    exponent = jnp.exp(scores - row_max)
    row_total = jnp.sum(exponent, -1, keepdims=True)
    weights = (exponent / row_total).astype(jnp.bfloat16)
    slots = text_three.shape[0]
    text_ctx = jnp.einsum(
        "hqk,khd->qhd", weights, split_heads(text_three[:, 2]), preferred_element_type=jnp.float32
    )
    layout_ctx = jnp.einsum(
        "hqk,khd->qhd", weights, split_heads(layout_three[:, 2]), preferred_element_type=jnp.float32
    )
    log_total = (row_max + jnp.log(row_total))[..., 0]
    return (
        text_ctx.reshape(slots, -1).astype(jnp.bfloat16),
        layout_ctx.reshape(slots, -1).astype(jnp.bfloat16),
        log_total,
    )


def _nn(a, b):
    return lax.dot_general(a, b, (((1,), (0,)), ((), ())), preferred_element_type=jnp.float32)


def _nt(a, b):
    return lax.dot_general(a, b, (((1,), (1,)), ((), ())), preferred_element_type=jnp.float32)


def attn_back_kernel(len_ref, text_ref, dc_ref, layout_ref, dcl_ref, lse_ref, text_out, layout_out, *, scales):
    text_scale, layout_scale = scales
    query, key, value = text_ref[0], text_ref[1], text_ref[2]
    query_l, key_l, value_l = layout_ref[0], layout_ref[1], layout_ref[2]
    scores = _nn(key.T, query) * text_scale + _nn(key_l.T, query_l) * layout_scale
    keys = lax.broadcasted_iota(jnp.int32, scores.shape, 0)
    scores = jnp.where(keys < len_ref[0], scores, NEG)
    probs = jnp.exp(scores - lse_ref[0])
    text_dp = _nn(value.T, dc_ref[...])
    layout_dp = _nn(value_l.T, dcl_ref[...])
    text_ds = probs * (text_dp - jnp.sum(probs * text_dp, 0, keepdims=True))
    layout_ds = probs * (layout_dp - jnp.sum(probs * layout_dp, 0, keepdims=True))
    text_g = text_ds.astype(jnp.bfloat16)
    joint_g = (text_ds + layout_ds).astype(jnp.bfloat16)
    weights = probs.astype(jnp.bfloat16)
    text_out[0] = (_nn(key, text_g) * text_scale).astype(text_out.dtype)
    text_out[1] = (_nt(query, text_g) * text_scale).astype(text_out.dtype)
    text_out[2] = _nt(dc_ref[...], weights).astype(text_out.dtype)
    layout_out[0] = (_nn(key_l, joint_g) * layout_scale).astype(layout_out.dtype)
    layout_out[1] = (_nt(query_l, joint_g) * layout_scale).astype(layout_out.dtype)
    layout_out[2] = _nt(dcl_ref[...], weights).astype(layout_out.dtype)


def attn_back_heads(length, text_t, dc_t, layout_t, dcl_t, lse, scales):
    parts, width, slots = text_t.shape
    narrow = layout_t.shape[1]
    wide, thin = width // H, narrow // H
    text_spec = pl.BlockSpec((parts, wide, slots), lambda h, n: (0, h, 0))
    layout_spec = pl.BlockSpec((parts, thin, slots), lambda h, n: (0, h, 0))
    flops = H * slots * slots * 2 * (4 * wide + 4 * thin)
    return pl.pallas_call(
        functools.partial(attn_back_kernel, scales=scales),
        grid_spec=pltpu.PrefetchScalarGridSpec(
            num_scalar_prefetch=1,
            grid=(H,),
            in_specs=[
                text_spec,
                pl.BlockSpec((wide, slots), lambda h, n: (h, 0)),
                layout_spec,
                pl.BlockSpec((thin, slots), lambda h, n: (h, 0)),
                pl.BlockSpec((1, 1, slots), lambda h, n: (h, 0, 0)),
            ],
            out_specs=[text_spec, layout_spec],
        ),
        out_shape=[
            jax.ShapeDtypeStruct(text_t.shape, jnp.bfloat16),
            jax.ShapeDtypeStruct(layout_t.shape, jnp.bfloat16),
        ],
        compiler_params=pltpu.CompilerParams(dimension_semantics=("arbitrary",)),
        cost_estimate=pl.CostEstimate(
            flops=flops,
            transcendentals=H * slots * slots,
            bytes_accessed=slots * (8 * width + 8 * narrow + 4 * H),
        ),
    )(length, text_t, dc_t, layout_t, dcl_t, lse)


def attend_back(text_three, layout_three, length, log_total, text_grad, layout_grad):
    return attn_back_heads(
        jnp.reshape(length, (1,)).astype(jnp.int32),
        text_three.transpose(1, 2, 0),
        text_grad.T,
        layout_three.transpose(1, 2, 0),
        layout_grad.T,
        log_total[:, None, :],
        (HD ** (-0.5), LHD ** (-0.5)),
    )


def project_back(attn, width, columns, grad_t, first_grad):
    if columns:
        three = attn[:, 0 : 3 * width].reshape(width, 3, width)
        input_grad = first_grad + jnp.einsum(
            "jes,dje->sd", grad_t, three, preferred_element_type=jnp.float32
        )
    else:
        three = attn[0 : 3 * width].reshape(3, width, width)
        input_grad = first_grad + jnp.einsum(
            "jes,jde->sd", grad_t, three, preferred_element_type=jnp.float32
        )
    column_sums = jnp.sum(grad_t.astype(jnp.float32), 2)
    return (input_grad, grad_t, column_sums[0], column_sums[2])


def branch_forward(inputs, context, attn, packed, first, second, width, columns):
    pieces = vector_parts(packed.astype(jnp.float32), width)
    out_block = block_of(attn, 3, width, columns)
    first_res = inputs.astype(jnp.float32) + (
        jnp.dot(context, out_block, preferred_element_type=jnp.float32) + pieces[2]
    )
    hidden = normalize(first_res, pieces[3], pieces[4])
    inner = (
        jnp.dot(hidden.astype(jnp.bfloat16), first, preferred_element_type=jnp.float32) + pieces[8]
    )
    activated = gelu_exact(inner).astype(jnp.bfloat16)
    second_res = hidden + (
        jnp.dot(activated, second, preferred_element_type=jnp.float32) + pieces[5]
    )
    result = normalize(second_res, pieces[6], pieces[7])
    return (result, (first_res, inner, second_res))


def branch_backward(attn, packed, first, second, width, columns, kept_rows, grad_out):
    first_res, inner, second_res = kept_rows
    pieces = vector_parts(packed.astype(jnp.float32), width)
    hidden, first_pull = jax.vjp(normalize, first_res, pieces[3], pieces[4])
    _, second_pull = jax.vjp(normalize, second_res, pieces[6], pieces[7])
    grad_second, late_scale, late_shift = second_pull(grad_out)
    round_second = grad_second.astype(jnp.bfloat16)
    activated, gelu_pull = jax.vjp(gelu_exact, inner)
    (grad_inner,) = gelu_pull(jnp.dot(round_second, second.T, preferred_element_type=jnp.float32))
    round_inner = grad_inner.astype(jnp.bfloat16)
    grad_hidden = grad_second + jnp.dot(round_inner, first.T, preferred_element_type=jnp.float32)
    grad_first, early_scale, early_shift = first_pull(grad_hidden)
    round_first = grad_first.astype(jnp.bfloat16)
    out_block = block_of(attn, 3, width, columns)
    grad_ctx = jnp.dot(round_first, out_block.T, preferred_element_type=jnp.float32).astype(
        jnp.bfloat16
    )
    operands = (
        hidden.astype(jnp.bfloat16),
        activated.astype(jnp.bfloat16),
        round_first,
        round_second,
        round_inner,
    )
    vector_sums = (
        jnp.sum(grad_first, 0),
        early_scale,
        early_shift,
        jnp.sum(grad_second, 0),
        late_scale,
        late_shift,
        jnp.sum(grad_inner, 0),
    )
    return (grad_first, grad_ctx, operands, vector_sums)


def branch_back_a(packed, second, width, kept_rows, grad_out):
    first_res, inner, second_res = kept_rows
    pieces = vector_parts(packed.astype(jnp.float32), width)
    hidden = normalize(first_res, pieces[3], pieces[4])
    _, second_pull = jax.vjp(normalize, second_res, pieces[6], pieces[7])
    grad_second, late_scale, late_shift = second_pull(grad_out)
    round_second = grad_second.astype(jnp.bfloat16)
    activated, gelu_pull = jax.vjp(gelu_exact, inner)
    (grad_inner,) = gelu_pull(jnp.dot(round_second, second.T, preferred_element_type=jnp.float32))
    round_inner = grad_inner.astype(jnp.bfloat16)
    return (
        grad_second,
        round_second,
        grad_inner,
        round_inner,
        hidden.astype(jnp.bfloat16),
        activated.astype(jnp.bfloat16),
        late_scale,
        late_shift,
    )


def branch_back_b(attn, packed, first, width, columns, kept_rows, part_a):
    first_res, _, _ = kept_rows
    grad_second, round_second, grad_inner, round_inner, hidden_low, active_low, late_scale, late_shift = part_a
    pieces = vector_parts(packed.astype(jnp.float32), width)
    _, first_pull = jax.vjp(normalize, first_res, pieces[3], pieces[4])
    grad_hidden = grad_second + jnp.dot(round_inner, first.T, preferred_element_type=jnp.float32)
    grad_first, early_scale, early_shift = first_pull(grad_hidden)
    round_first = grad_first.astype(jnp.bfloat16)
    out_block = block_of(attn, 3, width, columns)
    grad_ctx = jnp.dot(round_first, out_block.T, preferred_element_type=jnp.float32).astype(
        jnp.bfloat16
    )
    operands = (hidden_low, active_low, round_first, round_second, round_inner)
    vector_sums = (
        jnp.sum(grad_first, 0),
        early_scale,
        early_shift,
        jnp.sum(grad_second, 0),
        late_scale,
        late_shift,
        jnp.sum(grad_inner, 0),
    )
    return (grad_first, grad_ctx, operands, vector_sums)


def page_forward(text_rows, layout_rows, length, weights):
    (text_attn, text_first, text_second, text_packed, layout_attn, _, _, layout_packed) = weights
    width = text_rows.shape[1]
    narrow = layout_rows.shape[1]
    valid = jnp.arange(text_rows.shape[0], dtype=jnp.int32) < length
    text_three = project_three(text_rows, text_attn, text_packed, width, True)
    layout_three = project_three(layout_rows, layout_attn, layout_packed, narrow, False)
    text_ctx, layout_ctx, log_total = attend(text_three, layout_three, valid)
    text_out, text_kept = branch_forward(
        text_rows, text_ctx, text_attn, text_packed, text_first, text_second, width, True
    )
    mask = valid[:, None].astype(jnp.float32)
    kept_page = (text_three, layout_three, text_ctx, layout_ctx, log_total, text_kept)
    return ((text_out * mask).astype(jnp.bfloat16), kept_page)


def page_back_ffn(length, kept_page, text_cot, weights):
    text_attn, _, text_second, text_packed = weights[:4]
    text_kept = kept_page[5]
    width = text_attn.shape[0]
    slots = text_cot.shape[0]
    valid = jnp.arange(slots, dtype=jnp.int32) < length
    mask = valid[:, None].astype(jnp.float32)
    return branch_back_a(
        text_packed, text_second, width, text_kept, text_cot.astype(jnp.float32) * mask
    )


def page_back_attn(text_rows, layout_rows, length, kept_page, text_a, layout_cot, weights):
    (
        text_attn,
        text_first,
        _,
        text_packed,
        layout_attn,
        layout_first,
        layout_second,
        layout_packed,
    ) = weights
    text_three, layout_three, _, layout_ctx, log_total, text_kept = kept_page
    width = text_rows.shape[1]
    narrow = layout_rows.shape[1]
    slots = text_rows.shape[0]
    valid = jnp.arange(slots, dtype=jnp.int32) < length
    mask = valid[:, None].astype(jnp.float32)
    layout_out, layout_kept = branch_forward(
        layout_rows,
        layout_ctx,
        layout_attn,
        layout_packed,
        layout_first,
        layout_second,
        narrow,
        False,
    )
    layout_back = branch_backward(
        layout_attn,
        layout_packed,
        layout_first,
        layout_second,
        narrow,
        False,
        layout_kept,
        layout_cot.astype(jnp.float32) * mask,
    )
    text_back = branch_back_b(text_attn, text_packed, text_first, width, True, text_kept, text_a)
    text_res_grad, text_ctx_grad, text_ops, text_sums = text_back
    layout_res_grad, layout_ctx_grad, layout_ops, layout_sums = layout_back
    text_three_grad, layout_three_grad = attend_back(
        text_three, layout_three, length, log_total, text_ctx_grad, layout_ctx_grad
    )
    text_in_grad, text_rounded, text_query_bias, text_value_bias = project_back(
        text_attn, width, True, text_three_grad, text_res_grad
    )
    layout_in_grad, layout_rounded, layout_query_bias, layout_value_bias = project_back(
        layout_attn, narrow, False, layout_three_grad, layout_res_grad
    )
    hidden_low, active_low, first_low, second_low, inner_low = layout_ops
    three_w = jnp.einsum(
        "sd,jes->jde", layout_rows, layout_rounded, preferred_element_type=jnp.float32
    ).reshape(3 * narrow, narrow)
    out_w = jnp.einsum("sd,se->de", layout_ctx, first_low, preferred_element_type=jnp.float32)
    layout_attn_grad = jnp.concatenate([three_w, out_w], 0)
    layout_first_grad = jnp.einsum(
        "sd,sf->df", hidden_low, inner_low, preferred_element_type=jnp.float32
    )
    layout_second_grad = jnp.einsum(
        "sf,sd->fd", active_low, second_low, preferred_element_type=jnp.float32
    )
    layout_vec_grad = jnp.concatenate([layout_query_bias, layout_value_bias] + list(layout_sums))
    text_vec_grad = jnp.concatenate([text_query_bias, text_value_bias] + list(text_sums))
    small_terms = (
        text_vec_grad,
        layout_attn_grad,
        layout_first_grad,
        layout_second_grad,
        layout_vec_grad,
    )
    layout_low = (layout_out * mask).astype(jnp.bfloat16)
    grads = (text_in_grad, layout_in_grad)
    return (layout_low, grads, small_terms, text_rounded, text_ops[2])


def flat_rows(values):
    return values.reshape(-1, values.shape[-1])


AXES = ("dp", "shard")


def rows_for(size, width, aligned):
    rows = -(-size // width)
    if aligned:
        rows = -(-rows // 8) * 8
    return rows


def pack_rows(pieces, width, aligned):
    flat = jnp.concatenate([piece.reshape(-1) for piece in pieces])
    rows = rows_for(flat.shape[0], width, aligned)
    return jnp.pad(flat, (0, rows * width - flat.shape[0])).reshape(rows, width)


def unpack_small(flat, count, shapes):
    sizes = [rows * cols for rows, cols in shapes]
    offsets = [sum(sizes[:index]) for index in range(len(sizes))]
    parts = [flat[:, offset : offset + size] for offset, size in zip(offsets, sizes)]
    (attn_rows, attn_cols), (w1_rows, w1_cols), (w2_rows, w2_cols) = shapes[1:4]
    return (
        parts[0].reshape(-1),
        parts[1].reshape(count * attn_rows, attn_cols),
        parts[2].reshape(count, w1_rows, w1_cols).transpose(1, 0, 2).reshape(w1_rows, count * w1_cols),
        parts[3].reshape(count * w2_rows, w2_cols),
        parts[4].reshape(-1),
    )


def gather_weights(text_attn, text_w1, text_w2, text_vectors, layout_attn, layout_w1, layout_w2, layout_vectors):
    rows, width = text_attn.shape
    aligned = rows % 8 == 0
    small = (text_vectors, layout_attn, layout_w1, layout_w2, layout_vectors)
    small_rows = pack_rows(small, width, aligned)
    first = jnp.concatenate([text_attn, text_w1, small_rows], 0)
    first_all = lax.all_gather(first, AXES, axis=0, tiled=True)
    count = first_all.shape[0] // first.shape[0]
    first_all = first_all.reshape(count, first.shape[0], width)
    full_attn = first_all[:, :rows].reshape(count * rows, width)
    full_w1 = first_all[:, rows : 2 * rows].reshape(count * rows, width)
    small_flat = first_all[:, 2 * rows :].reshape(count, -1)
    shapes = [(1, text_vectors.shape[0]), layout_attn.shape, layout_w1.shape, layout_w2.shape, (1, layout_vectors.shape[0])]
    full_small = unpack_small(small_flat, count, shapes)
    full_w2 = lax.all_gather(text_w2, AXES, axis=0, tiled=True)
    return (full_attn, full_w1, full_w2) + full_small


def small_blocks(count, text_vec_grad, layout_attn_grad, layout_w1_grad, layout_w2_grad, layout_vec_grad):
    local_w1_cols = layout_w1_grad.shape[1] // count
    return (
        text_vec_grad.reshape(count, -1),
        layout_attn_grad.reshape(count, -1),
        layout_w1_grad.reshape(layout_w1_grad.shape[0], count, local_w1_cols)
        .transpose(1, 0, 2)
        .reshape(count, -1),
        layout_w2_grad.reshape(count, -1),
        layout_vec_grad.reshape(count, -1),
    )


def scatter_late(count, grad_attn, small_grads):
    width = grad_attn.shape[1]
    rows = grad_attn.shape[0] // count
    blocks = small_blocks(count, *small_grads)
    joined = jnp.concatenate(blocks, 1)
    size = joined.shape[1]
    small_rows = rows_for(size, width, rows % 8 == 0)
    joined = jnp.pad(joined, ((0, 0), (0, small_rows * width - size))).reshape(count, small_rows, width)
    packed = jnp.concatenate([grad_attn.reshape(count, rows, width), joined], 1)
    summed = lax.psum_scatter(
        packed.reshape(-1, width).astype(jnp.bfloat16), AXES, scatter_dimension=0, tiled=True
    ).astype(jnp.float32)
    attn_part = summed[:rows]
    flat = summed[rows:].reshape(-1)
    sizes = [block.shape[1] for block in blocks]
    offsets = [sum(sizes[:index]) for index in range(len(sizes))]
    parts = [flat[offset : offset + size] for offset, size in zip(offsets, sizes)]
    _, layout_attn_grad, layout_w1_grad, layout_w2_grad, _ = small_grads
    local_w1_cols = layout_w1_grad.shape[1] // count
    return (
        attn_part,
        parts[0],
        parts[1].reshape(layout_attn_grad.shape[0] // count, layout_attn_grad.shape[1]),
        parts[2].reshape(layout_w1_grad.shape[0], local_w1_cols),
        parts[3].reshape(layout_w2_grad.shape[0] // count, layout_w2_grad.shape[1]),
        parts[4],
    )


def pack_early(count, grad_first, grad_second):
    width = grad_first.shape[1]
    rows = grad_first.shape[0] // count
    packed = jnp.concatenate(
        [grad_first.reshape(count, rows, width), grad_second.reshape(count, rows, width)], 1
    )
    return packed.reshape(-1, width).astype(jnp.bfloat16)


def scatter_early(count, packed, second_shape):
    rows = packed.shape[0] // (2 * count)
    summed = lax.psum_scatter(packed, AXES, scatter_dimension=0, tiled=True).astype(jnp.float32)
    return (summed[:rows], summed[rows:].reshape(-1, second_shape[1]))


def body(
    text_in,
    layout_in,
    lengths,
    text_attn,
    text_w1,
    text_w2,
    text_vectors,
    layout_attn,
    layout_w1,
    layout_w2,
    layout_vectors,
    cot_text,
    cot_layout,
):
    count = lax.psum(1, AXES)
    weights = gather_weights(
        text_attn, text_w1, text_w2, text_vectors, layout_attn, layout_w1, layout_w2, layout_vectors
    )

    page_weights = (None,) * len(weights)
    out_text, kept_all = jax.vmap(page_forward, in_axes=(0, 0, 0, page_weights))(
        text_in, layout_in, lengths, weights
    )
    text_a = jax.vmap(page_back_ffn, in_axes=(0, 0, 0, page_weights))(
        lengths, kept_all, cot_text, weights
    )
    round_second, round_inner, text_hidden, text_active = text_a[1], text_a[3], text_a[4], text_a[5]
    early = (
        jnp.einsum("sd,sf->df", flat_rows(text_hidden), flat_rows(round_inner), preferred_element_type=jnp.float32),
        jnp.einsum("sf,sd->fd", flat_rows(text_active), flat_rows(round_second), preferred_element_type=jnp.float32),
    )
    packed = pack_early(count, *early)
    packed, text_a, kept_all = lax.optimization_barrier((packed, text_a, kept_all))
    grad_first, grad_second = scatter_early(count, packed, early[1].shape)
    out_layout, (text_grad, layout_grad), small_terms, text_rounded, text_first_low = jax.vmap(
        page_back_attn, in_axes=(0, 0, 0, 0, 0, 0, page_weights)
    )(text_in, layout_in, lengths, kept_all, text_a, cot_layout, weights)
    totals = tuple(jnp.sum(term, 0) for term in small_terms)
    three_part = jnp.einsum(
        "psd,pjes->dje", text_in, text_rounded, preferred_element_type=jnp.float32
    ).reshape(text_in.shape[2], -1)
    out_part = jnp.einsum(
        "sd,se->de", flat_rows(kept_all[2]), flat_rows(text_first_low), preferred_element_type=jnp.float32
    )
    summed = scatter_late(count, jnp.concatenate([three_part, out_part], 1), totals)
    return (
        out_text,
        out_layout,
        text_grad,
        layout_grad,
        summed[0],
        grad_first,
        grad_second,
        summed[1],
        summed[2],
        summed[3],
        summed[4],
        summed[5],
    )


def solution(mesh):
    placed = (
        P(("dp", "shard"), None, None),
        P(("dp", "shard"), None, None),
        P(("dp", "shard")),
        P(("dp", "shard"), None),
        P(("dp", "shard"), None),
        P(("dp", "shard"), None),
        P(("dp", "shard")),
        P(("dp", "shard"), None),
        P(None, ("dp", "shard")),
        P(("dp", "shard"), None),
        P(("dp", "shard")),
        P(("dp", "shard"), None, None),
        P(("dp", "shard"), None, None),
    )
    return jax.shard_map(
        body,
        mesh=mesh,
        in_specs=placed,
        out_specs=(
            P(("dp", "shard"), None, None),
            P(("dp", "shard"), None, None),
            P(("dp", "shard"), None, None),
            P(("dp", "shard"), None, None),
            P(("dp", "shard"), None),
            P(("dp", "shard"), None),
            P(("dp", "shard"), None),
            P(("dp", "shard")),
            P(("dp", "shard"), None),
            P(None, ("dp", "shard")),
            P(("dp", "shard"), None),
            P(("dp", "shard")),
        ),
        check_vma=False,
    )
```

```python
import functools

import jax
import jax.numpy as jnp
from jax import lax
from jax.experimental import pallas as pl
from jax.experimental.pallas import tpu as pltpu
from jax.sharding import PartitionSpec as P


H = 12
HD = 64
LHD = 16


EPS = 1e-05
NEG = -1000000000.0


def normalize(values, scale_row, shift_row):
    centered = values - jnp.mean(values, -1, keepdims=True)
    variance = jnp.mean(centered * centered, -1, keepdims=True)
    return centered * lax.rsqrt(variance + EPS) * scale_row + shift_row


def gelu_exact(values):
    return 0.5 * values * (1.0 + lax.erf(values * (0.5 ** 0.5)))


def vector_parts(packed, width):
    pieces = [packed[index * width : (index + 1) * width] for index in range(8)]
    return pieces + [packed[8 * width :]]


def block_of(attn, index, width, columns):
    if columns:
        return attn[:, index * width : (index + 1) * width]
    return attn[index * width : (index + 1) * width]


def project_three(inputs, attn, packed, width, columns):
    if columns:
        three = attn[:, 0 : 3 * width].reshape(width, 3, width)
        mixed = jnp.einsum("sd,dje->sje", inputs, three, preferred_element_type=jnp.float32)
    else:
        three = attn[0 : 3 * width].reshape(3, width, width)
        mixed = jnp.einsum("sd,jde->sje", inputs, three, preferred_element_type=jnp.float32)
    pieces = vector_parts(packed.astype(jnp.float32), width)
    offsets = jnp.stack([pieces[0], jnp.zeros_like(pieces[0]), pieces[1]])
    return (mixed + offsets[None]).astype(jnp.bfloat16)


def attend(text_three, layout_three, length):
    return attn_fwd_heads(
        jnp.reshape(length, (1,)).astype(jnp.int32),
        text_three.transpose(1, 2, 0),
        layout_three.transpose(1, 2, 0),
        (HD ** (-0.5), LHD ** (-0.5)),
    )


def _nn(a, b):
    return lax.dot_general(a, b, (((1,), (0,)), ((), ())), preferred_element_type=jnp.float32)


def _nt(a, b):
    return lax.dot_general(a, b, (((1,), (1,)), ((), ())), preferred_element_type=jnp.float32)


def attn_back_kernel(len_ref, text_ref, dc_ref, layout_ref, dcl_ref, lse_ref, text_out, layout_out, *, scales):
    text_scale, layout_scale = scales
    query, key, value = text_ref[0], text_ref[1], text_ref[2]
    query_l, key_l, value_l = layout_ref[0], layout_ref[1], layout_ref[2]
    scores = _nn(key.T, query) * text_scale + _nn(key_l.T, query_l) * layout_scale
    keys = lax.broadcasted_iota(jnp.int32, scores.shape, 0)
    scores = jnp.where(keys < len_ref[0], scores, NEG)
    probs = jnp.exp(scores - lse_ref[0])
    text_dp = _nn(value.T, dc_ref[...])
    layout_dp = _nn(value_l.T, dcl_ref[...])
    text_ds = probs * (text_dp - jnp.sum(probs * text_dp, 0, keepdims=True))
    layout_ds = probs * (layout_dp - jnp.sum(probs * layout_dp, 0, keepdims=True))
    text_g = text_ds.astype(jnp.bfloat16)
    joint_g = (text_ds + layout_ds).astype(jnp.bfloat16)
    weights = probs.astype(jnp.bfloat16)
    text_out[0] = (_nn(key, text_g) * text_scale).astype(text_out.dtype)
    text_out[1] = (_nt(query, text_g) * text_scale).astype(text_out.dtype)
    text_out[2] = _nt(dc_ref[...], weights).astype(text_out.dtype)
    layout_out[0] = (_nn(key_l, joint_g) * layout_scale).astype(layout_out.dtype)
    layout_out[1] = (_nt(query_l, joint_g) * layout_scale).astype(layout_out.dtype)
    layout_out[2] = _nt(dcl_ref[...], weights).astype(layout_out.dtype)


def attn_back_heads(length, text_t, dc_t, layout_t, dcl_t, lse, scales):
    parts, width, slots = text_t.shape
    narrow = layout_t.shape[1]
    wide, thin = width // H, narrow // H
    text_spec = pl.BlockSpec((parts, wide, slots), lambda h, n: (0, h, 0))
    layout_spec = pl.BlockSpec((parts, thin, slots), lambda h, n: (0, h, 0))
    flops = H * slots * slots * 2 * (4 * wide + 4 * thin)
    return pl.pallas_call(
        functools.partial(attn_back_kernel, scales=scales),
        grid_spec=pltpu.PrefetchScalarGridSpec(
            num_scalar_prefetch=1,
            grid=(H,),
            in_specs=[
                text_spec,
                pl.BlockSpec((wide, slots), lambda h, n: (h, 0)),
                layout_spec,
                pl.BlockSpec((thin, slots), lambda h, n: (h, 0)),
                pl.BlockSpec((1, 1, slots), lambda h, n: (h, 0, 0)),
            ],
            out_specs=[text_spec, layout_spec],
        ),
        out_shape=[
            jax.ShapeDtypeStruct(text_t.shape, jnp.bfloat16),
            jax.ShapeDtypeStruct(layout_t.shape, jnp.bfloat16),
        ],
        compiler_params=pltpu.CompilerParams(dimension_semantics=("arbitrary",)),
        cost_estimate=pl.CostEstimate(
            flops=flops,
            transcendentals=H * slots * slots,
            bytes_accessed=slots * (8 * width + 8 * narrow + 4 * H),
        ),
    )(length, text_t, dc_t, layout_t, dcl_t, lse)


def attn_fwd_kernel(len_ref, text_ref, layout_ref, ctx_out, ctxl_out, lse_out, *, scales):
    text_scale, layout_scale = scales
    query, key, value = text_ref[0], text_ref[1], text_ref[2]
    query_l, key_l, value_l = layout_ref[0], layout_ref[1], layout_ref[2]
    scores = _nn(key.T, query) * text_scale + _nn(key_l.T, query_l) * layout_scale
    keys = lax.broadcasted_iota(jnp.int32, scores.shape, 0)
    scores = jnp.where(keys < len_ref[0], scores, NEG)
    top = jnp.max(scores, 0, keepdims=True)
    exponent = jnp.exp(scores - top)
    total = jnp.sum(exponent, 0, keepdims=True)
    weights = (exponent / total).astype(jnp.bfloat16)
    ctx_out[...] = _nn(value, weights).astype(ctx_out.dtype)
    ctxl_out[...] = _nn(value_l, weights).astype(ctxl_out.dtype)
    lse_out[0] = top + jnp.log(total)


def attn_fwd_heads(length, text_t, layout_t, scales):
    parts, width, slots = text_t.shape
    narrow = layout_t.shape[1]
    wide, thin = width // H, narrow // H
    flops = H * slots * slots * 2 * (2 * wide + 2 * thin)
    return pl.pallas_call(
        functools.partial(attn_fwd_kernel, scales=scales),
        grid_spec=pltpu.PrefetchScalarGridSpec(
            num_scalar_prefetch=1,
            grid=(H,),
            in_specs=[
                pl.BlockSpec((parts, wide, slots), lambda h, n: (0, h, 0)),
                pl.BlockSpec((parts, thin, slots), lambda h, n: (0, h, 0)),
            ],
            out_specs=[
                pl.BlockSpec((wide, slots), lambda h, n: (h, 0)),
                pl.BlockSpec((thin, slots), lambda h, n: (h, 0)),
                pl.BlockSpec((1, 1, slots), lambda h, n: (h, 0, 0)),
            ],
        ),
        out_shape=[
            jax.ShapeDtypeStruct((width, slots), jnp.bfloat16),
            jax.ShapeDtypeStruct((narrow, slots), jnp.bfloat16),
            jax.ShapeDtypeStruct((H, 1, slots), jnp.float32),
        ],
        compiler_params=pltpu.CompilerParams(dimension_semantics=("arbitrary",)),
        cost_estimate=pl.CostEstimate(
            flops=flops,
            transcendentals=H * slots * slots,
            bytes_accessed=slots * (8 * width + 8 * narrow + 4 * H),
        ),
    )(length, text_t, layout_t)


def attend_back(text_three, layout_three, length, log_total, text_grad, layout_grad):
    return attn_back_heads(
        jnp.reshape(length, (1,)).astype(jnp.int32),
        text_three.transpose(1, 2, 0),
        text_grad.T,
        layout_three.transpose(1, 2, 0),
        layout_grad.T,
        log_total,
        (HD ** (-0.5), LHD ** (-0.5)),
    )


def project_back(attn, width, columns, grad_t, first_grad):
    if columns:
        three = attn[:, 0 : 3 * width].reshape(width, 3, width)
        input_grad = first_grad + jnp.einsum(
            "jes,dje->sd", grad_t, three, preferred_element_type=jnp.float32
        )
    else:
        three = attn[0 : 3 * width].reshape(3, width, width)
        input_grad = first_grad + jnp.einsum(
            "jes,jde->sd", grad_t, three, preferred_element_type=jnp.float32
        )
    column_sums = jnp.sum(grad_t.astype(jnp.float32), 2)
    return (input_grad, grad_t, column_sums[0], column_sums[2])


def branch_forward(inputs, context, attn, packed, first, second, width, columns):
    pieces = vector_parts(packed.astype(jnp.float32), width)
    out_block = block_of(attn, 3, width, columns)
    first_res = inputs.astype(jnp.float32) + (
        jnp.dot(context, out_block, preferred_element_type=jnp.float32) + pieces[2]
    )
    hidden = normalize(first_res, pieces[3], pieces[4])
    inner = (
        jnp.dot(hidden.astype(jnp.bfloat16), first, preferred_element_type=jnp.float32) + pieces[8]
    )
    activated = gelu_exact(inner).astype(jnp.bfloat16)
    second_res = hidden + (
        jnp.dot(activated, second, preferred_element_type=jnp.float32) + pieces[5]
    )
    result = normalize(second_res, pieces[6], pieces[7])
    return (result, (first_res, inner, second_res))


def branch_backward(attn, packed, first, second, width, columns, kept_rows, grad_out):
    first_res, inner, second_res = kept_rows
    pieces = vector_parts(packed.astype(jnp.float32), width)
    hidden, first_pull = jax.vjp(normalize, first_res, pieces[3], pieces[4])
    _, second_pull = jax.vjp(normalize, second_res, pieces[6], pieces[7])
    grad_second, late_scale, late_shift = second_pull(grad_out)
    round_second = grad_second.astype(jnp.bfloat16)
    activated, gelu_pull = jax.vjp(gelu_exact, inner)
    (grad_inner,) = gelu_pull(jnp.dot(round_second, second.T, preferred_element_type=jnp.float32))
    round_inner = grad_inner.astype(jnp.bfloat16)
    grad_hidden = grad_second + jnp.dot(round_inner, first.T, preferred_element_type=jnp.float32)
    grad_first, early_scale, early_shift = first_pull(grad_hidden)
    round_first = grad_first.astype(jnp.bfloat16)
    out_block = block_of(attn, 3, width, columns)
    grad_ctx = jnp.dot(round_first, out_block.T, preferred_element_type=jnp.float32).astype(
        jnp.bfloat16
    )
    operands = (
        hidden.astype(jnp.bfloat16),
        activated.astype(jnp.bfloat16),
        round_first,
        round_second,
        round_inner,
    )
    vector_sums = (
        jnp.sum(grad_first, 0),
        early_scale,
        early_shift,
        jnp.sum(grad_second, 0),
        late_scale,
        late_shift,
        jnp.sum(grad_inner, 0),
    )
    return (grad_first, grad_ctx, operands, vector_sums)


def branch_back_a(packed, second, width, kept_rows, grad_out):
    first_res, inner, second_res = kept_rows
    pieces = vector_parts(packed.astype(jnp.float32), width)
    hidden = normalize(first_res, pieces[3], pieces[4])
    _, second_pull = jax.vjp(normalize, second_res, pieces[6], pieces[7])
    grad_second, late_scale, late_shift = second_pull(grad_out)
    round_second = grad_second.astype(jnp.bfloat16)
    activated, gelu_pull = jax.vjp(gelu_exact, inner)
    (grad_inner,) = gelu_pull(jnp.dot(round_second, second.T, preferred_element_type=jnp.float32))
    round_inner = grad_inner.astype(jnp.bfloat16)
    return (
        grad_second,
        round_second,
        grad_inner,
        round_inner,
        hidden.astype(jnp.bfloat16),
        activated.astype(jnp.bfloat16),
        late_scale,
        late_shift,
    )


def branch_back_b(attn, packed, first, width, columns, kept_rows, part_a):
    first_res, _, _ = kept_rows
    grad_second, round_second, grad_inner, round_inner, hidden_low, active_low, late_scale, late_shift = part_a
    pieces = vector_parts(packed.astype(jnp.float32), width)
    _, first_pull = jax.vjp(normalize, first_res, pieces[3], pieces[4])
    grad_hidden = grad_second + jnp.dot(round_inner, first.T, preferred_element_type=jnp.float32)
    grad_first, early_scale, early_shift = first_pull(grad_hidden)
    round_first = grad_first.astype(jnp.bfloat16)
    out_block = block_of(attn, 3, width, columns)
    grad_ctx = jnp.dot(round_first, out_block.T, preferred_element_type=jnp.float32).astype(
        jnp.bfloat16
    )
    operands = (hidden_low, active_low, round_first, round_second, round_inner)
    vector_sums = (
        jnp.sum(grad_first, 0),
        early_scale,
        early_shift,
        jnp.sum(grad_second, 0),
        late_scale,
        late_shift,
        jnp.sum(grad_inner, 0),
    )
    return (grad_first, grad_ctx, operands, vector_sums)


def page_forward(text_rows, layout_rows, length, weights):
    (text_attn, text_first, text_second, text_packed, layout_attn, _, _, layout_packed) = weights
    width = text_rows.shape[1]
    narrow = layout_rows.shape[1]
    valid = jnp.arange(text_rows.shape[0], dtype=jnp.int32) < length
    text_three = project_three(text_rows, text_attn, text_packed, width, True)
    layout_three = project_three(layout_rows, layout_attn, layout_packed, narrow, False)
    text_ctx, layout_ctx, log_total = attend(text_three, layout_three, length)
    text_out, text_kept = branch_forward(
        text_rows, text_ctx.T, text_attn, text_packed, text_first, text_second, width, True
    )
    mask = valid[:, None].astype(jnp.float32)
    kept_page = (text_three, layout_three, text_ctx, layout_ctx, log_total, text_kept)
    return ((text_out * mask).astype(jnp.bfloat16), kept_page)


def page_back_ffn(length, kept_page, text_cot, weights):
    text_attn, _, text_second, text_packed = weights[:4]
    text_kept = kept_page[5]
    width = text_attn.shape[0]
    slots = text_cot.shape[0]
    valid = jnp.arange(slots, dtype=jnp.int32) < length
    mask = valid[:, None].astype(jnp.float32)
    return branch_back_a(
        text_packed, text_second, width, text_kept, text_cot.astype(jnp.float32) * mask
    )


def page_back_attn(text_rows, layout_rows, length, kept_page, text_a, layout_cot, weights):
    (
        text_attn,
        text_first,
        _,
        text_packed,
        layout_attn,
        layout_first,
        layout_second,
        layout_packed,
    ) = weights
    text_three, layout_three, _, layout_ctx, log_total, text_kept = kept_page
    width = text_rows.shape[1]
    narrow = layout_rows.shape[1]
    slots = text_rows.shape[0]
    valid = jnp.arange(slots, dtype=jnp.int32) < length
    mask = valid[:, None].astype(jnp.float32)
    layout_out, layout_kept = branch_forward(
        layout_rows,
        layout_ctx.T,
        layout_attn,
        layout_packed,
        layout_first,
        layout_second,
        narrow,
        False,
    )
    layout_back = branch_backward(
        layout_attn,
        layout_packed,
        layout_first,
        layout_second,
        narrow,
        False,
        layout_kept,
        layout_cot.astype(jnp.float32) * mask,
    )
    text_back = branch_back_b(text_attn, text_packed, text_first, width, True, text_kept, text_a)
    text_res_grad, text_ctx_grad, text_ops, text_sums = text_back
    layout_res_grad, layout_ctx_grad, layout_ops, layout_sums = layout_back
    text_three_grad, layout_three_grad = attend_back(
        text_three, layout_three, length, log_total, text_ctx_grad, layout_ctx_grad
    )
    text_in_grad, text_rounded, text_query_bias, text_value_bias = project_back(
        text_attn, width, True, text_three_grad, text_res_grad
    )
    layout_in_grad, layout_rounded, layout_query_bias, layout_value_bias = project_back(
        layout_attn, narrow, False, layout_three_grad, layout_res_grad
    )
    hidden_low, active_low, first_low, second_low, inner_low = layout_ops
    three_w = jnp.einsum(
        "sd,jes->jde", layout_rows, layout_rounded, preferred_element_type=jnp.float32
    ).reshape(3 * narrow, narrow)
    out_w = jnp.einsum("ds,se->de", layout_ctx, first_low, preferred_element_type=jnp.float32)
    layout_attn_grad = jnp.concatenate([three_w, out_w], 0)
    layout_first_grad = jnp.einsum(
        "sd,sf->df", hidden_low, inner_low, preferred_element_type=jnp.float32
    )
    layout_second_grad = jnp.einsum(
        "sf,sd->fd", active_low, second_low, preferred_element_type=jnp.float32
    )
    layout_vec_grad = jnp.concatenate([layout_query_bias, layout_value_bias] + list(layout_sums))
    text_vec_grad = jnp.concatenate([text_query_bias, text_value_bias] + list(text_sums))
    small_terms = (
        text_vec_grad,
        layout_attn_grad,
        layout_first_grad,
        layout_second_grad,
        layout_vec_grad,
    )
    layout_low = (layout_out * mask).astype(jnp.bfloat16)
    grads = (text_in_grad, layout_in_grad)
    return (layout_low, grads, small_terms, text_rounded, text_ops[2])


def flat_rows(values):
    return values.reshape(-1, values.shape[-1])


AXES = ("dp", "shard")


def rows_for(size, width, aligned):
    rows = -(-size // width)
    if aligned:
        rows = -(-rows // 8) * 8
    return rows


def pack_rows(pieces, width, aligned):
    flat = jnp.concatenate([piece.reshape(-1) for piece in pieces])
    rows = rows_for(flat.shape[0], width, aligned)
    return jnp.pad(flat, (0, rows * width - flat.shape[0])).reshape(rows, width)


def unpack_small(flat, count, shapes):
    sizes = [rows * cols for rows, cols in shapes]
    offsets = [sum(sizes[:index]) for index in range(len(sizes))]
    parts = [flat[:, offset : offset + size] for offset, size in zip(offsets, sizes)]
    (attn_rows, attn_cols), (w1_rows, w1_cols), (w2_rows, w2_cols) = shapes[1:4]
    return (
        parts[0].reshape(-1),
        parts[1].reshape(count * attn_rows, attn_cols),
        parts[2].reshape(count, w1_rows, w1_cols).transpose(1, 0, 2).reshape(w1_rows, count * w1_cols),
        parts[3].reshape(count * w2_rows, w2_cols),
        parts[4].reshape(-1),
    )


def gather_weights(text_attn, text_w1, text_w2, text_vectors, layout_attn, layout_w1, layout_w2, layout_vectors):
    rows, width = text_attn.shape
    aligned = rows % 8 == 0
    small = (text_vectors, layout_attn, layout_w1, layout_w2, layout_vectors)
    small_rows = pack_rows(small, width, aligned)
    first = jnp.concatenate([text_attn, text_w1, small_rows], 0)
    first_all = lax.all_gather(first, AXES, axis=0, tiled=True)
    count = first_all.shape[0] // first.shape[0]
    first_all = first_all.reshape(count, first.shape[0], width)
    full_attn = first_all[:, :rows].reshape(count * rows, width)
    full_w1 = first_all[:, rows : 2 * rows].reshape(count * rows, width)
    small_flat = first_all[:, 2 * rows :].reshape(count, -1)
    shapes = [(1, text_vectors.shape[0]), layout_attn.shape, layout_w1.shape, layout_w2.shape, (1, layout_vectors.shape[0])]
    full_small = unpack_small(small_flat, count, shapes)
    full_w2 = lax.all_gather(text_w2, AXES, axis=0, tiled=True)
    return (full_attn, full_w1, full_w2) + full_small


def small_blocks(count, text_vec_grad, layout_attn_grad, layout_w1_grad, layout_w2_grad, layout_vec_grad):
    local_w1_cols = layout_w1_grad.shape[1] // count
    return (
        text_vec_grad.reshape(count, -1),
        layout_attn_grad.reshape(count, -1),
        layout_w1_grad.reshape(layout_w1_grad.shape[0], count, local_w1_cols)
        .transpose(1, 0, 2)
        .reshape(count, -1),
        layout_w2_grad.reshape(count, -1),
        layout_vec_grad.reshape(count, -1),
    )


def scatter_late(count, grad_attn, small_grads):
    width = grad_attn.shape[1]
    rows = grad_attn.shape[0] // count
    blocks = small_blocks(count, *small_grads)
    joined = jnp.concatenate(blocks, 1)
    size = joined.shape[1]
    small_rows = rows_for(size, width, rows % 8 == 0)
    joined = jnp.pad(joined, ((0, 0), (0, small_rows * width - size))).reshape(count, small_rows, width)
    packed = jnp.concatenate([grad_attn.reshape(count, rows, width), joined], 1)
    summed = lax.psum_scatter(
        packed.reshape(-1, width).astype(jnp.bfloat16), AXES, scatter_dimension=0, tiled=True
    ).astype(jnp.float32)
    attn_part = summed[:rows]
    flat = summed[rows:].reshape(-1)
    sizes = [block.shape[1] for block in blocks]
    offsets = [sum(sizes[:index]) for index in range(len(sizes))]
    parts = [flat[offset : offset + size] for offset, size in zip(offsets, sizes)]
    _, layout_attn_grad, layout_w1_grad, layout_w2_grad, _ = small_grads
    local_w1_cols = layout_w1_grad.shape[1] // count
    return (
        attn_part,
        parts[0],
        parts[1].reshape(layout_attn_grad.shape[0] // count, layout_attn_grad.shape[1]),
        parts[2].reshape(layout_w1_grad.shape[0], local_w1_cols),
        parts[3].reshape(layout_w2_grad.shape[0] // count, layout_w2_grad.shape[1]),
        parts[4],
    )


def pack_early(count, grad_first, grad_second):
    width = grad_first.shape[1]
    rows = grad_first.shape[0] // count
    packed = jnp.concatenate(
        [grad_first.reshape(count, rows, width), grad_second.reshape(count, rows, width)], 1
    )
    return packed.reshape(-1, width).astype(jnp.bfloat16)


def scatter_early(count, packed, second_shape):
    rows = packed.shape[0] // (2 * count)
    summed = lax.psum_scatter(packed, AXES, scatter_dimension=0, tiled=True).astype(jnp.float32)
    return (summed[:rows], summed[rows:].reshape(-1, second_shape[1]))


def body(
    text_in,
    layout_in,
    lengths,
    text_attn,
    text_w1,
    text_w2,
    text_vectors,
    layout_attn,
    layout_w1,
    layout_w2,
    layout_vectors,
    cot_text,
    cot_layout,
):
    count = lax.psum(1, AXES)
    weights = gather_weights(
        text_attn, text_w1, text_w2, text_vectors, layout_attn, layout_w1, layout_w2, layout_vectors
    )

    page_weights = (None,) * len(weights)
    out_text, kept_all = jax.vmap(page_forward, in_axes=(0, 0, 0, page_weights))(
        text_in, layout_in, lengths, weights
    )
    text_a = jax.vmap(page_back_ffn, in_axes=(0, 0, 0, page_weights))(
        lengths, kept_all, cot_text, weights
    )
    round_second, round_inner, text_hidden, text_active = text_a[1], text_a[3], text_a[4], text_a[5]
    early = (
        jnp.einsum("sd,sf->df", flat_rows(text_hidden), flat_rows(round_inner), preferred_element_type=jnp.float32),
        jnp.einsum("sf,sd->fd", flat_rows(text_active), flat_rows(round_second), preferred_element_type=jnp.float32),
    )
    packed = pack_early(count, *early)
    packed, text_a, kept_all = lax.optimization_barrier((packed, text_a, kept_all))
    grad_first, grad_second = scatter_early(count, packed, early[1].shape)
    out_layout, (text_grad, layout_grad), small_terms, text_rounded, text_first_low = jax.vmap(
        page_back_attn, in_axes=(0, 0, 0, 0, 0, 0, page_weights)
    )(text_in, layout_in, lengths, kept_all, text_a, cot_layout, weights)
    totals = tuple(jnp.sum(term, 0) for term in small_terms)
    three_part = jnp.einsum(
        "psd,pjes->dje", text_in, text_rounded, preferred_element_type=jnp.float32
    ).reshape(text_in.shape[2], -1)
    out_part = jnp.einsum(
        "pds,pse->de", kept_all[2], text_first_low, preferred_element_type=jnp.float32
    )
    summed = scatter_late(count, jnp.concatenate([three_part, out_part], 1), totals)
    return (
        out_text,
        out_layout,
        text_grad,
        layout_grad,
        summed[0],
        grad_first,
        grad_second,
        summed[1],
        summed[2],
        summed[3],
        summed[4],
        summed[5],
    )


def solution(mesh):
    placed = (
        P(("dp", "shard"), None, None),
        P(("dp", "shard"), None, None),
        P(("dp", "shard")),
        P(("dp", "shard"), None),
        P(("dp", "shard"), None),
        P(("dp", "shard"), None),
        P(("dp", "shard")),
        P(("dp", "shard"), None),
        P(None, ("dp", "shard")),
        P(("dp", "shard"), None),
        P(("dp", "shard")),
        P(("dp", "shard"), None, None),
        P(("dp", "shard"), None, None),
    )
    return jax.shard_map(
        body,
        mesh=mesh,
        in_specs=placed,
        out_specs=(
            P(("dp", "shard"), None, None),
            P(("dp", "shard"), None, None),
            P(("dp", "shard"), None, None),
            P(("dp", "shard"), None, None),
            P(("dp", "shard"), None),
            P(("dp", "shard"), None),
            P(("dp", "shard"), None),
            P(("dp", "shard")),
            P(("dp", "shard"), None),
            P(None, ("dp", "shard")),
            P(("dp", "shard"), None),
            P(("dp", "shard")),
        ),
        check_vma=False,
    )
```

```python
import functools

import jax
import jax.numpy as jnp
from jax import lax
from jax.experimental import pallas as pl
from jax.experimental.pallas import tpu as pltpu
from jax.sharding import PartitionSpec as P


H = 12
HD = 64
LHD = 16


EPS = 1e-05
NEG = -1000000000.0


def normalize(values, scale_row, shift_row):
    centered = values - jnp.mean(values, -1, keepdims=True)
    variance = jnp.mean(centered * centered, -1, keepdims=True)
    return centered * lax.rsqrt(variance + EPS) * scale_row + shift_row


def gelu_exact(values):
    return 0.5 * values * (1.0 + lax.erf(values * (0.5 ** 0.5)))


def vector_parts(packed, width):
    pieces = [packed[index * width : (index + 1) * width] for index in range(8)]
    return pieces + [packed[8 * width :]]


def block_of(attn, index, width, columns):
    if columns:
        return attn[:, index * width : (index + 1) * width]
    return attn[index * width : (index + 1) * width]


def project_three(inputs, attn, packed, width, columns):
    if columns:
        three = attn[:, 0 : 3 * width].reshape(width, 3, width)
        mixed = jnp.einsum("sd,dje->sje", inputs, three, preferred_element_type=jnp.float32)
    else:
        three = attn[0 : 3 * width].reshape(3, width, width)
        mixed = jnp.einsum("sd,jde->sje", inputs, three, preferred_element_type=jnp.float32)
    pieces = vector_parts(packed.astype(jnp.float32), width)
    offsets = jnp.stack([pieces[0], jnp.zeros_like(pieces[0]), pieces[1]])
    return (mixed + offsets[None]).astype(jnp.bfloat16)


def attend(text_three, layout_three, length):
    return attn_fwd_heads(
        jnp.reshape(length, (1,)).astype(jnp.int32),
        text_three.transpose(1, 2, 0),
        layout_three.transpose(1, 2, 0),
        (HD ** (-0.5), LHD ** (-0.5)),
    )


def _nn(a, b):
    return lax.dot_general(a, b, (((1,), (0,)), ((), ())), preferred_element_type=jnp.float32)


def _nt(a, b):
    return lax.dot_general(a, b, (((1,), (1,)), ((), ())), preferred_element_type=jnp.float32)


def attn_back_kernel(len_ref, text_ref, dc_ref, layout_ref, dcl_ref, lse_ref, text_out, layout_out, *, scales):
    text_scale, layout_scale = scales
    query, key, value = text_ref[0], text_ref[1], text_ref[2]
    query_l, key_l, value_l = layout_ref[0], layout_ref[1], layout_ref[2]
    scores = _nn(key.T, query) * text_scale + _nn(key_l.T, query_l) * layout_scale
    keys = lax.broadcasted_iota(jnp.int32, scores.shape, 0)
    scores = jnp.where(keys < len_ref[0], scores, NEG)
    probs = jnp.exp(scores - lse_ref[0])
    text_dp = _nn(value.T, dc_ref[...])
    layout_dp = _nn(value_l.T, dcl_ref[...])
    text_ds = probs * (text_dp - jnp.sum(probs * text_dp, 0, keepdims=True))
    layout_ds = probs * (layout_dp - jnp.sum(probs * layout_dp, 0, keepdims=True))
    text_g = text_ds.astype(jnp.bfloat16)
    joint_g = (text_ds + layout_ds).astype(jnp.bfloat16)
    weights = probs.astype(jnp.bfloat16)
    text_out[0] = (_nn(key, text_g) * text_scale).astype(text_out.dtype)
    text_out[1] = (_nt(query, text_g) * text_scale).astype(text_out.dtype)
    text_out[2] = _nt(dc_ref[...], weights).astype(text_out.dtype)
    layout_out[0] = (_nn(key_l, joint_g) * layout_scale).astype(layout_out.dtype)
    layout_out[1] = (_nt(query_l, joint_g) * layout_scale).astype(layout_out.dtype)
    layout_out[2] = _nt(dcl_ref[...], weights).astype(layout_out.dtype)


def attn_back_heads(length, text_t, dc_t, layout_t, dcl_t, lse, scales):
    parts, width, slots = text_t.shape
    narrow = layout_t.shape[1]
    wide, thin = width // H, narrow // H
    text_spec = pl.BlockSpec((parts, wide, slots), lambda h, n: (0, h, 0))
    layout_spec = pl.BlockSpec((parts, thin, slots), lambda h, n: (0, h, 0))
    flops = H * slots * slots * 2 * (4 * wide + 4 * thin)
    return pl.pallas_call(
        functools.partial(attn_back_kernel, scales=scales),
        grid_spec=pltpu.PrefetchScalarGridSpec(
            num_scalar_prefetch=1,
            grid=(H,),
            in_specs=[
                text_spec,
                pl.BlockSpec((wide, slots), lambda h, n: (h, 0)),
                layout_spec,
                pl.BlockSpec((thin, slots), lambda h, n: (h, 0)),
                pl.BlockSpec((1, 1, slots), lambda h, n: (h, 0, 0)),
            ],
            out_specs=[text_spec, layout_spec],
        ),
        out_shape=[
            jax.ShapeDtypeStruct(text_t.shape, jnp.bfloat16),
            jax.ShapeDtypeStruct(layout_t.shape, jnp.bfloat16),
        ],
        compiler_params=pltpu.CompilerParams(dimension_semantics=("arbitrary",)),
        cost_estimate=pl.CostEstimate(
            flops=flops,
            transcendentals=H * slots * slots,
            bytes_accessed=slots * (8 * width + 8 * narrow + 4 * H),
        ),
    )(length, text_t, dc_t, layout_t, dcl_t, lse)


def attn_fwd_kernel(len_ref, text_ref, layout_ref, ctx_out, ctxl_out, lse_out, *, scales):
    text_scale, layout_scale = scales
    query, key, value = text_ref[0], text_ref[1], text_ref[2]
    query_l, key_l, value_l = layout_ref[0], layout_ref[1], layout_ref[2]
    scores = _nn(key.T, query) * text_scale + _nn(key_l.T, query_l) * layout_scale
    keys = lax.broadcasted_iota(jnp.int32, scores.shape, 0)
    scores = jnp.where(keys < len_ref[0], scores, NEG)
    top = jnp.max(scores, 0, keepdims=True)
    exponent = jnp.exp(scores - top)
    total = jnp.sum(exponent, 0, keepdims=True)
    weights = (exponent / total).astype(jnp.bfloat16)
    ctx_out[...] = _nn(value, weights).astype(ctx_out.dtype)
    ctxl_out[...] = _nn(value_l, weights).astype(ctxl_out.dtype)
    lse_out[0] = top + jnp.log(total)


def attn_fwd_heads(length, text_t, layout_t, scales):
    parts, width, slots = text_t.shape
    narrow = layout_t.shape[1]
    wide, thin = width // H, narrow // H
    flops = H * slots * slots * 2 * (2 * wide + 2 * thin)
    return pl.pallas_call(
        functools.partial(attn_fwd_kernel, scales=scales),
        grid_spec=pltpu.PrefetchScalarGridSpec(
            num_scalar_prefetch=1,
            grid=(H,),
            in_specs=[
                pl.BlockSpec((parts, wide, slots), lambda h, n: (0, h, 0)),
                pl.BlockSpec((parts, thin, slots), lambda h, n: (0, h, 0)),
            ],
            out_specs=[
                pl.BlockSpec((wide, slots), lambda h, n: (h, 0)),
                pl.BlockSpec((thin, slots), lambda h, n: (h, 0)),
                pl.BlockSpec((1, 1, slots), lambda h, n: (h, 0, 0)),
            ],
        ),
        out_shape=[
            jax.ShapeDtypeStruct((width, slots), jnp.bfloat16),
            jax.ShapeDtypeStruct((narrow, slots), jnp.bfloat16),
            jax.ShapeDtypeStruct((H, 1, slots), jnp.float32),
        ],
        compiler_params=pltpu.CompilerParams(dimension_semantics=("arbitrary",)),
        cost_estimate=pl.CostEstimate(
            flops=flops,
            transcendentals=H * slots * slots,
            bytes_accessed=slots * (8 * width + 8 * narrow + 4 * H),
        ),
    )(length, text_t, layout_t)


def attend_back(text_three, layout_three, length, log_total, text_grad, layout_grad):
    return attn_back_heads(
        jnp.reshape(length, (1,)).astype(jnp.int32),
        text_three.transpose(1, 2, 0),
        text_grad.T,
        layout_three.transpose(1, 2, 0),
        layout_grad.T,
        log_total,
        (HD ** (-0.5), LHD ** (-0.5)),
    )


def project_back(attn, width, columns, grad_t, first_grad):
    if columns:
        three = attn[:, 0 : 3 * width].reshape(width, 3, width)
        input_grad = first_grad + jnp.einsum(
            "jes,dje->sd", grad_t, three, preferred_element_type=jnp.float32
        )
    else:
        three = attn[0 : 3 * width].reshape(3, width, width)
        input_grad = first_grad + jnp.einsum(
            "jes,jde->sd", grad_t, three, preferred_element_type=jnp.float32
        )
    column_sums = jnp.sum(grad_t.astype(jnp.float32), 2)
    return (input_grad, grad_t, column_sums[0], column_sums[2])


def branch_forward(inputs, context, attn, packed, first, second, width, columns):
    pieces = vector_parts(packed.astype(jnp.float32), width)
    out_block = block_of(attn, 3, width, columns)
    first_res = inputs.astype(jnp.float32) + (
        jnp.dot(context, out_block, preferred_element_type=jnp.float32) + pieces[2]
    )
    hidden = normalize(first_res, pieces[3], pieces[4])
    inner = (
        jnp.dot(hidden.astype(jnp.bfloat16), first, preferred_element_type=jnp.float32) + pieces[8]
    )
    activated = gelu_exact(inner).astype(jnp.bfloat16)
    second_res = hidden + (
        jnp.dot(activated, second, preferred_element_type=jnp.float32) + pieces[5]
    )
    result = normalize(second_res, pieces[6], pieces[7])
    return (result, (first_res, inner, second_res))


def branch_backward(attn, packed, first, second, width, columns, kept_rows, grad_out):
    first_res, inner, second_res = kept_rows
    pieces = vector_parts(packed.astype(jnp.float32), width)
    hidden, first_pull = jax.vjp(normalize, first_res, pieces[3], pieces[4])
    _, second_pull = jax.vjp(normalize, second_res, pieces[6], pieces[7])
    grad_second, late_scale, late_shift = second_pull(grad_out)
    round_second = grad_second.astype(jnp.bfloat16)
    activated, gelu_pull = jax.vjp(gelu_exact, inner)
    (grad_inner,) = gelu_pull(jnp.dot(round_second, second.T, preferred_element_type=jnp.float32))
    round_inner = grad_inner.astype(jnp.bfloat16)
    grad_hidden = grad_second + jnp.dot(round_inner, first.T, preferred_element_type=jnp.float32)
    grad_first, early_scale, early_shift = first_pull(grad_hidden)
    round_first = grad_first.astype(jnp.bfloat16)
    out_block = block_of(attn, 3, width, columns)
    grad_ctx = jnp.dot(round_first, out_block.T, preferred_element_type=jnp.float32).astype(
        jnp.bfloat16
    )
    operands = (
        hidden.astype(jnp.bfloat16),
        activated.astype(jnp.bfloat16),
        round_first,
        round_second,
        round_inner,
    )
    vector_sums = (
        jnp.sum(grad_first, 0),
        early_scale,
        early_shift,
        jnp.sum(grad_second, 0),
        late_scale,
        late_shift,
        jnp.sum(grad_inner, 0),
    )
    return (grad_first, grad_ctx, operands, vector_sums)


def branch_back_a(packed, width, kept_rows, grad_out):
    first_res, inner, second_res = kept_rows
    pieces = vector_parts(packed.astype(jnp.float32), width)
    hidden = normalize(first_res, pieces[3], pieces[4])
    _, second_pull = jax.vjp(normalize, second_res, pieces[6], pieces[7])
    grad_second, late_scale, late_shift = second_pull(grad_out)
    round_second = grad_second.astype(jnp.bfloat16)
    return (
        grad_second,
        round_second,
        hidden.astype(jnp.bfloat16),
        gelu_exact(inner).astype(jnp.bfloat16),
        late_scale,
        late_shift,
    )


def branch_back_b(attn, packed, first, second, width, columns, kept_rows, part_a):
    first_res, inner, _ = kept_rows
    grad_second, round_second, hidden_low, active_low, late_scale, late_shift = part_a
    _, gelu_pull = jax.vjp(gelu_exact, inner)
    (grad_inner,) = gelu_pull(jnp.dot(round_second, second.T, preferred_element_type=jnp.float32))
    round_inner = grad_inner.astype(jnp.bfloat16)
    pieces = vector_parts(packed.astype(jnp.float32), width)
    _, first_pull = jax.vjp(normalize, first_res, pieces[3], pieces[4])
    grad_hidden = grad_second + jnp.dot(round_inner, first.T, preferred_element_type=jnp.float32)
    grad_first, early_scale, early_shift = first_pull(grad_hidden)
    round_first = grad_first.astype(jnp.bfloat16)
    out_block = block_of(attn, 3, width, columns)
    grad_ctx = jnp.dot(round_first, out_block.T, preferred_element_type=jnp.float32).astype(
        jnp.bfloat16
    )
    operands = (hidden_low, active_low, round_first, round_second, round_inner)
    vector_sums = (
        jnp.sum(grad_first, 0),
        early_scale,
        early_shift,
        jnp.sum(grad_second, 0),
        late_scale,
        late_shift,
        jnp.sum(grad_inner, 0),
    )
    return (grad_first, grad_ctx, operands, vector_sums)


def page_forward(text_rows, layout_rows, length, weights):
    (text_attn, text_first, text_second, text_packed, layout_attn, _, _, layout_packed) = weights
    width = text_rows.shape[1]
    narrow = layout_rows.shape[1]
    valid = jnp.arange(text_rows.shape[0], dtype=jnp.int32) < length
    text_three = project_three(text_rows, text_attn, text_packed, width, True)
    layout_three = project_three(layout_rows, layout_attn, layout_packed, narrow, False)
    text_ctx, layout_ctx, log_total = attend(text_three, layout_three, length)
    text_out, text_kept = branch_forward(
        text_rows, text_ctx.T, text_attn, text_packed, text_first, text_second, width, True
    )
    mask = valid[:, None].astype(jnp.float32)
    kept_page = (text_three, layout_three, text_ctx, layout_ctx, log_total, text_kept)
    return ((text_out * mask).astype(jnp.bfloat16), kept_page)


def page_back_ffn(length, kept_page, text_cot, weights):
    text_attn, _, _, text_packed = weights[:4]
    text_kept = kept_page[5]
    width = text_attn.shape[0]
    slots = text_cot.shape[0]
    valid = jnp.arange(slots, dtype=jnp.int32) < length
    mask = valid[:, None].astype(jnp.float32)
    return branch_back_a(text_packed, width, text_kept, text_cot.astype(jnp.float32) * mask)


def page_back_attn(text_rows, layout_rows, length, kept_page, text_a, layout_cot, weights):
    (
        text_attn,
        text_first,
        text_second,
        text_packed,
        layout_attn,
        layout_first,
        layout_second,
        layout_packed,
    ) = weights
    text_three, layout_three, _, layout_ctx, log_total, text_kept = kept_page
    width = text_rows.shape[1]
    narrow = layout_rows.shape[1]
    slots = text_rows.shape[0]
    valid = jnp.arange(slots, dtype=jnp.int32) < length
    mask = valid[:, None].astype(jnp.float32)
    layout_out, layout_kept = branch_forward(
        layout_rows,
        layout_ctx.T,
        layout_attn,
        layout_packed,
        layout_first,
        layout_second,
        narrow,
        False,
    )
    layout_back = branch_backward(
        layout_attn,
        layout_packed,
        layout_first,
        layout_second,
        narrow,
        False,
        layout_kept,
        layout_cot.astype(jnp.float32) * mask,
    )
    text_back = branch_back_b(
        text_attn, text_packed, text_first, text_second, width, True, text_kept, text_a
    )
    text_res_grad, text_ctx_grad, text_ops, text_sums = text_back
    layout_res_grad, layout_ctx_grad, layout_ops, layout_sums = layout_back
    text_three_grad, layout_three_grad = attend_back(
        text_three, layout_three, length, log_total, text_ctx_grad, layout_ctx_grad
    )
    text_in_grad, text_rounded, text_query_bias, text_value_bias = project_back(
        text_attn, width, True, text_three_grad, text_res_grad
    )
    layout_in_grad, layout_rounded, layout_query_bias, layout_value_bias = project_back(
        layout_attn, narrow, False, layout_three_grad, layout_res_grad
    )
    hidden_low, active_low, first_low, second_low, inner_low = layout_ops
    three_w = jnp.einsum(
        "sd,jes->jde", layout_rows, layout_rounded, preferred_element_type=jnp.float32
    ).reshape(3 * narrow, narrow)
    out_w = jnp.einsum("ds,se->de", layout_ctx, first_low, preferred_element_type=jnp.float32)
    layout_attn_grad = jnp.concatenate([three_w, out_w], 0)
    layout_first_grad = jnp.einsum(
        "sd,sf->df", hidden_low, inner_low, preferred_element_type=jnp.float32
    )
    layout_second_grad = jnp.einsum(
        "sf,sd->fd", active_low, second_low, preferred_element_type=jnp.float32
    )
    layout_vec_grad = jnp.concatenate([layout_query_bias, layout_value_bias] + list(layout_sums))
    text_vec_grad = jnp.concatenate([text_query_bias, text_value_bias] + list(text_sums))
    small_terms = (
        text_vec_grad,
        layout_attn_grad,
        layout_first_grad,
        layout_second_grad,
        layout_vec_grad,
    )
    layout_low = (layout_out * mask).astype(jnp.bfloat16)
    grads = (text_in_grad, layout_in_grad)
    return (layout_low, grads, small_terms, text_rounded, text_ops[2], text_ops[4])


def flat_rows(values):
    return values.reshape(-1, values.shape[-1])


AXES = ("dp", "shard")


def rows_for(size, width, aligned):
    rows = -(-size // width)
    if aligned:
        rows = -(-rows // 8) * 8
    return rows


def pack_rows(pieces, width, aligned):
    flat = jnp.concatenate([piece.reshape(-1) for piece in pieces])
    rows = rows_for(flat.shape[0], width, aligned)
    return jnp.pad(flat, (0, rows * width - flat.shape[0])).reshape(rows, width)


def unpack_small(flat, count, shapes):
    sizes = [rows * cols for rows, cols in shapes]
    offsets = [sum(sizes[:index]) for index in range(len(sizes))]
    parts = [flat[:, offset : offset + size] for offset, size in zip(offsets, sizes)]
    (attn_rows, attn_cols), (w1_rows, w1_cols), (w2_rows, w2_cols) = shapes[1:4]
    return (
        parts[0].reshape(-1),
        parts[1].reshape(count * attn_rows, attn_cols),
        parts[2].reshape(count, w1_rows, w1_cols).transpose(1, 0, 2).reshape(w1_rows, count * w1_cols),
        parts[3].reshape(count * w2_rows, w2_cols),
        parts[4].reshape(-1),
    )


def gather_weights(text_attn, text_w1, text_w2, text_vectors, layout_attn, layout_w1, layout_w2, layout_vectors):
    rows, width = text_attn.shape
    aligned = rows % 8 == 0
    small = (text_vectors, layout_attn, layout_w1, layout_w2, layout_vectors)
    small_rows = pack_rows(small, width, aligned)
    first = jnp.concatenate([text_attn, text_w1, small_rows], 0)
    first_all = lax.all_gather(first, AXES, axis=0, tiled=True)
    count = first_all.shape[0] // first.shape[0]
    first_all = first_all.reshape(count, first.shape[0], width)
    full_attn = first_all[:, :rows].reshape(count * rows, width)
    full_w1 = first_all[:, rows : 2 * rows].reshape(count * rows, width)
    small_flat = first_all[:, 2 * rows :].reshape(count, -1)
    shapes = [(1, text_vectors.shape[0]), layout_attn.shape, layout_w1.shape, layout_w2.shape, (1, layout_vectors.shape[0])]
    full_small = unpack_small(small_flat, count, shapes)
    full_w2 = lax.all_gather(text_w2, AXES, axis=0, tiled=True)
    return (full_attn, full_w1, full_w2) + full_small


def small_blocks(count, text_vec_grad, layout_attn_grad, layout_w1_grad, layout_w2_grad, layout_vec_grad):
    local_w1_cols = layout_w1_grad.shape[1] // count
    return (
        text_vec_grad.reshape(count, -1),
        layout_attn_grad.reshape(count, -1),
        layout_w1_grad.reshape(layout_w1_grad.shape[0], count, local_w1_cols)
        .transpose(1, 0, 2)
        .reshape(count, -1),
        layout_w2_grad.reshape(count, -1),
        layout_vec_grad.reshape(count, -1),
    )


def scatter_late(count, grad_attn, grad_first, small_grads):
    width = grad_attn.shape[1]
    rows = grad_attn.shape[0] // count
    blocks = small_blocks(count, *small_grads)
    joined = jnp.concatenate(blocks, 1)
    size = joined.shape[1]
    small_rows = rows_for(size, width, rows % 8 == 0)
    joined = jnp.pad(joined, ((0, 0), (0, small_rows * width - size))).reshape(count, small_rows, width)
    packed = jnp.concatenate(
        [grad_attn.reshape(count, rows, width), grad_first.reshape(count, rows, width), joined], 1
    )
    summed = lax.psum_scatter(
        packed.reshape(-1, width).astype(jnp.bfloat16), AXES, scatter_dimension=0, tiled=True
    ).astype(jnp.float32)
    attn_part = summed[:rows]
    first_part = summed[rows : 2 * rows]
    flat = summed[2 * rows :].reshape(-1)
    sizes = [block.shape[1] for block in blocks]
    offsets = [sum(sizes[:index]) for index in range(len(sizes))]
    parts = [flat[offset : offset + size] for offset, size in zip(offsets, sizes)]
    _, layout_attn_grad, layout_w1_grad, layout_w2_grad, _ = small_grads
    local_w1_cols = layout_w1_grad.shape[1] // count
    return (
        attn_part,
        first_part,
        parts[0],
        parts[1].reshape(layout_attn_grad.shape[0] // count, layout_attn_grad.shape[1]),
        parts[2].reshape(layout_w1_grad.shape[0], local_w1_cols),
        parts[3].reshape(layout_w2_grad.shape[0] // count, layout_w2_grad.shape[1]),
        parts[4],
    )


def body(
    text_in,
    layout_in,
    lengths,
    text_attn,
    text_w1,
    text_w2,
    text_vectors,
    layout_attn,
    layout_w1,
    layout_w2,
    layout_vectors,
    cot_text,
    cot_layout,
):
    count = lax.psum(1, AXES)
    weights = gather_weights(
        text_attn, text_w1, text_w2, text_vectors, layout_attn, layout_w1, layout_w2, layout_vectors
    )

    page_weights = (None,) * len(weights)
    out_text, kept_all = jax.vmap(page_forward, in_axes=(0, 0, 0, page_weights))(
        text_in, layout_in, lengths, weights
    )
    text_a = jax.vmap(page_back_ffn, in_axes=(0, 0, 0, page_weights))(
        lengths, kept_all, cot_text, weights
    )
    round_second, text_hidden, text_active = text_a[1], text_a[2], text_a[3]
    second_grad = jnp.einsum(
        "sf,sd->fd", flat_rows(text_active), flat_rows(round_second), preferred_element_type=jnp.float32
    ).astype(jnp.bfloat16)
    second_grad, text_a, kept_all = lax.optimization_barrier((second_grad, text_a, kept_all))
    grad_second = lax.psum_scatter(second_grad, AXES, scatter_dimension=0, tiled=True).astype(
        jnp.float32
    )
    out_layout, (text_grad, layout_grad), small_terms, text_rounded, text_first_low, round_inner = (
        jax.vmap(page_back_attn, in_axes=(0, 0, 0, 0, 0, 0, page_weights))(
            text_in, layout_in, lengths, kept_all, text_a, cot_layout, weights
        )
    )
    totals = tuple(jnp.sum(term, 0) for term in small_terms)
    first_grad = jnp.einsum(
        "sd,sf->df", flat_rows(text_hidden), flat_rows(round_inner), preferred_element_type=jnp.float32
    )
    three_part = jnp.einsum(
        "psd,pjes->dje", text_in, text_rounded, preferred_element_type=jnp.float32
    ).reshape(text_in.shape[2], -1)
    out_part = jnp.einsum(
        "pds,pse->de", kept_all[2], text_first_low, preferred_element_type=jnp.float32
    )
    summed = scatter_late(count, jnp.concatenate([three_part, out_part], 1), first_grad, totals)
    return (
        out_text,
        out_layout,
        text_grad,
        layout_grad,
        summed[0],
        summed[1],
        grad_second,
        summed[2],
        summed[3],
        summed[4],
        summed[5],
        summed[6],
    )


def solution(mesh):
    placed = (
        P(("dp", "shard"), None, None),
        P(("dp", "shard"), None, None),
        P(("dp", "shard")),
        P(("dp", "shard"), None),
        P(("dp", "shard"), None),
        P(("dp", "shard"), None),
        P(("dp", "shard")),
        P(("dp", "shard"), None),
        P(None, ("dp", "shard")),
        P(("dp", "shard"), None),
        P(("dp", "shard")),
        P(("dp", "shard"), None, None),
        P(("dp", "shard"), None, None),
    )
    return jax.shard_map(
        body,
        mesh=mesh,
        in_specs=placed,
        out_specs=(
            P(("dp", "shard"), None, None),
            P(("dp", "shard"), None, None),
            P(("dp", "shard"), None, None),
            P(("dp", "shard"), None, None),
            P(("dp", "shard"), None),
            P(("dp", "shard"), None),
            P(("dp", "shard"), None),
            P(("dp", "shard")),
            P(("dp", "shard"), None),
            P(None, ("dp", "shard")),
            P(("dp", "shard"), None),
            P(("dp", "shard")),
        ),
        check_vma=False,
    )
```

```python
import functools

import jax
import jax.numpy as jnp
from jax import lax
from jax.experimental import pallas as pl
from jax.experimental.pallas import tpu as pltpu
from jax.sharding import PartitionSpec as P


H = 12
HD = 64
LHD = 16


EPS = 1e-05
NEG = -1000000000.0


def normalize(values, scale_row, shift_row):
    centered = values - jnp.mean(values, -1, keepdims=True)
    variance = jnp.mean(centered * centered, -1, keepdims=True)
    return centered * lax.rsqrt(variance + EPS) * scale_row + shift_row


def gelu_exact(values):
    return 0.5 * values * (1.0 + lax.erf(values * (0.5 ** 0.5)))


def vector_parts(packed, width):
    pieces = [packed[index * width : (index + 1) * width] for index in range(8)]
    return pieces + [packed[8 * width :]]


def block_of(attn, index, width, columns):
    if columns:
        return attn[:, index * width : (index + 1) * width]
    return attn[index * width : (index + 1) * width]


def project_three(inputs, attn, packed, width, columns):
    if columns:
        three = attn[:, 0 : 3 * width].reshape(width, 3, width)
        mixed = jnp.einsum("sd,dje->sje", inputs, three, preferred_element_type=jnp.float32)
    else:
        three = attn[0 : 3 * width].reshape(3, width, width)
        mixed = jnp.einsum("sd,jde->sje", inputs, three, preferred_element_type=jnp.float32)
    pieces = vector_parts(packed.astype(jnp.float32), width)
    offsets = jnp.stack([pieces[0], jnp.zeros_like(pieces[0]), pieces[1]])
    return (mixed + offsets[None]).astype(jnp.bfloat16)


def attend(text_three, layout_three, length):
    return attn_fwd_heads(
        jnp.reshape(length, (1,)).astype(jnp.int32),
        text_three.transpose(1, 2, 0),
        layout_three.transpose(1, 2, 0),
        (HD ** (-0.5), LHD ** (-0.5)),
    )


def _nn(a, b):
    return lax.dot_general(a, b, (((1,), (0,)), ((), ())), preferred_element_type=jnp.float32)


def _nt(a, b):
    return lax.dot_general(a, b, (((1,), (1,)), ((), ())), preferred_element_type=jnp.float32)


def attn_back_kernel(len_ref, text_ref, dc_ref, layout_ref, dcl_ref, lse_ref, text_out, layout_out, *, scales):
    text_scale, layout_scale = scales
    query, key, value = text_ref[0], text_ref[1], text_ref[2]
    query_l, key_l, value_l = layout_ref[0], layout_ref[1], layout_ref[2]
    scores = _nn(key.T, query) * text_scale + _nn(key_l.T, query_l) * layout_scale
    keys = lax.broadcasted_iota(jnp.int32, scores.shape, 0)
    scores = jnp.where(keys < len_ref[0], scores, NEG)
    probs = jnp.exp(scores - lse_ref[0])
    text_dp = _nn(value.T, dc_ref[...])
    layout_dp = _nn(value_l.T, dcl_ref[...])
    text_ds = probs * (text_dp - jnp.sum(probs * text_dp, 0, keepdims=True))
    layout_ds = probs * (layout_dp - jnp.sum(probs * layout_dp, 0, keepdims=True))
    text_g = text_ds.astype(jnp.bfloat16)
    joint_g = (text_ds + layout_ds).astype(jnp.bfloat16)
    weights = probs.astype(jnp.bfloat16)
    text_out[0] = (_nn(key, text_g) * text_scale).astype(text_out.dtype)
    text_out[1] = (_nt(query, text_g) * text_scale).astype(text_out.dtype)
    text_out[2] = _nt(dc_ref[...], weights).astype(text_out.dtype)
    layout_out[0] = (_nn(key_l, joint_g) * layout_scale).astype(layout_out.dtype)
    layout_out[1] = (_nt(query_l, joint_g) * layout_scale).astype(layout_out.dtype)
    layout_out[2] = _nt(dcl_ref[...], weights).astype(layout_out.dtype)


def attn_back_heads(length, text_t, dc_t, layout_t, dcl_t, lse, scales):
    parts, width, slots = text_t.shape
    narrow = layout_t.shape[1]
    wide, thin = width // H, narrow // H
    text_spec = pl.BlockSpec((parts, wide, slots), lambda h, n: (0, h, 0))
    layout_spec = pl.BlockSpec((parts, thin, slots), lambda h, n: (0, h, 0))
    flops = H * slots * slots * 2 * (4 * wide + 4 * thin)
    return pl.pallas_call(
        functools.partial(attn_back_kernel, scales=scales),
        grid_spec=pltpu.PrefetchScalarGridSpec(
            num_scalar_prefetch=1,
            grid=(H,),
            in_specs=[
                text_spec,
                pl.BlockSpec((wide, slots), lambda h, n: (h, 0)),
                layout_spec,
                pl.BlockSpec((thin, slots), lambda h, n: (h, 0)),
                pl.BlockSpec((1, 1, slots), lambda h, n: (h, 0, 0)),
            ],
            out_specs=[text_spec, layout_spec],
        ),
        out_shape=[
            jax.ShapeDtypeStruct(text_t.shape, jnp.bfloat16),
            jax.ShapeDtypeStruct(layout_t.shape, jnp.bfloat16),
        ],
        compiler_params=pltpu.CompilerParams(dimension_semantics=("arbitrary",)),
        cost_estimate=pl.CostEstimate(
            flops=flops,
            transcendentals=H * slots * slots,
            bytes_accessed=slots * (8 * width + 8 * narrow + 4 * H),
        ),
    )(length, text_t, dc_t, layout_t, dcl_t, lse)


def attn_fwd_kernel(len_ref, text_ref, layout_ref, ctx_out, ctxl_out, lse_out, *, scales):
    text_scale, layout_scale = scales
    query, key, value = text_ref[0], text_ref[1], text_ref[2]
    query_l, key_l, value_l = layout_ref[0], layout_ref[1], layout_ref[2]
    scores = _nn(key.T, query) * text_scale + _nn(key_l.T, query_l) * layout_scale
    keys = lax.broadcasted_iota(jnp.int32, scores.shape, 0)
    scores = jnp.where(keys < len_ref[0], scores, NEG)
    top = jnp.max(scores, 0, keepdims=True)
    exponent = jnp.exp(scores - top)
    total = jnp.sum(exponent, 0, keepdims=True)
    weights = (exponent / total).astype(jnp.bfloat16)
    ctx_out[...] = _nn(value, weights).astype(ctx_out.dtype)
    ctxl_out[...] = _nn(value_l, weights).astype(ctxl_out.dtype)
    lse_out[0] = top + jnp.log(total)


def attn_fwd_heads(length, text_t, layout_t, scales):
    parts, width, slots = text_t.shape
    narrow = layout_t.shape[1]
    wide, thin = width // H, narrow // H
    flops = H * slots * slots * 2 * (2 * wide + 2 * thin)
    return pl.pallas_call(
        functools.partial(attn_fwd_kernel, scales=scales),
        grid_spec=pltpu.PrefetchScalarGridSpec(
            num_scalar_prefetch=1,
            grid=(H,),
            in_specs=[
                pl.BlockSpec((parts, wide, slots), lambda h, n: (0, h, 0)),
                pl.BlockSpec((parts, thin, slots), lambda h, n: (0, h, 0)),
            ],
            out_specs=[
                pl.BlockSpec((wide, slots), lambda h, n: (h, 0)),
                pl.BlockSpec((thin, slots), lambda h, n: (h, 0)),
                pl.BlockSpec((1, 1, slots), lambda h, n: (h, 0, 0)),
            ],
        ),
        out_shape=[
            jax.ShapeDtypeStruct((width, slots), jnp.bfloat16),
            jax.ShapeDtypeStruct((narrow, slots), jnp.bfloat16),
            jax.ShapeDtypeStruct((H, 1, slots), jnp.float32),
        ],
        compiler_params=pltpu.CompilerParams(dimension_semantics=("arbitrary",)),
        cost_estimate=pl.CostEstimate(
            flops=flops,
            transcendentals=H * slots * slots,
            bytes_accessed=slots * (8 * width + 8 * narrow + 4 * H),
        ),
    )(length, text_t, layout_t)


def attend_back(text_three, layout_three, length, log_total, text_grad, layout_grad):
    return attn_back_heads(
        jnp.reshape(length, (1,)).astype(jnp.int32),
        text_three.transpose(1, 2, 0),
        text_grad.T,
        layout_three.transpose(1, 2, 0),
        layout_grad.T,
        log_total,
        (HD ** (-0.5), LHD ** (-0.5)),
    )


def project_back(attn, width, columns, grad_t, first_grad):
    if columns:
        three = attn[:, 0 : 3 * width].reshape(width, 3, width)
        input_grad = first_grad + jnp.einsum(
            "jes,dje->sd", grad_t, three, preferred_element_type=jnp.float32
        )
    else:
        three = attn[0 : 3 * width].reshape(3, width, width)
        input_grad = first_grad + jnp.einsum(
            "jes,jde->sd", grad_t, three, preferred_element_type=jnp.float32
        )
    column_sums = jnp.sum(grad_t.astype(jnp.float32), 2)
    return (input_grad, grad_t, column_sums[0], column_sums[2])


def branch_forward(inputs, context, attn, packed, first, second, width, columns):
    pieces = vector_parts(packed.astype(jnp.float32), width)
    out_block = block_of(attn, 3, width, columns)
    first_res = inputs.astype(jnp.float32) + (
        jnp.dot(context, out_block, preferred_element_type=jnp.float32) + pieces[2]
    )
    hidden = normalize(first_res, pieces[3], pieces[4])
    inner = (
        jnp.dot(hidden.astype(jnp.bfloat16), first, preferred_element_type=jnp.float32) + pieces[8]
    )
    activated = gelu_exact(inner).astype(jnp.bfloat16)
    second_res = hidden + (
        jnp.dot(activated, second, preferred_element_type=jnp.float32) + pieces[5]
    )
    result = normalize(second_res, pieces[6], pieces[7])
    return (result, (first_res, inner, second_res))


def branch_backward(attn, packed, first, second, width, columns, kept_rows, grad_out):
    first_res, inner, second_res = kept_rows
    pieces = vector_parts(packed.astype(jnp.float32), width)
    hidden, first_pull = jax.vjp(normalize, first_res, pieces[3], pieces[4])
    _, second_pull = jax.vjp(normalize, second_res, pieces[6], pieces[7])
    grad_second, late_scale, late_shift = second_pull(grad_out)
    round_second = grad_second.astype(jnp.bfloat16)
    activated, gelu_pull = jax.vjp(gelu_exact, inner)
    (grad_inner,) = gelu_pull(jnp.dot(round_second, second.T, preferred_element_type=jnp.float32))
    round_inner = grad_inner.astype(jnp.bfloat16)
    grad_hidden = grad_second + jnp.dot(round_inner, first.T, preferred_element_type=jnp.float32)
    grad_first, early_scale, early_shift = first_pull(grad_hidden)
    round_first = grad_first.astype(jnp.bfloat16)
    out_block = block_of(attn, 3, width, columns)
    grad_ctx = jnp.dot(round_first, out_block.T, preferred_element_type=jnp.float32).astype(
        jnp.bfloat16
    )
    operands = (
        hidden.astype(jnp.bfloat16),
        activated.astype(jnp.bfloat16),
        round_first,
        round_second,
        round_inner,
    )
    vector_sums = (
        jnp.sum(grad_first, 0),
        early_scale,
        early_shift,
        jnp.sum(grad_second, 0),
        late_scale,
        late_shift,
        jnp.sum(grad_inner, 0),
    )
    return (grad_first, grad_ctx, operands, vector_sums)


def branch_back_a(packed, width, kept_rows, grad_out):
    first_res, inner, second_res = kept_rows
    pieces = vector_parts(packed.astype(jnp.float32), width)
    hidden = normalize(first_res, pieces[3], pieces[4])
    _, second_pull = jax.vjp(normalize, second_res, pieces[6], pieces[7])
    grad_second, late_scale, late_shift = second_pull(grad_out)
    round_second = grad_second.astype(jnp.bfloat16)
    return (
        grad_second,
        round_second,
        hidden.astype(jnp.bfloat16),
        gelu_exact(inner).astype(jnp.bfloat16),
        late_scale,
        late_shift,
    )


def branch_back_b(attn, packed, first, second, width, columns, kept_rows, part_a):
    first_res, inner, _ = kept_rows
    grad_second, round_second, hidden_low, active_low, late_scale, late_shift = part_a
    _, gelu_pull = jax.vjp(gelu_exact, inner)
    (grad_inner,) = gelu_pull(jnp.dot(round_second, second.T, preferred_element_type=jnp.float32))
    round_inner = grad_inner.astype(jnp.bfloat16)
    pieces = vector_parts(packed.astype(jnp.float32), width)
    _, first_pull = jax.vjp(normalize, first_res, pieces[3], pieces[4])
    grad_hidden = grad_second + jnp.dot(round_inner, first.T, preferred_element_type=jnp.float32)
    grad_first, early_scale, early_shift = first_pull(grad_hidden)
    round_first = grad_first.astype(jnp.bfloat16)
    out_block = block_of(attn, 3, width, columns)
    grad_ctx = jnp.dot(round_first, out_block.T, preferred_element_type=jnp.float32).astype(
        jnp.bfloat16
    )
    operands = (hidden_low, active_low, round_first, round_second, round_inner)
    vector_sums = (
        jnp.sum(grad_first, 0),
        early_scale,
        early_shift,
        jnp.sum(grad_second, 0),
        late_scale,
        late_shift,
        jnp.sum(grad_inner, 0),
    )
    return (grad_first, grad_ctx, operands, vector_sums)


def page_forward(text_rows, layout_rows, length, weights):
    (text_attn, text_first, text_second, text_packed, layout_attn, _, _, layout_packed) = weights
    width = text_rows.shape[1]
    narrow = layout_rows.shape[1]
    valid = jnp.arange(text_rows.shape[0], dtype=jnp.int32) < length
    text_three = project_three(text_rows, text_attn, text_packed, width, True)
    layout_three = project_three(layout_rows, layout_attn, layout_packed, narrow, False)
    text_ctx, layout_ctx, log_total = attend(text_three, layout_three, length)
    text_out, text_kept = branch_forward(
        text_rows, text_ctx.T, text_attn, text_packed, text_first, text_second, width, True
    )
    mask = valid[:, None].astype(jnp.float32)
    kept_page = (text_three, layout_three, text_ctx, layout_ctx, log_total, text_kept)
    return ((text_out * mask).astype(jnp.bfloat16), kept_page)


def page_back_ffn(length, kept_page, text_cot, weights):
    text_attn, _, _, text_packed = weights[:4]
    text_kept = kept_page[5]
    width = text_attn.shape[0]
    slots = text_cot.shape[0]
    valid = jnp.arange(slots, dtype=jnp.int32) < length
    mask = valid[:, None].astype(jnp.float32)
    return branch_back_a(text_packed, width, text_kept, text_cot.astype(jnp.float32) * mask)


def page_back_attn(text_rows, layout_rows, length, kept_page, text_a, layout_cot, weights):
    (
        text_attn,
        text_first,
        text_second,
        text_packed,
        layout_attn,
        layout_first,
        layout_second,
        layout_packed,
    ) = weights
    text_three, layout_three, _, layout_ctx, log_total, text_kept = kept_page
    width = text_rows.shape[1]
    narrow = layout_rows.shape[1]
    slots = text_rows.shape[0]
    valid = jnp.arange(slots, dtype=jnp.int32) < length
    mask = valid[:, None].astype(jnp.float32)
    layout_out, layout_kept = branch_forward(
        layout_rows,
        layout_ctx.T,
        layout_attn,
        layout_packed,
        layout_first,
        layout_second,
        narrow,
        False,
    )
    layout_back = branch_backward(
        layout_attn,
        layout_packed,
        layout_first,
        layout_second,
        narrow,
        False,
        layout_kept,
        layout_cot.astype(jnp.float32) * mask,
    )
    text_back = branch_back_b(
        text_attn, text_packed, text_first, text_second, width, True, text_kept, text_a
    )
    text_res_grad, text_ctx_grad, text_ops, text_sums = text_back
    layout_res_grad, layout_ctx_grad, layout_ops, layout_sums = layout_back
    text_three_grad, layout_three_grad = attend_back(
        text_three, layout_three, length, log_total, text_ctx_grad, layout_ctx_grad
    )
    text_in_grad, text_rounded, text_query_bias, text_value_bias = project_back(
        text_attn, width, True, text_three_grad, text_res_grad
    )
    layout_in_grad, layout_rounded, layout_query_bias, layout_value_bias = project_back(
        layout_attn, narrow, False, layout_three_grad, layout_res_grad
    )
    hidden_low, active_low, first_low, second_low, inner_low = layout_ops
    three_w = jnp.einsum(
        "sd,jes->jde", layout_rows, layout_rounded, preferred_element_type=jnp.float32
    ).reshape(3 * narrow, narrow)
    out_w = jnp.einsum("ds,se->de", layout_ctx, first_low, preferred_element_type=jnp.float32)
    layout_attn_grad = jnp.concatenate([three_w, out_w], 0)
    layout_first_grad = jnp.einsum(
        "sd,sf->df", hidden_low, inner_low, preferred_element_type=jnp.float32
    )
    layout_second_grad = jnp.einsum(
        "sf,sd->fd", active_low, second_low, preferred_element_type=jnp.float32
    )
    layout_vec_grad = jnp.concatenate([layout_query_bias, layout_value_bias] + list(layout_sums))
    text_vec_grad = jnp.concatenate([text_query_bias, text_value_bias] + list(text_sums))
    small_terms = (
        text_vec_grad,
        layout_attn_grad,
        layout_first_grad,
        layout_second_grad,
        layout_vec_grad,
    )
    layout_low = (layout_out * mask).astype(jnp.bfloat16)
    grads = (text_in_grad, layout_in_grad)
    return (layout_low, grads, small_terms, text_rounded, text_ops[2], text_ops[4])


def flat_rows(values):
    return values.reshape(-1, values.shape[-1])


AXES = ("dp", "shard")


def rows_for(size, width, aligned):
    rows = -(-size // width)
    if aligned:
        rows = -(-rows // 8) * 8
    return rows


def pack_rows(pieces, width, aligned):
    flat = jnp.concatenate([piece.reshape(-1) for piece in pieces])
    rows = rows_for(flat.shape[0], width, aligned)
    return jnp.pad(flat, (0, rows * width - flat.shape[0])).reshape(rows, width)


def unpack_small(flat, count, shapes):
    sizes = [rows * cols for rows, cols in shapes]
    offsets = [sum(sizes[:index]) for index in range(len(sizes))]
    parts = [flat[:, offset : offset + size] for offset, size in zip(offsets, sizes)]
    (attn_rows, attn_cols), (w1_rows, w1_cols), (w2_rows, w2_cols) = shapes[1:4]
    return (
        parts[0].reshape(-1),
        parts[1].reshape(count * attn_rows, attn_cols),
        parts[2].reshape(count, w1_rows, w1_cols).transpose(1, 0, 2).reshape(w1_rows, count * w1_cols),
        parts[3].reshape(count * w2_rows, w2_cols),
        parts[4].reshape(-1),
    )


def gather_weights(text_attn, text_w1, text_w2, text_vectors, layout_attn, layout_w1, layout_w2, layout_vectors):
    rows, width = text_attn.shape
    aligned = rows % 8 == 0
    small = (text_vectors, layout_attn, layout_w1, layout_w2, layout_vectors)
    small_rows = pack_rows(small, width, aligned)
    first = jnp.concatenate([text_attn, text_w1, small_rows], 0)
    first_all = lax.all_gather(first, AXES, axis=0, tiled=True)
    count = first_all.shape[0] // first.shape[0]
    first_all = first_all.reshape(count, first.shape[0], width)
    full_attn = first_all[:, :rows].reshape(count * rows, width)
    full_w1 = first_all[:, rows : 2 * rows].reshape(count * rows, width)
    small_flat = first_all[:, 2 * rows :].reshape(count, -1)
    shapes = [(1, text_vectors.shape[0]), layout_attn.shape, layout_w1.shape, layout_w2.shape, (1, layout_vectors.shape[0])]
    full_small = unpack_small(small_flat, count, shapes)
    full_w2 = lax.all_gather(text_w2, AXES, axis=0, tiled=True)
    return (full_attn, full_w1, full_w2) + full_small


def small_blocks(count, text_vec_grad, layout_attn_grad, layout_w1_grad, layout_w2_grad, layout_vec_grad):
    local_w1_cols = layout_w1_grad.shape[1] // count
    return (
        text_vec_grad.reshape(count, -1),
        layout_attn_grad.reshape(count, -1),
        layout_w1_grad.reshape(layout_w1_grad.shape[0], count, local_w1_cols)
        .transpose(1, 0, 2)
        .reshape(count, -1),
        layout_w2_grad.reshape(count, -1),
        layout_vec_grad.reshape(count, -1),
    )


def scatter_late(count, grad_attn, grad_first, small_grads):
    width = grad_first.shape[1]
    rows = grad_first.shape[0] // count
    blocks = small_blocks(count, *small_grads)
    joined = jnp.concatenate(blocks, 1)
    size = joined.shape[1]
    small_rows = rows_for(size, width, rows % 8 == 0)
    joined = jnp.pad(joined, ((0, 0), (0, small_rows * width - size))).reshape(count, small_rows, width)
    attn_rows = jnp.concatenate(
        [part.astype(jnp.bfloat16).reshape(count, rows, -1) for part in grad_attn], 2
    )
    packed = jnp.concatenate(
        [attn_rows, grad_first.astype(jnp.bfloat16).reshape(count, rows, width), joined.astype(jnp.bfloat16)], 1
    )
    summed = lax.psum_scatter(
        packed.reshape(-1, width).astype(jnp.bfloat16), AXES, scatter_dimension=0, tiled=True
    ).astype(jnp.float32)
    attn_part = summed[:rows]
    first_part = summed[rows : 2 * rows]
    flat = summed[2 * rows :].reshape(-1)
    sizes = [block.shape[1] for block in blocks]
    offsets = [sum(sizes[:index]) for index in range(len(sizes))]
    parts = [flat[offset : offset + size] for offset, size in zip(offsets, sizes)]
    _, layout_attn_grad, layout_w1_grad, layout_w2_grad, _ = small_grads
    local_w1_cols = layout_w1_grad.shape[1] // count
    return (
        attn_part,
        first_part,
        parts[0],
        parts[1].reshape(layout_attn_grad.shape[0] // count, layout_attn_grad.shape[1]),
        parts[2].reshape(layout_w1_grad.shape[0], local_w1_cols),
        parts[3].reshape(layout_w2_grad.shape[0] // count, layout_w2_grad.shape[1]),
        parts[4],
    )


def body(
    text_in,
    layout_in,
    lengths,
    text_attn,
    text_w1,
    text_w2,
    text_vectors,
    layout_attn,
    layout_w1,
    layout_w2,
    layout_vectors,
    cot_text,
    cot_layout,
):
    count = lax.psum(1, AXES)
    weights = gather_weights(
        text_attn, text_w1, text_w2, text_vectors, layout_attn, layout_w1, layout_w2, layout_vectors
    )

    page_weights = (None,) * len(weights)
    out_text, kept_all = jax.vmap(page_forward, in_axes=(0, 0, 0, page_weights))(
        text_in, layout_in, lengths, weights
    )
    text_a = jax.vmap(page_back_ffn, in_axes=(0, 0, 0, page_weights))(
        lengths, kept_all, cot_text, weights
    )
    round_second, text_hidden, text_active = text_a[1], text_a[2], text_a[3]
    second_grad = jnp.einsum(
        "sf,sd->fd", flat_rows(text_active), flat_rows(round_second), preferred_element_type=jnp.float32
    ).astype(jnp.bfloat16)
    second_grad, text_a, kept_all = lax.optimization_barrier((second_grad, text_a, kept_all))
    grad_second = lax.psum_scatter(second_grad, AXES, scatter_dimension=0, tiled=True).astype(
        jnp.float32
    )
    out_layout, (text_grad, layout_grad), small_terms, text_rounded, text_first_low, round_inner = (
        jax.vmap(page_back_attn, in_axes=(0, 0, 0, 0, 0, 0, page_weights))(
            text_in, layout_in, lengths, kept_all, text_a, cot_layout, weights
        )
    )
    totals = tuple(jnp.sum(term, 0) for term in small_terms)
    first_grad = jnp.einsum(
        "sd,sf->df", flat_rows(text_hidden), flat_rows(round_inner), preferred_element_type=jnp.float32
    )
    three_part = jnp.einsum(
        "psd,pjes->dje", text_in, text_rounded, preferred_element_type=jnp.float32
    ).reshape(text_in.shape[2], -1)
    out_part = jnp.einsum(
        "pds,pse->de", kept_all[2], text_first_low, preferred_element_type=jnp.float32
    )
    summed = scatter_late(count, (three_part, out_part), first_grad, totals)
    return (
        out_text,
        out_layout,
        text_grad,
        layout_grad,
        summed[0],
        summed[1],
        grad_second,
        summed[2],
        summed[3],
        summed[4],
        summed[5],
        summed[6],
    )


def solution(mesh):
    placed = (
        P(("dp", "shard"), None, None),
        P(("dp", "shard"), None, None),
        P(("dp", "shard")),
        P(("dp", "shard"), None),
        P(("dp", "shard"), None),
        P(("dp", "shard"), None),
        P(("dp", "shard")),
        P(("dp", "shard"), None),
        P(None, ("dp", "shard")),
        P(("dp", "shard"), None),
        P(("dp", "shard")),
        P(("dp", "shard"), None, None),
        P(("dp", "shard"), None, None),
    )
    return jax.shard_map(
        body,
        mesh=mesh,
        in_specs=placed,
        out_specs=(
            P(("dp", "shard"), None, None),
            P(("dp", "shard"), None, None),
            P(("dp", "shard"), None, None),
            P(("dp", "shard"), None, None),
            P(("dp", "shard"), None),
            P(("dp", "shard"), None),
            P(("dp", "shard"), None),
            P(("dp", "shard")),
            P(("dp", "shard"), None),
            P(None, ("dp", "shard")),
            P(("dp", "shard"), None),
            P(("dp", "shard")),
        ),
        check_vma=False,
    )
```
